32 devices in a mesh: dp: 2 (over core), lat: 8 (over z, y), lon: 2 (over x).
Axes of the slice: x: 2, y: 2, z: 4, core: 2. Of those that a mesh axis runs over, the one named last changes fastest.
Arguments:
- tokens: bfloat16 [2, 64, 32, 1024], P('dp', 'lat', 'lon'), may hold values from -40 to 40
- cotangent: bfloat16 [2, 64, 32, 1024], P('dp', 'lat', 'lon'), may hold values from -6 to 6
- valid_cells: int32 [64, 32], replicated, may hold values 0 or 1
- w_qkv: bfloat16 [1024, 3072], P('dp'), may hold values from -1 to 1
- w_out: bfloat16 [1024, 1024], P('dp'), may hold values from -0.1875 to 0.1875
Outputs:
- d_input: bfloat16 [2, 64, 32, 1024], P('dp', 'lat', 'lon')
- d_w_out: float32 [1024, 1024], P(('dp', 'lat'), 'lon')
The draws below stay inside these ranges and needn't reach their ends.
All inputs are finite; a program needn't handle non-finite values.
Results may differ from the reference program's by a relative error of at most 0.015.
The reference program's roundings to bfloat16 on the way count: a program that leaves them out, or rounds other values in their place, can miss the bound.
Values may be sent and summed in bfloat16 or wider, within the bound.
No kernel may reach another device: no remote copies, remote signals or barrier semaphores. Data moves between devices by JAX's collectives and lax.ppermute only.
A program may use at most 128 MiB of HBM per device.

```python
import jax
import jax.numpy as jnp
from jax import lax

D = 1024
HEADS = 16
HEAD_DIM = 64
RADIUS = 6
TILE = 8
MEMBERS = 2
ROWS = 64
COLS = 32
SHARDS = 32


def draw_tokens(key, part):
    base_key = jax.random.fold_in(key, 0)
    shape = (MEMBERS, ROWS, COLS, D)
    values = jnp.clip(jax.random.normal(base_key, shape, jnp.float32), -6.0, 6.0)
    return values.astype(jnp.bfloat16)


def draw_w_qkv(key, part):
    first_key = jax.random.fold_in(key, 0)
    base = jnp.clip(jax.random.normal(first_key, (D, 3 * D), jnp.float32), -6.0, 6.0) * D ** (-0.5)
    return base.astype(jnp.bfloat16)


def plant(array, rng, low, top_value):
    longest = array.shape.index(max(array.shape))
    spots = []
    for shift in (0, 1):
        where = [jax.random.randint(jax.random.fold_in(rng, axis), (), 0, length) for axis, length in enumerate(array.shape)]
        where[longest] = (where[longest] + shift) % array.shape[longest]
        spots.append(tuple(where))
    return array.at[spots[0]].set(low).at[spots[1]].set(top_value)


def levels(rng, dims, cuts, least, largest):
    def one(position, shards_of):
        draws = jax.random.uniform(jax.random.fold_in(jax.random.fold_in(rng, 6), position), (shards_of,), jnp.float32, least / len(cuts), largest / len(cuts))
        return jnp.repeat(jnp.exp(draws), dims[position] // shards_of).reshape((-1,) + (1,) * (len(dims) - position - 1))

    gain = one(*cuts[0])
    for cut in cuts[1:]:
        gain = gain * one(*cut)
    return gain


def centred(rng, dims, deviation, bound, cuts=(), kind=jnp.bfloat16):
    gain = levels(rng, dims, cuts, -0.22, 0.18) if cuts else 1.0
    drawn = jax.random.normal(rng, dims, jnp.float32) * deviation * gain
    return jnp.minimum(jnp.maximum(drawn, -bound), bound).astype(kind)


def setup_inputs(seed: int = 0) -> dict:
    seeds = jax.random.split(jax.random.key(seed), 6)
    return {
        "tokens": draw_tokens(jax.random.fold_in(seeds[5], 71), 0),
        "cotangent": centred(seeds[1], (MEMBERS, ROWS, COLS, D), 1.0, 6.0, ((0, 2), (1, 8), (2, 2))),
        "valid_cells": plant((jax.random.randint(seeds[2], (ROWS, COLS), 0, 8) < 7).astype(jnp.int32), jax.random.fold_in(seeds[2], 1), 0, 1),
        "w_qkv": draw_w_qkv(jax.random.fold_in(seeds[5], 71), 0),
        "w_out": centred(seeds[4], (D, D), D ** -0.5, 0.1875, ((0, 2),)),
    }


def to_tiles(field):
    tile_rows = field.shape[0] // TILE
    tile_cols = field.shape[1] // TILE
    shaped = field.reshape((tile_rows, TILE, tile_cols, TILE) + field.shape[2:])
    order = (0, 2, 1, 3) + tuple(range(4, shaped.ndim))
    return shaped.transpose(order).reshape((tile_rows, tile_cols, TILE * TILE) + field.shape[2:])


def from_tiles(tiled):
    tile_rows, tile_cols = tiled.shape[0], tiled.shape[1]
    shaped = tiled.reshape((tile_rows, tile_cols, TILE, TILE) + tiled.shape[3:])
    order = (0, 2, 1, 3) + tuple(range(4, shaped.ndim))
    return shaped.transpose(order).reshape((tile_rows * TILE, tile_cols * TILE) + tiled.shape[3:])


def padded_blocks(tiled):
    rows_padded = jnp.pad(tiled, ((1, 1),) + ((0, 0),) * (tiled.ndim - 1))
    return jnp.concatenate([rows_padded[:, -1:], rows_padded, rows_padded[:, :1]], axis=1)


def neighbourhood(tiled):
    padded = padded_blocks(tiled)
    tile_rows, tile_cols = tiled.shape[0], tiled.shape[1]
    pieces = [padded[1 + row_step:1 + row_step + tile_rows, 1 + col_step:1 + col_step + tile_cols]
              for row_step in (-1, 0, 1) for col_step in (-1, 0, 1)]
    return jnp.concatenate(pieces, axis=2)


def fold_back(window_terms):
    tile_rows, tile_cols = window_terms.shape[0], window_terms.shape[1]
    parts = window_terms.reshape((tile_rows, tile_cols, 9, TILE * TILE) + window_terms.shape[3:])
    padded = jnp.zeros((tile_rows + 2, tile_cols + 2) + parts.shape[3:], jnp.float32)
    for row_step in (-1, 0, 1):
        for col_step in (-1, 0, 1):
            padded = padded.at[1 + row_step:1 + row_step + tile_rows, 1 + col_step:1 + col_step + tile_cols].add(
                parts[:, :, (row_step + 1) * 3 + col_step + 1])
    inner_rows = padded[1:-1]
    middle = inner_rows[:, 1:-1]
    middle = middle.at[:, -1].add(inner_rows[:, 0])
    middle = middle.at[:, 0].add(inner_rows[:, -1])
    return middle


def window_offsets():
    query_pos = jnp.arange(TILE * TILE)
    key_pos = jnp.arange(9 * TILE * TILE)
    block_index = key_pos // (TILE * TILE)
    inner_pos = key_pos % (TILE * TILE)
    key_row = (block_index // 3 - 1) * TILE + inner_pos // TILE
    key_col = (block_index % 3 - 1) * TILE + inner_pos % TILE
    delta_row = key_row[None, :] - (query_pos // TILE)[:, None]
    delta_col = key_col[None, :] - (query_pos % TILE)[:, None]
    inside = (jnp.abs(delta_row) <= RADIUS) & (jnp.abs(delta_col) <= RADIUS)
    itself = (delta_row == 0) & (delta_col == 0)
    return inside, itself


def member_terms(inputs_here, grad_here, w_qkv, w_out, allowed):
    row_count, col_count = inputs_here.shape[0], inputs_here.shape[1]
    flat_inputs = inputs_here.reshape(row_count * col_count, D)
    flat_grad = grad_here.reshape(row_count * col_count, D)
    projected = jnp.dot(flat_inputs, w_qkv, preferred_element_type=jnp.float32).astype(jnp.bfloat16)
    grad_attn = jnp.dot(flat_grad, w_out.T, preferred_element_type=jnp.float32).astype(jnp.bfloat16)
    tiled_proj = to_tiles(projected.reshape(row_count, col_count, 3, HEADS, HEAD_DIM))
    tiled_grad = to_tiles(grad_attn.reshape(row_count, col_count, HEADS, HEAD_DIM))
    score_scale = HEAD_DIM ** -0.5

    def one_head(head_index):
        query = tiled_proj[:, :, :, 0, head_index].astype(jnp.float32)
        keys = neighbourhood(tiled_proj[:, :, :, 1, head_index]).astype(jnp.float32)
        values = neighbourhood(tiled_proj[:, :, :, 2, head_index]).astype(jnp.float32)
        grad_tile = tiled_grad[:, :, :, head_index].astype(jnp.float32)
        scores = jnp.einsum('rcqd,rckd->rcqk', query, keys) * score_scale
        row_peak = jnp.max(jnp.where(allowed, scores, -jnp.inf), axis=-1, keepdims=True)
        weights = jnp.where(allowed, jnp.exp(scores - row_peak), 0.0)
        probabilities = weights / jnp.sum(weights, axis=-1, keepdims=True)
        probs_low = probabilities.astype(jnp.bfloat16).astype(jnp.float32)
        attended = jnp.einsum('rcqk,rckd->rcqd', probs_low, values).astype(jnp.bfloat16)
        grad_probs = jnp.einsum('rcqd,rckd->rcqk', grad_tile, values)
        centre = jnp.sum(probabilities * grad_probs, axis=-1, keepdims=True)
        grad_scores = (probabilities * (grad_probs - centre) * score_scale).astype(jnp.bfloat16).astype(jnp.float32)
        grad_query = jnp.einsum('rcqk,rckd->rcqd', grad_scores, keys).astype(jnp.bfloat16)
        grad_keys = fold_back(jnp.einsum('rcqk,rcqd->rckd', grad_scores, query)).astype(jnp.bfloat16)
        grad_values = fold_back(jnp.einsum('rcqk,rcqd->rckd', probs_low, grad_tile)).astype(jnp.bfloat16)
        return attended, grad_query, grad_keys, grad_values

    results = lax.map(one_head, jnp.arange(HEADS))

    def merge_heads(stacked):
        moved = jnp.moveaxis(stacked, 0, 3)
        shaped = moved.reshape(moved.shape[0], moved.shape[1], moved.shape[2], D)
        return from_tiles(shaped).reshape(row_count * col_count, D)

    attended_flat = merge_heads(results[0])
    grad_proj = jnp.concatenate([merge_heads(results[1]), merge_heads(results[2]), merge_heads(results[3])], axis=1)
    d_flat = jnp.dot(grad_proj, w_qkv.T, preferred_element_type=jnp.float32).astype(jnp.bfloat16)
    weight_term = jnp.dot(attended_flat.T, flat_grad, preferred_element_type=jnp.float32)
    return d_flat.reshape(row_count, col_count, D), weight_term


def reference(tokens, cotangent, valid_cells, w_qkv, w_out):
    inside, itself = window_offsets()
    key_valid = neighbourhood(to_tiles(valid_cells))
    allowed = inside[None, None] & ((key_valid[:, :, None, :] == 1) | itself[None, None])

    def member(member_pair):
        return member_terms(member_pair[0], member_pair[1], w_qkv, w_out, allowed)

    d_input, weight_terms = lax.map(member, (tokens, cotangent))
    d_w_out = jnp.sum(weight_terms, axis=0) / SHARDS
    return d_input, d_w_out
```

```python
import functools

import jax
import jax.numpy as jnp
from jax import lax
from jax.experimental import pallas as pl
from jax.sharding import PartitionSpec as P

HEADS = 16
RADIUS = 6

TRANS_B = (((1,), (1,)), ((), ()))


def passed_along(value, axis, steps):
    count = lax.axis_size(axis)
    pairs = [(source, (source + steps) % count) for source in range(count)]
    return lax.ppermute(value, axis, pairs)


def shifted(value, axis, by):
    count = lax.axis_size(axis)
    pairs = [(i, i + by) for i in range(count) if 0 <= i + by < count]
    return lax.ppermute(value, axis, pairs)


def extended(block, sides, width, periodic):
    for axis, dim in sides:
        count = lax.axis_size(axis)
        forward = [(i, i + 1) for i in range(count - 1)]
        if periodic:
            forward.append((count - 1, 0))
        backward = [(target, source) for source, target in forward]
        low = lax.ppermute(
            lax.slice_in_dim(block, block.shape[dim] - width, None, axis=dim), axis, forward
        )
        high = lax.ppermute(lax.slice_in_dim(block, 0, width, axis=dim), axis, backward)
        block = jnp.concatenate([low, block, high], axis=dim)
    return block


def attention_kernel(q_ref, k_ref, v_ref, g_ref, allow_ref, att_ref, gq_ref, gk_ref, gv_ref,
                     *, head_dim, scale):
    q = q_ref[...]
    k = k_ref[...]
    v = v_ref[...]
    g = g_ref[...]
    allowed = allow_ref[...] > 0.0
    lanes = q.shape[1]
    lane = lax.broadcasted_iota(jnp.int32, (1, lanes), 1)
    q32 = q.astype(jnp.float32)
    g32 = g.astype(jnp.float32)
    att = jnp.zeros(q.shape, jnp.float32)
    gq = jnp.zeros(q.shape, jnp.float32)
    gk = jnp.zeros(k.shape, jnp.float32)
    gv = jnp.zeros(v.shape, jnp.float32)
    for j in range(lanes // head_dim):
        sel = (lane >= j * head_dim) & (lane < (j + 1) * head_dim)
        qj = jnp.where(sel, q32, 0.0).astype(jnp.bfloat16)
        gj = jnp.where(sel, g32, 0.0).astype(jnp.bfloat16)
        scores = lax.dot_general(qj, k, TRANS_B, preferred_element_type=jnp.float32) * scale
        peak = jnp.max(jnp.where(allowed, scores, -jnp.inf), axis=1, keepdims=True)
        weights = jnp.where(allowed, jnp.exp(scores - peak), 0.0)
        probs = weights / jnp.sum(weights, axis=1, keepdims=True)
        probs_low = probs.astype(jnp.bfloat16)
        att_j = jnp.dot(probs_low, v, preferred_element_type=jnp.float32)
        grad_probs = lax.dot_general(gj, v, TRANS_B, preferred_element_type=jnp.float32)
        centre = jnp.sum(probs * grad_probs, axis=1, keepdims=True)
        grad_scores = (probs * (grad_probs - centre) * scale).astype(jnp.bfloat16)
        gq_j = jnp.dot(grad_scores, k, preferred_element_type=jnp.float32)
        scores_t = grad_scores.astype(jnp.float32).T.astype(jnp.bfloat16)
        probs_t = probs_low.astype(jnp.float32).T.astype(jnp.bfloat16)
        gk_j = jnp.dot(scores_t, q, preferred_element_type=jnp.float32)
        gv_j = jnp.dot(probs_t, g, preferred_element_type=jnp.float32)
        att = jnp.where(sel, att_j, att)
        gq = jnp.where(sel, gq_j, gq)
        gk = jnp.where(sel, gk_j, gk)
        gv = jnp.where(sel, gv_j, gv)
    att_ref[...] = att.astype(att_ref.dtype)
    gq_ref[...] = gq.astype(gq_ref.dtype)
    gk_ref[...] = gk
    gv_ref[...] = gv


def block_attention(query, key_values, grad_attn, allowed, heads):
    queries, width = query.shape
    keys = key_values.shape[0]
    head_dim = width // heads
    lanes = 128
    pairs = width // lanes
    kernel = functools.partial(attention_kernel, head_dim=head_dim, scale=head_dim ** (-0.5))
    flops = 2 * queries * keys * width * 2 * 6
    cost = pl.CostEstimate(
        flops=flops,
        transcendentals=queries * keys * heads,
        bytes_accessed=2 * (2 * queries * width + 2 * keys * width + 2 * queries * width)
        + 4 * queries * keys + 4 * 2 * keys * width,
    )
    return pl.pallas_call(
        kernel,
        grid=(pairs,),
        in_specs=[
            pl.BlockSpec((queries, lanes), lambda h: (0, h)),
            pl.BlockSpec((keys, lanes), lambda h: (0, h)),
            pl.BlockSpec((keys, lanes), lambda h: (0, h + pairs)),
            pl.BlockSpec((queries, lanes), lambda h: (0, h)),
            pl.BlockSpec((queries, keys), lambda h: (0, 0)),
        ],
        out_specs=[
            pl.BlockSpec((queries, lanes), lambda h: (0, h)),
            pl.BlockSpec((queries, lanes), lambda h: (0, h)),
            pl.BlockSpec((keys, lanes), lambda h: (0, h)),
            pl.BlockSpec((keys, lanes), lambda h: (0, h)),
        ],
        out_shape=[
            jax.ShapeDtypeStruct((queries, width), jnp.bfloat16),
            jax.ShapeDtypeStruct((queries, width), jnp.bfloat16),
            jax.ShapeDtypeStruct((keys, width), jnp.float32),
            jax.ShapeDtypeStruct((keys, width), jnp.float32),
        ],
        cost_estimate=cost,
        name="block_attention",
    )(query, key_values, key_values, grad_attn, allowed)


def fold_rims(grad_ext, height, breadth, radius):
    def return_lon(rim, by):
        return passed_along(rim.astype(jnp.bfloat16), "lon", by).astype(jnp.float32)

    def return_lat(rim, by):
        return shifted(rim.astype(jnp.bfloat16), "lat", by).astype(jnp.float32)

    from_right = return_lon(grad_ext[:, :radius], -1)
    from_left = return_lon(grad_ext[:, breadth + radius :], 1)
    middle = (
        grad_ext[:, radius : breadth + radius]
        + jnp.pad(from_right, ((0, 0), (breadth - radius, 0), (0, 0)))
        + jnp.pad(from_left, ((0, 0), (0, breadth - radius), (0, 0)))
    )
    from_below = return_lat(middle[:radius], -1)
    from_above = return_lat(middle[height + radius :], 1)
    own = (
        middle[radius : height + radius]
        + jnp.pad(from_below, ((height - radius, 0), (0, 0), (0, 0)))
        + jnp.pad(from_above, ((0, height - radius), (0, 0), (0, 0)))
    )
    return own


def partner_rows_product(lhs, weights, axis):
    count = lax.axis_size(axis)
    if count != 2:
        full = lax.all_gather(weights, axis, axis=0, tiled=True)
        return lax.dot_general(lhs, full, TRANS_B, preferred_element_type=jnp.float32).astype(
            jnp.bfloat16
        )
    other = lax.ppermute(weights, axis, [(0, 1), (1, 0)])
    mine_part = lax.dot_general(lhs, weights, TRANS_B, preferred_element_type=jnp.float32)
    other_part = lax.dot_general(lhs, other, TRANS_B, preferred_element_type=jnp.float32)
    mine_part = mine_part.astype(jnp.bfloat16)
    other_part = other_part.astype(jnp.bfloat16)
    first = lax.axis_index(axis) == 0
    return jnp.where(
        first,
        jnp.concatenate([mine_part, other_part], axis=1),
        jnp.concatenate([other_part, mine_part], axis=1),
    )


def shards(tokens, cotangent, valid_cells, w_qkv, w_out):
    inputs_here = tokens[0]
    grad_here = cotangent[0]
    height, breadth, width = inputs_here.shape
    radius = RADIUS
    ext_rows = height + 2 * radius
    ext_cols = breadth + 2 * radius
    pad_cols = -(-ext_cols // 8) * 8
    token_count = height * breadth
    key_count = ext_rows * pad_cols
    flat_inputs = inputs_here.reshape(token_count, width)
    flat_grad = grad_here.reshape(token_count, width)

    tok_lon = extended(inputs_here, (("lon", 1),), radius, True)
    tok_ext = extended(tok_lon, (("lat", 0),), radius, False)
    tok_ext = jnp.pad(tok_ext, ((0, 0), (0, pad_cols - ext_cols), (0, 0)))
    tok_ext = tok_ext.reshape(key_count, width)

    panels = lax.all_gather(w_qkv, "dp", axis=0, tiled=True)
    grad_attn = partner_rows_product(flat_grad, w_out, "dp")

    query = jnp.dot(flat_inputs, panels[:, :width], preferred_element_type=jnp.float32)
    query = query.astype(jnp.bfloat16)
    key_values = jnp.dot(tok_ext, panels[:, width:], preferred_element_type=jnp.float32)
    key_values = key_values.astype(jnp.bfloat16)

    wrapped = jnp.concatenate(
        [valid_cells[:, -radius:], valid_cells, valid_cells[:, :radius]], axis=1
    )
    framed = jnp.pad(wrapped, ((radius, radius), (0, 0)))
    valid_ext = lax.dynamic_slice(
        framed,
        (lax.axis_index("lat") * height, lax.axis_index("lon") * breadth),
        (ext_rows, ext_cols),
    )
    valid_ext = jnp.pad(valid_ext, ((0, 0), (0, pad_cols - ext_cols))).reshape(1, key_count)
    query_pos = jnp.arange(token_count)
    key_pos = jnp.arange(key_count)
    delta_row = (key_pos // pad_cols)[None, :] - radius - (query_pos // breadth)[:, None]
    delta_col = (key_pos % pad_cols)[None, :] - radius - (query_pos % breadth)[:, None]
    inside = (jnp.abs(delta_row) <= radius) & (jnp.abs(delta_col) <= radius)
    itself = (delta_row == 0) & (delta_col == 0)
    allowed = (inside & ((valid_ext == 1) | itself)).astype(jnp.float32)

    attended, grad_query, grad_keys, grad_values = block_attention(
        query, key_values, grad_attn, allowed, HEADS
    )

    device_count = lax.axis_size("dp") * lax.axis_size("lat") * lax.axis_size("lon")
    factor = 1.0 / device_count
    weight_term = (
        lax.dot_general(
            attended, flat_grad, (((0,), (0,)), ((), ())), preferred_element_type=jnp.float32
        )
        * factor
    ).astype(jnp.bfloat16)
    row_blocks = lax.axis_size("dp") * lax.axis_size("lat")
    col_blocks = lax.axis_size("lon")
    rows_each = width // row_blocks
    cols_each = width // col_blocks
    ordered = (
        weight_term.reshape(row_blocks, rows_each, col_blocks, cols_each)
        .transpose(0, 2, 1, 3)
        .reshape(row_blocks * col_blocks * rows_each, cols_each)
    )
    d_w_out = lax.psum_scatter(
        ordered, ("dp", "lat", "lon"), scatter_dimension=0, tiled=True
    ).astype(jnp.float32)

    grad_k_own = fold_rims(
        grad_keys.reshape(ext_rows, pad_cols, width)[:, :ext_cols], height, breadth, radius
    )
    grad_v_own = fold_rims(
        grad_values.reshape(ext_rows, pad_cols, width)[:, :ext_cols], height, breadth, radius
    )
    grad_proj = jnp.concatenate(
        [
            grad_query,
            grad_k_own.astype(jnp.bfloat16).reshape(token_count, width),
            grad_v_own.astype(jnp.bfloat16).reshape(token_count, width),
        ],
        axis=1,
    )
    d_flat = lax.dot_general(grad_proj, panels, TRANS_B, preferred_element_type=jnp.float32)
    d_input = d_flat.astype(jnp.bfloat16).reshape(1, height, breadth, width)
    return (d_input, d_w_out)


def solution(mesh):
    in_specs = (
        P("dp", "lat", "lon", None),
        P("dp", "lat", "lon", None),
        P(),
        P("dp", None),
        P("dp", None),
    )
    out_specs = (P("dp", "lat", "lon", None), P(("dp", "lat"), "lon"))
    return jax.shard_map(shards, mesh=mesh, in_specs=in_specs, out_specs=out_specs, check_vma=False)
```

```python
import functools

import jax
import jax.numpy as jnp
from jax import lax
from jax.experimental import pallas as pl
from jax.sharding import PartitionSpec as P

HEADS = 16
RADIUS = 6

TRANS_B = (((1,), (1,)), ((), ()))


def passed_along(value, axis, steps):
    count = lax.axis_size(axis)
    pairs = [(source, (source + steps) % count) for source in range(count)]
    return lax.ppermute(value, axis, pairs)


def shifted(value, axis, by):
    count = lax.axis_size(axis)
    pairs = [(i, i + by) for i in range(count) if 0 <= i + by < count]
    return lax.ppermute(value, axis, pairs)


def extended(block, sides, width, periodic):
    for axis, dim in sides:
        count = lax.axis_size(axis)
        forward = [(i, i + 1) for i in range(count - 1)]
        if periodic:
            forward.append((count - 1, 0))
        backward = [(target, source) for source, target in forward]
        low = lax.ppermute(
            lax.slice_in_dim(block, block.shape[dim] - width, None, axis=dim), axis, forward
        )
        high = lax.ppermute(lax.slice_in_dim(block, 0, width, axis=dim), axis, backward)
        block = jnp.concatenate([low, block, high], axis=dim)
    return block


def attention_kernel(q_ref, k_ref, v_ref, g_ref, allow_ref, att_ref, gq_ref, gk_ref, gv_ref,
                     *, head_dim, scale):
    q = q_ref[...]
    k = k_ref[...]
    v = v_ref[...]
    g = g_ref[...]
    allowed = allow_ref[...] > 0.0
    lanes = q.shape[1]
    lane = lax.broadcasted_iota(jnp.int32, (1, lanes), 1)
    q32 = q.astype(jnp.float32)
    g32 = g.astype(jnp.float32)
    att = jnp.zeros(q.shape, jnp.float32)
    gq = jnp.zeros(q.shape, jnp.float32)
    gk = jnp.zeros(k.shape, jnp.float32)
    gv = jnp.zeros(v.shape, jnp.float32)
    for j in range(lanes // head_dim):
        sel = (lane >= j * head_dim) & (lane < (j + 1) * head_dim)
        qj = jnp.where(sel, q32, 0.0).astype(jnp.bfloat16)
        gj = jnp.where(sel, g32, 0.0).astype(jnp.bfloat16)
        scores = lax.dot_general(qj, k, TRANS_B, preferred_element_type=jnp.float32) * scale
        peak = jnp.max(jnp.where(allowed, scores, -jnp.inf), axis=1, keepdims=True)
        weights = jnp.where(allowed, jnp.exp(scores - peak), 0.0)
        probs = weights / jnp.sum(weights, axis=1, keepdims=True)
        probs_low = probs.astype(jnp.bfloat16)
        att_j = jnp.dot(probs_low, v, preferred_element_type=jnp.float32)
        grad_probs = lax.dot_general(gj, v, TRANS_B, preferred_element_type=jnp.float32)
        centre = jnp.sum(probs * grad_probs, axis=1, keepdims=True)
        grad_scores = (probs * (grad_probs - centre) * scale).astype(jnp.bfloat16)
        gq_j = jnp.dot(grad_scores, k, preferred_element_type=jnp.float32)
        scores_t = grad_scores.astype(jnp.float32).T.astype(jnp.bfloat16)
        probs_t = probs_low.astype(jnp.float32).T.astype(jnp.bfloat16)
        gk_j = jnp.dot(scores_t, q, preferred_element_type=jnp.float32)
        gv_j = jnp.dot(probs_t, g, preferred_element_type=jnp.float32)
        att = jnp.where(sel, att_j, att)
        gq = jnp.where(sel, gq_j, gq)
        gk = jnp.where(sel, gk_j, gk)
        gv = jnp.where(sel, gv_j, gv)
    att_ref[...] = att.astype(att_ref.dtype)
    gq_ref[...] = gq.astype(gq_ref.dtype)
    gk_ref[...] = gk
    gv_ref[...] = gv


def block_attention(query, key_values, grad_attn, allowed, heads):
    queries, width = query.shape
    keys = key_values.shape[0]
    head_dim = width // heads
    lanes = 128
    pairs = width // lanes
    kernel = functools.partial(attention_kernel, head_dim=head_dim, scale=head_dim ** (-0.5))
    flops = 2 * queries * keys * width * 2 * 6
    cost = pl.CostEstimate(
        flops=flops,
        transcendentals=queries * keys * heads,
        bytes_accessed=2 * (2 * queries * width + 2 * keys * width + 2 * queries * width)
        + 4 * queries * keys + 4 * 2 * keys * width,
    )
    return pl.pallas_call(
        kernel,
        grid=(pairs,),
        in_specs=[
            pl.BlockSpec((queries, lanes), lambda h: (0, h)),
            pl.BlockSpec((keys, lanes), lambda h: (0, h)),
            pl.BlockSpec((keys, lanes), lambda h: (0, h + pairs)),
            pl.BlockSpec((queries, lanes), lambda h: (0, h)),
            pl.BlockSpec((queries, keys), lambda h: (0, 0)),
        ],
        out_specs=[
            pl.BlockSpec((queries, lanes), lambda h: (0, h)),
            pl.BlockSpec((queries, lanes), lambda h: (0, h)),
            pl.BlockSpec((keys, lanes), lambda h: (0, h)),
            pl.BlockSpec((keys, lanes), lambda h: (0, h)),
        ],
        out_shape=[
            jax.ShapeDtypeStruct((queries, width), jnp.bfloat16),
            jax.ShapeDtypeStruct((queries, width), jnp.bfloat16),
            jax.ShapeDtypeStruct((keys, width), jnp.float32),
            jax.ShapeDtypeStruct((keys, width), jnp.float32),
        ],
        cost_estimate=cost,
        name="block_attention",
    )(query, key_values, key_values, grad_attn, allowed)


def grid_pairs(delta_lat, delta_lon):
    lat_count = lax.axis_size("lat")
    lon_count = lax.axis_size("lon")
    pairs = []
    for la in range(lat_count):
        if 0 <= la + delta_lat < lat_count:
            for lo in range(lon_count):
                target = (la + delta_lat) * lon_count + (lo + delta_lon) % lon_count
                pairs.append((la * lon_count + lo, target))
    return pairs


def sent_to(value, delta_lat, delta_lon):
    return lax.ppermute(value, ("lat", "lon"), grid_pairs(delta_lat, delta_lon))


def part(count, radius, step, giving):
    if step == 0:
        return slice(0, count)
    if (step < 0) == giving:
        return slice(count - radius, count)
    return slice(0, radius)


def halo_gather(block, radius):
    height, breadth = block.shape[0], block.shape[1]
    rows = []
    for da in (-1, 0, 1):
        row = []
        for db in (-1, 0, 1):
            if da == 0 and db == 0:
                row.append(block)
                continue
            piece = block[part(height, radius, da, True), part(breadth, radius, db, True)]
            row.append(sent_to(piece, -da, -db))
        rows.append(jnp.concatenate(row, axis=1))
    return jnp.concatenate(rows, axis=0)


def halo_return(ext_list, height, breadth, radius):
    row_slices = {-1: slice(0, radius), 0: slice(radius, radius + height), 1: slice(radius + height, None)}
    col_slices = {-1: slice(0, radius), 0: slice(radius, radius + breadth), 1: slice(radius + breadth, None)}
    owns = [ext[row_slices[0], col_slices[0]] for ext in ext_list]
    widths = [ext.shape[-1] for ext in ext_list]
    for da in (-1, 0, 1):
        for db in (-1, 0, 1):
            if da == 0 and db == 0:
                continue
            pieces = [ext[row_slices[da], col_slices[db]] for ext in ext_list]
            joined = jnp.concatenate(pieces, axis=-1).astype(jnp.bfloat16)
            got = sent_to(joined, da, db).astype(jnp.float32)
            rs = part(height, radius, da, True)
            cs = part(breadth, radius, db, True)
            pad_rows = (rs.start, height - rs.stop)
            pad_cols = (cs.start, breadth - cs.stop)
            offset = 0
            for index, width in enumerate(widths):
                piece = got[..., offset : offset + width]
                offset += width
                owns[index] = owns[index] + jnp.pad(piece, (pad_rows, pad_cols, (0, 0)))
    return owns


def partner_rows_product(lhs, weights, axis):
    count = lax.axis_size(axis)
    if count != 2:
        full = lax.all_gather(weights, axis, axis=0, tiled=True)
        return lax.dot_general(lhs, full, TRANS_B, preferred_element_type=jnp.float32).astype(
            jnp.bfloat16
        )
    other = lax.ppermute(weights, axis, [(0, 1), (1, 0)])
    mine_part = lax.dot_general(lhs, weights, TRANS_B, preferred_element_type=jnp.float32)
    other_part = lax.dot_general(lhs, other, TRANS_B, preferred_element_type=jnp.float32)
    mine_part = mine_part.astype(jnp.bfloat16)
    other_part = other_part.astype(jnp.bfloat16)
    first = lax.axis_index(axis) == 0
    return jnp.where(
        first,
        jnp.concatenate([mine_part, other_part], axis=1),
        jnp.concatenate([other_part, mine_part], axis=1),
    )


def exchange_blocks(blocks, axis):
    count = lax.axis_size(axis)
    if count == 2:
        me = lax.axis_index(axis)
        mine = lax.dynamic_index_in_dim(blocks, me, 0, keepdims=False)
        theirs = lax.dynamic_index_in_dim(blocks, 1 - me, 0, keepdims=False)
        got = lax.ppermute(theirs, axis, [(0, 1), (1, 0)])
        return jnp.where(me == 0, jnp.stack([mine, got]), jnp.stack([got, mine]))
    flat = blocks.reshape((-1,) + blocks.shape[2:])
    out = lax.all_to_all(flat, axis, 0, 0, tiled=True)
    return out.reshape(blocks.shape)


def gather_members(value, axis):
    count = lax.axis_size(axis)
    if count == 2:
        me = lax.axis_index(axis)
        got = lax.ppermute(value, axis, [(0, 1), (1, 0)])
        return jnp.where(me == 0, jnp.stack([value, got]), jnp.stack([got, value]))
    return lax.all_gather(value, axis, axis=0, tiled=False)


def shards(tokens, cotangent, valid_cells, w_qkv, w_out):
    inputs_here = tokens[0]
    grad_here = cotangent[0]
    height, breadth, width = inputs_here.shape
    radius = RADIUS
    ext_rows = height + 2 * radius
    ext_cols = breadth + 2 * radius
    pad_cols = -(-ext_cols // 8) * 8
    token_count = height * breadth
    key_count = ext_rows * pad_cols
    flat_inputs = inputs_here.reshape(token_count, width)
    flat_grad = grad_here.reshape(token_count, width)
    dp_count = lax.axis_size("dp")
    lat_count = lax.axis_size("lat")
    lon_count = lax.axis_size("lon")
    rows_half = width // dp_count
    cols_block = width // lon_count
    rows_block = rows_half // lat_count

    tok_ext = halo_gather(inputs_here, radius)
    tok_ext = jnp.pad(tok_ext, ((0, 0), (0, pad_cols - ext_cols), (0, 0)))
    tok_ext = tok_ext.reshape(key_count, width)

    cot_blocks = flat_grad.reshape(token_count, lon_count, cols_block).transpose(1, 0, 2)
    cot_lon = exchange_blocks(cot_blocks, "lon")
    cot_group = gather_members(cot_lon, "dp")

    panels = lax.all_gather(w_qkv, "dp", axis=0, tiled=True)
    grad_attn = partner_rows_product(flat_grad, w_out, "dp")

    query = jnp.dot(flat_inputs, panels[:, :width], preferred_element_type=jnp.float32)
    query = query.astype(jnp.bfloat16)
    key_values = jnp.dot(tok_ext, panels[:, width:], preferred_element_type=jnp.float32)
    key_values = key_values.astype(jnp.bfloat16)

    wrapped = jnp.concatenate(
        [valid_cells[:, -radius:], valid_cells, valid_cells[:, :radius]], axis=1
    )
    framed = jnp.pad(wrapped, ((radius, radius), (0, 0)))
    valid_ext = lax.dynamic_slice(
        framed,
        (lax.axis_index("lat") * height, lax.axis_index("lon") * breadth),
        (ext_rows, ext_cols),
    )
    valid_ext = jnp.pad(valid_ext, ((0, 0), (0, pad_cols - ext_cols))).reshape(1, key_count)
    query_pos = jnp.arange(token_count)
    key_pos = jnp.arange(key_count)
    delta_row = (key_pos // pad_cols)[None, :] - radius - (query_pos // breadth)[:, None]
    delta_col = (key_pos % pad_cols)[None, :] - radius - (query_pos % breadth)[:, None]
    inside = (jnp.abs(delta_row) <= radius) & (jnp.abs(delta_col) <= radius)
    itself = (delta_row == 0) & (delta_col == 0)
    allowed = (inside & ((valid_ext == 1) | itself)).astype(jnp.float32)

    attended, grad_query, grad_keys, grad_values = block_attention(
        query, key_values, grad_attn, allowed, HEADS
    )

    att_blocks = attended.reshape(token_count, dp_count, rows_half).transpose(1, 0, 2)
    att_dp = exchange_blocks(att_blocks, "dp")
    att_group = gather_members(att_dp, "lon")
    att_group = att_group.transpose(1, 0, 2, 3).reshape(-1, rows_half)
    cot_group = cot_group.reshape(-1, cols_block)
    device_count = dp_count * lat_count * lon_count
    partial = lax.dot_general(
        att_group, cot_group, (((0,), (0,)), ((), ())), preferred_element_type=jnp.float32
    ) * (1.0 / device_count)
    lat_index = lax.axis_index("lat")
    total = lax.dynamic_slice_in_dim(partial, lat_index * rows_block, rows_block, axis=0)
    for shift in range(1, lat_count):
        target = (lat_index + shift) % lat_count
        piece = lax.dynamic_slice_in_dim(partial, target * rows_block, rows_block, axis=0)
        pairs = [(i, (i + shift) % lat_count) for i in range(lat_count)]
        total = total + lax.ppermute(piece, "lat", pairs)
    d_w_out = total

    grad_k_ext = grad_keys.reshape(ext_rows, pad_cols, width)[:, :ext_cols]
    grad_v_ext = grad_values.reshape(ext_rows, pad_cols, width)[:, :ext_cols]
    grad_k_own, grad_v_own = halo_return([grad_k_ext, grad_v_ext], height, breadth, radius)
    grad_proj = jnp.concatenate(
        [
            grad_query,
            grad_k_own.astype(jnp.bfloat16).reshape(token_count, width),
            grad_v_own.astype(jnp.bfloat16).reshape(token_count, width),
        ],
        axis=1,
    )
    d_flat = lax.dot_general(grad_proj, panels, TRANS_B, preferred_element_type=jnp.float32)
    d_input = d_flat.astype(jnp.bfloat16).reshape(1, height, breadth, width)
    return (d_input, d_w_out)


def solution(mesh):
    in_specs = (
        P("dp", "lat", "lon", None),
        P("dp", "lat", "lon", None),
        P(),
        P("dp", None),
        P("dp", None),
    )
    out_specs = (P("dp", "lat", "lon", None), P(("dp", "lat"), "lon"))
    return jax.shard_map(shards, mesh=mesh, in_specs=in_specs, out_specs=out_specs, check_vma=False)
```

```python
import functools

import jax
import jax.numpy as jnp
from jax import lax
from jax.experimental import pallas as pl
from jax.sharding import PartitionSpec as P

HEADS = 16
RADIUS = 6

TRANS_B = (((1,), (1,)), ((), ()))


def passed_along(value, axis, steps):
    count = lax.axis_size(axis)
    pairs = [(source, (source + steps) % count) for source in range(count)]
    return lax.ppermute(value, axis, pairs)


def shifted(value, axis, by):
    count = lax.axis_size(axis)
    pairs = [(i, i + by) for i in range(count) if 0 <= i + by < count]
    return lax.ppermute(value, axis, pairs)


def extended(block, sides, width, periodic):
    for axis, dim in sides:
        count = lax.axis_size(axis)
        forward = [(i, i + 1) for i in range(count - 1)]
        if periodic:
            forward.append((count - 1, 0))
        backward = [(target, source) for source, target in forward]
        low = lax.ppermute(
            lax.slice_in_dim(block, block.shape[dim] - width, None, axis=dim), axis, forward
        )
        high = lax.ppermute(lax.slice_in_dim(block, 0, width, axis=dim), axis, backward)
        block = jnp.concatenate([low, block, high], axis=dim)
    return block


def attention_kernel(q_ref, k_ref, v_ref, g_ref, allow_ref, att_ref, gq_ref, gk_ref, gv_ref,
                     *, head_dim, scale):
    q = q_ref[...]
    k = k_ref[...]
    v = v_ref[...]
    g = g_ref[...]
    allowed = allow_ref[...] > 0.0
    lanes = q.shape[1]
    lane = lax.broadcasted_iota(jnp.int32, (1, lanes), 1)
    q32 = q.astype(jnp.float32)
    g32 = g.astype(jnp.float32)
    att = jnp.zeros(q.shape, jnp.float32)
    gq = jnp.zeros(q.shape, jnp.float32)
    gk = jnp.zeros(k.shape, jnp.float32)
    gv = jnp.zeros(v.shape, jnp.float32)
    for j in range(lanes // head_dim):
        sel = (lane >= j * head_dim) & (lane < (j + 1) * head_dim)
        qj = jnp.where(sel, q32, 0.0).astype(jnp.bfloat16)
        gj = jnp.where(sel, g32, 0.0).astype(jnp.bfloat16)
        scores = lax.dot_general(qj, k, TRANS_B, preferred_element_type=jnp.float32) * scale
        peak = jnp.max(jnp.where(allowed, scores, -jnp.inf), axis=1, keepdims=True)
        weights = jnp.where(allowed, jnp.exp(scores - peak), 0.0)
        probs = weights / jnp.sum(weights, axis=1, keepdims=True)
        probs_low = probs.astype(jnp.bfloat16)
        att_j = jnp.dot(probs_low, v, preferred_element_type=jnp.float32)
        grad_probs = lax.dot_general(gj, v, TRANS_B, preferred_element_type=jnp.float32)
        centre = jnp.sum(probs * grad_probs, axis=1, keepdims=True)
        grad_scores = (probs * (grad_probs - centre) * scale).astype(jnp.bfloat16)
        gq_j = jnp.dot(grad_scores, k, preferred_element_type=jnp.float32)
        scores_t = grad_scores.astype(jnp.float32).T.astype(jnp.bfloat16)
        probs_t = probs_low.astype(jnp.float32).T.astype(jnp.bfloat16)
        gk_j = jnp.dot(scores_t, q, preferred_element_type=jnp.float32)
        gv_j = jnp.dot(probs_t, g, preferred_element_type=jnp.float32)
        att = jnp.where(sel, att_j, att)
        gq = jnp.where(sel, gq_j, gq)
        gk = jnp.where(sel, gk_j, gk)
        gv = jnp.where(sel, gv_j, gv)
    att_ref[...] = att.astype(att_ref.dtype)
    gq_ref[...] = gq.astype(gq_ref.dtype)
    gk_ref[...] = gk
    gv_ref[...] = gv


def block_attention(query, key_values, grad_attn, allowed, heads):
    queries, width = query.shape
    keys = key_values.shape[0]
    head_dim = width // heads
    lanes = 128
    pairs = width // lanes
    kernel = functools.partial(attention_kernel, head_dim=head_dim, scale=head_dim ** (-0.5))
    flops = 2 * queries * keys * width * 2 * 6
    cost = pl.CostEstimate(
        flops=flops,
        transcendentals=queries * keys * heads,
        bytes_accessed=2 * (2 * queries * width + 2 * keys * width + 2 * queries * width)
        + 4 * queries * keys + 4 * 2 * keys * width,
    )
    return pl.pallas_call(
        kernel,
        grid=(pairs,),
        in_specs=[
            pl.BlockSpec((queries, lanes), lambda h: (0, h)),
            pl.BlockSpec((keys, lanes), lambda h: (0, h)),
            pl.BlockSpec((keys, lanes), lambda h: (0, h + pairs)),
            pl.BlockSpec((queries, lanes), lambda h: (0, h)),
            pl.BlockSpec((queries, keys), lambda h: (0, 0)),
        ],
        out_specs=[
            pl.BlockSpec((queries, lanes), lambda h: (0, h)),
            pl.BlockSpec((queries, lanes), lambda h: (0, h)),
            pl.BlockSpec((keys, lanes), lambda h: (0, h)),
            pl.BlockSpec((keys, lanes), lambda h: (0, h)),
        ],
        out_shape=[
            jax.ShapeDtypeStruct((queries, width), jnp.bfloat16),
            jax.ShapeDtypeStruct((queries, width), jnp.bfloat16),
            jax.ShapeDtypeStruct((keys, width), jnp.float32),
            jax.ShapeDtypeStruct((keys, width), jnp.float32),
        ],
        cost_estimate=cost,
        name="block_attention",
    )(query, key_values, key_values, grad_attn, allowed)


def grid_pairs(delta_lat, delta_lon):
    lat_count = lax.axis_size("lat")
    lon_count = lax.axis_size("lon")
    pairs = []
    for la in range(lat_count):
        if 0 <= la + delta_lat < lat_count:
            for lo in range(lon_count):
                target = (la + delta_lat) * lon_count + (lo + delta_lon) % lon_count
                pairs.append((la * lon_count + lo, target))
    return pairs


def sent_to(value, delta_lat, delta_lon):
    return lax.ppermute(value, ("lat", "lon"), grid_pairs(delta_lat, delta_lon))


def part(count, radius, step, giving):
    if step == 0:
        return slice(0, count)
    if (step < 0) == giving:
        return slice(count - radius, count)
    return slice(0, radius)


def halo_gather(block, radius):
    height, breadth = block.shape[0], block.shape[1]
    rows = []
    for da in (-1, 0, 1):
        row = []
        for db in (-1, 0, 1):
            if da == 0 and db == 0:
                row.append(block)
                continue
            piece = block[part(height, radius, da, True), part(breadth, radius, db, True)]
            row.append(sent_to(piece, -da, -db))
        rows.append(jnp.concatenate(row, axis=1))
    return jnp.concatenate(rows, axis=0)


def halo_return(ext_list, height, breadth, radius):
    row_slices = {-1: slice(0, radius), 0: slice(radius, radius + height), 1: slice(radius + height, None)}
    col_slices = {-1: slice(0, radius), 0: slice(radius, radius + breadth), 1: slice(radius + breadth, None)}
    owns = [ext[row_slices[0], col_slices[0]] for ext in ext_list]
    widths = [ext.shape[-1] for ext in ext_list]
    for da in (-1, 0, 1):
        for db in (-1, 0, 1):
            if da == 0 and db == 0:
                continue
            pieces = [ext[row_slices[da], col_slices[db]] for ext in ext_list]
            joined = jnp.concatenate(pieces, axis=-1).astype(jnp.bfloat16)
            got = sent_to(joined, da, db).astype(jnp.float32)
            rs = part(height, radius, da, True)
            cs = part(breadth, radius, db, True)
            pad_rows = (rs.start, height - rs.stop)
            pad_cols = (cs.start, breadth - cs.stop)
            offset = 0
            for index, width in enumerate(widths):
                piece = got[..., offset : offset + width]
                offset += width
                owns[index] = owns[index] + jnp.pad(piece, (pad_rows, pad_cols, (0, 0)))
    return owns


def partner_rows_product(lhs, weights, axis):
    count = lax.axis_size(axis)
    if count != 2:
        full = lax.all_gather(weights, axis, axis=0, tiled=True)
        return lax.dot_general(lhs, full, TRANS_B, preferred_element_type=jnp.float32).astype(
            jnp.bfloat16
        )
    other = lax.ppermute(weights, axis, [(0, 1), (1, 0)])
    mine_part = lax.dot_general(lhs, weights, TRANS_B, preferred_element_type=jnp.float32)
    other_part = lax.dot_general(lhs, other, TRANS_B, preferred_element_type=jnp.float32)
    mine_part = mine_part.astype(jnp.bfloat16)
    other_part = other_part.astype(jnp.bfloat16)
    first = lax.axis_index(axis) == 0
    return jnp.where(
        first,
        jnp.concatenate([mine_part, other_part], axis=1),
        jnp.concatenate([other_part, mine_part], axis=1),
    )


def exchange_blocks(blocks, axis):
    count = lax.axis_size(axis)
    if count == 2:
        me = lax.axis_index(axis)
        mine = lax.dynamic_index_in_dim(blocks, me, 0, keepdims=False)
        theirs = lax.dynamic_index_in_dim(blocks, 1 - me, 0, keepdims=False)
        got = lax.ppermute(theirs, axis, [(0, 1), (1, 0)])
        return jnp.where(me == 0, jnp.stack([mine, got]), jnp.stack([got, mine]))
    flat = blocks.reshape((-1,) + blocks.shape[2:])
    out = lax.all_to_all(flat, axis, 0, 0, tiled=True)
    return out.reshape(blocks.shape)


def gather_members(value, axis):
    count = lax.axis_size(axis)
    if count == 2:
        me = lax.axis_index(axis)
        got = lax.ppermute(value, axis, [(0, 1), (1, 0)])
        return jnp.where(me == 0, jnp.stack([value, got]), jnp.stack([got, value]))
    return lax.all_gather(value, axis, axis=0, tiled=False)


def swap(value, axis):
    return lax.ppermute(value, axis, [(0, 1), (1, 0)])


def columns(value, index, size):
    return lax.dynamic_slice_in_dim(value, index * size, size, axis=1)


def split_rows(joined, shapes):
    out = []
    offset = 0
    for shape in shapes:
        count = 1
        for extent in shape[:-1]:
            count *= extent
        count = count * shape[-1] // joined.shape[-1]
        out.append(joined[offset : offset + count].reshape(shape))
        offset += count
    return out


def join_rows(parts, lanes):
    return jnp.concatenate([p.reshape(-1, lanes) for p in parts], axis=0)


def lat_return(ext_list, height, radius):
    owns = []
    tops = join_rows([ext[:radius] for ext in ext_list], ext_list[0].shape[-1])
    bottoms = join_rows([ext[radius + height :] for ext in ext_list], ext_list[0].shape[-1])
    shapes = [ext[:radius].shape for ext in ext_list]
    from_below = split_rows(shifted(tops.astype(jnp.bfloat16), "lat", -1), shapes)
    from_above = split_rows(shifted(bottoms.astype(jnp.bfloat16), "lat", 1), shapes)
    for ext, below, above in zip(ext_list, from_below, from_above):
        middle = (
            ext[radius : radius + height]
            + jnp.pad(below.astype(jnp.float32), ((height - radius, 0), (0, 0), (0, 0)))
            + jnp.pad(above.astype(jnp.float32), ((0, height - radius), (0, 0), (0, 0)))
        )
        owns.append(middle)
    return owns


def add_lon_rims(mid_list, from_right, from_left, breadth, radius):
    owns = []
    for mid, right, left in zip(mid_list, from_right, from_left):
        owns.append(
            mid[:, radius : radius + breadth]
            + jnp.pad(right.astype(jnp.float32), ((0, 0), (breadth - radius, 0), (0, 0)))
            + jnp.pad(left.astype(jnp.float32), ((0, 0), (0, breadth - radius), (0, 0)))
        )
    return owns


def shards(tokens, cotangent, valid_cells, w_qkv, w_out):
    inputs_here = tokens[0]
    grad_here = cotangent[0]
    height, breadth, width = inputs_here.shape
    radius = RADIUS
    ext_rows = height + 2 * radius
    ext_cols = breadth + 2 * radius
    pad_cols = -(-ext_cols // 8) * 8
    token_count = height * breadth
    key_count = ext_rows * pad_cols
    flat_inputs = inputs_here.reshape(token_count, width)
    flat_grad = grad_here.reshape(token_count, width)
    dp_count = lax.axis_size("dp")
    lat_count = lax.axis_size("lat")
    lon_count = lax.axis_size("lon")
    rows_half = width // dp_count
    cols_block = width // lon_count
    rows_block = rows_half // lat_count
    dp_index = lax.axis_index("dp")
    lon_index = lax.axis_index("lon")
    fast = dp_count == 2 and lon_count == 2

    panels = lax.all_gather(w_qkv, "dp", axis=0, tiled=True)

    if fast:
        dp_got = swap(jnp.concatenate([w_out, flat_grad], axis=0), "dp")
        w_out_other = dp_got[: w_out.shape[0]]
        cot_dp = dp_got[w_out.shape[0] :]
        cot_send = jnp.concatenate(
            [columns(flat_grad, 1 - lon_index, cols_block), columns(cot_dp, 1 - lon_index, cols_block)],
            axis=0,
        )
        first = inputs_here[:, :radius]
        last = inputs_here[:, breadth - radius :]
        lon_got = swap(join_rows([last, first, cot_send], width), "lon")
        its_last, its_first, cot_lon = split_rows(
            lon_got, [last.shape, first.shape, cot_send.shape]
        )
        tok_lon = jnp.concatenate([its_last, inputs_here, its_first], axis=1)
        cot_group = jnp.concatenate(
            [
                columns(flat_grad, lon_index, cols_block),
                columns(cot_dp, lon_index, cols_block),
                cot_lon,
            ],
            axis=0,
        )
        mine_part = lax.dot_general(flat_grad, w_out, TRANS_B, preferred_element_type=jnp.float32)
        other_part = lax.dot_general(
            flat_grad, w_out_other, TRANS_B, preferred_element_type=jnp.float32
        )
        mine_part = mine_part.astype(jnp.bfloat16)
        other_part = other_part.astype(jnp.bfloat16)
        grad_attn = jnp.where(
            dp_index == 0,
            jnp.concatenate([mine_part, other_part], axis=1),
            jnp.concatenate([other_part, mine_part], axis=1),
        )
    else:
        tok_lon = extended(inputs_here, (("lon", 1),), radius, True)
        cot_blocks = flat_grad.reshape(token_count, lon_count, cols_block).transpose(1, 0, 2)
        cot_lon = exchange_blocks(cot_blocks, "lon")
        cot_group = gather_members(cot_lon, "dp").reshape(-1, cols_block)
        grad_attn = partner_rows_product(flat_grad, w_out, "dp")

    tok_ext = extended(tok_lon, (("lat", 0),), radius, False)
    tok_ext = jnp.pad(tok_ext, ((0, 0), (0, pad_cols - ext_cols), (0, 0)))
    tok_ext = tok_ext.reshape(key_count, width)

    query = jnp.dot(flat_inputs, panels[:, :width], preferred_element_type=jnp.float32)
    query = query.astype(jnp.bfloat16)
    key_values = jnp.dot(tok_ext, panels[:, width:], preferred_element_type=jnp.float32)
    key_values = key_values.astype(jnp.bfloat16)

    wrapped = jnp.concatenate(
        [valid_cells[:, -radius:], valid_cells, valid_cells[:, :radius]], axis=1
    )
    framed = jnp.pad(wrapped, ((radius, radius), (0, 0)))
    valid_ext = lax.dynamic_slice(
        framed,
        (lax.axis_index("lat") * height, lon_index * breadth),
        (ext_rows, ext_cols),
    )
    valid_ext = jnp.pad(valid_ext, ((0, 0), (0, pad_cols - ext_cols))).reshape(1, key_count)
    query_pos = jnp.arange(token_count)
    key_pos = jnp.arange(key_count)
    delta_row = (key_pos // pad_cols)[None, :] - radius - (query_pos // breadth)[:, None]
    delta_col = (key_pos % pad_cols)[None, :] - radius - (query_pos % breadth)[:, None]
    inside = (jnp.abs(delta_row) <= radius) & (jnp.abs(delta_col) <= radius)
    itself = (delta_row == 0) & (delta_col == 0)
    allowed = (inside & ((valid_ext == 1) | itself)).astype(jnp.float32)

    attended, grad_query, grad_keys, grad_values = block_attention(
        query, key_values, grad_attn, allowed, HEADS
    )

    grad_k_ext = grad_keys.reshape(ext_rows, pad_cols, width)[:, :ext_cols]
    grad_v_ext = grad_values.reshape(ext_rows, pad_cols, width)[:, :ext_cols]
    mids = lat_return([grad_k_ext, grad_v_ext], height, radius)
    lefts = [mid[:, :radius] for mid in mids]
    rights = [mid[:, radius + breadth :] for mid in mids]

    if fast:
        own_att = columns(attended, dp_index, rows_half)
        att_from_dp = swap(columns(attended, 1 - dp_index, rows_half), "dp")
        att_dp = jnp.concatenate([own_att, att_from_dp], axis=0)
        lanes = 2 * width
        rim_parts = [p.astype(jnp.bfloat16) for p in lefts + rights]
        got = swap(join_rows(rim_parts + [att_dp], lanes), "lon")
        pieces = split_rows(got, [p.shape for p in rim_parts] + [att_dp.shape])
        from_right = pieces[:2]
        from_left = pieces[2:4]
        att_group = jnp.concatenate([att_dp, pieces[4]], axis=0)
    else:
        from_right = [passed_along(p.astype(jnp.bfloat16), "lon", -1) for p in lefts]
        from_left = [passed_along(p.astype(jnp.bfloat16), "lon", 1) for p in rights]
        att_blocks = attended.reshape(token_count, dp_count, rows_half).transpose(1, 0, 2)
        att_dp = exchange_blocks(att_blocks, "dp")
        att_group = gather_members(att_dp, "lon")
        att_group = att_group.transpose(1, 0, 2, 3).reshape(-1, rows_half)
    grad_k_own, grad_v_own = add_lon_rims(mids, from_right, from_left, breadth, radius)

    device_count = dp_count * lat_count * lon_count
    partial = lax.dot_general(
        att_group, cot_group, (((0,), (0,)), ((), ())), preferred_element_type=jnp.float32
    ) * (1.0 / device_count)
    spread = lax.all_to_all(partial, "lat", 0, 0, tiled=True)
    d_w_out = spread.reshape(lat_count, rows_block, cols_block).sum(axis=0)

    grad_proj = jnp.concatenate(
        [
            grad_query,
            grad_k_own.astype(jnp.bfloat16).reshape(token_count, width),
            grad_v_own.astype(jnp.bfloat16).reshape(token_count, width),
        ],
        axis=1,
    )
    d_flat = lax.dot_general(grad_proj, panels, TRANS_B, preferred_element_type=jnp.float32)
    d_input = d_flat.astype(jnp.bfloat16).reshape(1, height, breadth, width)
    return (d_input, d_w_out)


def solution(mesh):
    in_specs = (
        P("dp", "lat", "lon", None),
        P("dp", "lat", "lon", None),
        P(),
        P("dp", None),
        P("dp", None),
    )
    out_specs = (P("dp", "lat", "lon", None), P(("dp", "lat"), "lon"))
    return jax.shard_map(shards, mesh=mesh, in_specs=in_specs, out_specs=out_specs, check_vma=False)
```

```python
import functools

import jax
import jax.numpy as jnp
from jax import lax
from jax.experimental import pallas as pl
from jax.sharding import PartitionSpec as P

HEADS = 16
RADIUS = 6

TRANS_B = (((1,), (1,)), ((), ()))


def passed_along(value, axis, steps):
    count = lax.axis_size(axis)
    pairs = [(source, (source + steps) % count) for source in range(count)]
    return lax.ppermute(value, axis, pairs)


def shifted(value, axis, by):
    count = lax.axis_size(axis)
    pairs = [(i, i + by) for i in range(count) if 0 <= i + by < count]
    return lax.ppermute(value, axis, pairs)


def extended(block, sides, width, periodic):
    for axis, dim in sides:
        count = lax.axis_size(axis)
        forward = [(i, i + 1) for i in range(count - 1)]
        if periodic:
            forward.append((count - 1, 0))
        backward = [(target, source) for source, target in forward]
        low = lax.ppermute(
            lax.slice_in_dim(block, block.shape[dim] - width, None, axis=dim), axis, forward
        )
        high = lax.ppermute(lax.slice_in_dim(block, 0, width, axis=dim), axis, backward)
        block = jnp.concatenate([low, block, high], axis=dim)
    return block


def attention_kernel(q_ref, k_ref, v_ref, g_ref, allow_ref, att_ref, gq_ref, gk_ref, gv_ref,
                     *, head_dim, scale):
    q = q_ref[...]
    k = k_ref[...]
    v = v_ref[...]
    g = g_ref[...]
    allowed = allow_ref[...] > 0.0
    lanes = q.shape[1]
    lane = lax.broadcasted_iota(jnp.int32, (1, lanes), 1)
    q32 = q.astype(jnp.float32)
    g32 = g.astype(jnp.float32)
    att = jnp.zeros(q.shape, jnp.float32)
    gq = jnp.zeros(q.shape, jnp.float32)
    gk = jnp.zeros(k.shape, jnp.float32)
    gv = jnp.zeros(v.shape, jnp.float32)
    for j in range(lanes // head_dim):
        sel = (lane >= j * head_dim) & (lane < (j + 1) * head_dim)
        qj = jnp.where(sel, q32, 0.0).astype(jnp.bfloat16)
        gj = jnp.where(sel, g32, 0.0).astype(jnp.bfloat16)
        scores = lax.dot_general(qj, k, TRANS_B, preferred_element_type=jnp.float32) * scale
        peak = jnp.max(jnp.where(allowed, scores, -jnp.inf), axis=1, keepdims=True)
        weights = jnp.where(allowed, jnp.exp(scores - peak), 0.0)
        probs = weights / jnp.sum(weights, axis=1, keepdims=True)
        probs_low = probs.astype(jnp.bfloat16)
        att_j = jnp.dot(probs_low, v, preferred_element_type=jnp.float32)
        grad_probs = lax.dot_general(gj, v, TRANS_B, preferred_element_type=jnp.float32)
        centre = jnp.sum(probs * grad_probs, axis=1, keepdims=True)
        grad_scores = (probs * (grad_probs - centre) * scale).astype(jnp.bfloat16)
        gq_j = jnp.dot(grad_scores, k, preferred_element_type=jnp.float32)
        scores_t = grad_scores.astype(jnp.float32).T.astype(jnp.bfloat16)
        probs_t = probs_low.astype(jnp.float32).T.astype(jnp.bfloat16)
        gk_j = jnp.dot(scores_t, q, preferred_element_type=jnp.float32)
        gv_j = jnp.dot(probs_t, g, preferred_element_type=jnp.float32)
        att = jnp.where(sel, att_j, att)
        gq = jnp.where(sel, gq_j, gq)
        gk = jnp.where(sel, gk_j, gk)
        gv = jnp.where(sel, gv_j, gv)
    att_ref[...] = att.astype(att_ref.dtype)
    gq_ref[...] = gq.astype(gq_ref.dtype)
    gk_ref[...] = gk
    gv_ref[...] = gv


def block_attention(query, key_values, grad_attn, allowed, heads):
    queries, width = query.shape
    keys = key_values.shape[0]
    head_dim = width // heads
    lanes = 128
    pairs = width // lanes
    kernel = functools.partial(attention_kernel, head_dim=head_dim, scale=head_dim ** (-0.5))
    flops = 2 * queries * keys * width * 2 * 6
    cost = pl.CostEstimate(
        flops=flops,
        transcendentals=queries * keys * heads,
        bytes_accessed=2 * (2 * queries * width + 2 * keys * width + 2 * queries * width)
        + 4 * queries * keys + 4 * 2 * keys * width,
    )
    return pl.pallas_call(
        kernel,
        grid=(pairs,),
        in_specs=[
            pl.BlockSpec((queries, lanes), lambda h: (0, h)),
            pl.BlockSpec((keys, lanes), lambda h: (0, h)),
            pl.BlockSpec((keys, lanes), lambda h: (0, h + pairs)),
            pl.BlockSpec((queries, lanes), lambda h: (0, h)),
            pl.BlockSpec((queries, keys), lambda h: (0, 0)),
        ],
        out_specs=[
            pl.BlockSpec((queries, lanes), lambda h: (0, h)),
            pl.BlockSpec((queries, lanes), lambda h: (0, h)),
            pl.BlockSpec((keys, lanes), lambda h: (0, h)),
            pl.BlockSpec((keys, lanes), lambda h: (0, h)),
        ],
        out_shape=[
            jax.ShapeDtypeStruct((queries, width), jnp.bfloat16),
            jax.ShapeDtypeStruct((queries, width), jnp.bfloat16),
            jax.ShapeDtypeStruct((keys, width), jnp.float32),
            jax.ShapeDtypeStruct((keys, width), jnp.float32),
        ],
        cost_estimate=cost,
        name="block_attention",
    )(query, key_values, key_values, grad_attn, allowed)


def grid_pairs(delta_lat, delta_lon):
    lat_count = lax.axis_size("lat")
    lon_count = lax.axis_size("lon")
    pairs = []
    for la in range(lat_count):
        if 0 <= la + delta_lat < lat_count:
            for lo in range(lon_count):
                target = (la + delta_lat) * lon_count + (lo + delta_lon) % lon_count
                pairs.append((la * lon_count + lo, target))
    return pairs


def sent_to(value, delta_lat, delta_lon):
    return lax.ppermute(value, ("lat", "lon"), grid_pairs(delta_lat, delta_lon))


def part(count, radius, step, giving):
    if step == 0:
        return slice(0, count)
    if (step < 0) == giving:
        return slice(count - radius, count)
    return slice(0, radius)


def grouped_send(pieces, lanes):
    lon_count = lax.axis_size("lon")
    groups = {}
    for index, (dl, db, value) in enumerate(pieces):
        groups.setdefault((dl, db % lon_count), []).append(index)
    out = [None] * len(pieces)
    for (dl, db), members in groups.items():
        values = [pieces[i][2] for i in members]
        got = sent_to(join_rows(values, lanes), dl, db)
        for i, piece in zip(members, split_rows(got, [v.shape for v in values])):
            out[i] = piece
    return out


def halo_gather(block, radius):
    height, breadth, lanes = block.shape
    spots = []
    pieces = []
    for da in (-1, 0, 1):
        for db in (-1, 0, 1):
            if da == 0 and db == 0:
                continue
            piece = block[part(height, radius, da, True), part(breadth, radius, db, True)]
            spots.append((da, db))
            pieces.append((-da, -db, piece))
    got = dict(zip(spots, grouped_send(pieces, lanes)))
    got[(0, 0)] = block
    rows = [jnp.concatenate([got[(da, db)] for db in (-1, 0, 1)], axis=1) for da in (-1, 0, 1)]
    return jnp.concatenate(rows, axis=0)


def halo_return(ext_list, height, breadth, radius):
    row_slices = {-1: slice(0, radius), 0: slice(radius, radius + height), 1: slice(radius + height, None)}
    col_slices = {-1: slice(0, radius), 0: slice(radius, radius + breadth), 1: slice(radius + breadth, None)}
    owns = [ext[row_slices[0], col_slices[0]] for ext in ext_list]
    widths = [ext.shape[-1] for ext in ext_list]
    spots = []
    pieces = []
    for da in (-1, 0, 1):
        for db in (-1, 0, 1):
            if da == 0 and db == 0:
                continue
            joined = jnp.concatenate(
                [ext[row_slices[da], col_slices[db]] for ext in ext_list], axis=-1
            ).astype(jnp.bfloat16)
            spots.append((da, db))
            pieces.append((da, db, joined))
    for (da, db), got in zip(spots, grouped_send(pieces, sum(widths))):
        rs = part(height, radius, da, True)
        cs = part(breadth, radius, db, True)
        pad_rows = (rs.start, height - rs.stop)
        pad_cols = (cs.start, breadth - cs.stop)
        offset = 0
        for index, width in enumerate(widths):
            piece = got[..., offset : offset + width].astype(jnp.float32)
            offset += width
            owns[index] = owns[index] + jnp.pad(piece, (pad_rows, pad_cols, (0, 0)))
    return owns


def partner_rows_product(lhs, weights, axis):
    count = lax.axis_size(axis)
    if count != 2:
        full = lax.all_gather(weights, axis, axis=0, tiled=True)
        return lax.dot_general(lhs, full, TRANS_B, preferred_element_type=jnp.float32).astype(
            jnp.bfloat16
        )
    other = lax.ppermute(weights, axis, [(0, 1), (1, 0)])
    mine_part = lax.dot_general(lhs, weights, TRANS_B, preferred_element_type=jnp.float32)
    other_part = lax.dot_general(lhs, other, TRANS_B, preferred_element_type=jnp.float32)
    mine_part = mine_part.astype(jnp.bfloat16)
    other_part = other_part.astype(jnp.bfloat16)
    first = lax.axis_index(axis) == 0
    return jnp.where(
        first,
        jnp.concatenate([mine_part, other_part], axis=1),
        jnp.concatenate([other_part, mine_part], axis=1),
    )


def exchange_blocks(blocks, axis):
    count = lax.axis_size(axis)
    if count == 2:
        me = lax.axis_index(axis)
        mine = lax.dynamic_index_in_dim(blocks, me, 0, keepdims=False)
        theirs = lax.dynamic_index_in_dim(blocks, 1 - me, 0, keepdims=False)
        got = lax.ppermute(theirs, axis, [(0, 1), (1, 0)])
        return jnp.where(me == 0, jnp.stack([mine, got]), jnp.stack([got, mine]))
    flat = blocks.reshape((-1,) + blocks.shape[2:])
    out = lax.all_to_all(flat, axis, 0, 0, tiled=True)
    return out.reshape(blocks.shape)


def gather_members(value, axis):
    count = lax.axis_size(axis)
    if count == 2:
        me = lax.axis_index(axis)
        got = lax.ppermute(value, axis, [(0, 1), (1, 0)])
        return jnp.where(me == 0, jnp.stack([value, got]), jnp.stack([got, value]))
    return lax.all_gather(value, axis, axis=0, tiled=False)


def swap(value, axis):
    return lax.ppermute(value, axis, [(0, 1), (1, 0)])


def columns(value, index, size):
    return lax.dynamic_slice_in_dim(value, index * size, size, axis=1)


def split_rows(joined, shapes):
    out = []
    offset = 0
    for shape in shapes:
        count = 1
        for extent in shape[:-1]:
            count *= extent
        count = count * shape[-1] // joined.shape[-1]
        out.append(joined[offset : offset + count].reshape(shape))
        offset += count
    return out


def join_rows(parts, lanes):
    return jnp.concatenate([p.reshape(-1, lanes) for p in parts], axis=0)


def lat_return(ext_list, height, radius):
    owns = []
    tops = join_rows([ext[:radius] for ext in ext_list], ext_list[0].shape[-1])
    bottoms = join_rows([ext[radius + height :] for ext in ext_list], ext_list[0].shape[-1])
    shapes = [ext[:radius].shape for ext in ext_list]
    from_below = split_rows(shifted(tops.astype(jnp.bfloat16), "lat", -1), shapes)
    from_above = split_rows(shifted(bottoms.astype(jnp.bfloat16), "lat", 1), shapes)
    for ext, below, above in zip(ext_list, from_below, from_above):
        middle = (
            ext[radius : radius + height]
            + jnp.pad(below.astype(jnp.float32), ((height - radius, 0), (0, 0), (0, 0)))
            + jnp.pad(above.astype(jnp.float32), ((0, height - radius), (0, 0), (0, 0)))
        )
        owns.append(middle)
    return owns


def add_lon_rims(mid_list, from_right, from_left, breadth, radius):
    owns = []
    for mid, right, left in zip(mid_list, from_right, from_left):
        owns.append(
            mid[:, radius : radius + breadth]
            + jnp.pad(right.astype(jnp.float32), ((0, 0), (breadth - radius, 0), (0, 0)))
            + jnp.pad(left.astype(jnp.float32), ((0, 0), (0, breadth - radius), (0, 0)))
        )
    return owns


def shards(tokens, cotangent, valid_cells, w_qkv, w_out):
    inputs_here = tokens[0]
    grad_here = cotangent[0]
    height, breadth, width = inputs_here.shape
    radius = RADIUS
    ext_rows = height + 2 * radius
    ext_cols = breadth + 2 * radius
    pad_cols = -(-ext_cols // 8) * 8
    token_count = height * breadth
    key_count = ext_rows * pad_cols
    flat_inputs = inputs_here.reshape(token_count, width)
    flat_grad = grad_here.reshape(token_count, width)
    dp_count = lax.axis_size("dp")
    lat_count = lax.axis_size("lat")
    lon_count = lax.axis_size("lon")
    rows_half = width // dp_count
    cols_block = width // lon_count
    rows_block = rows_half // lat_count
    dp_index = lax.axis_index("dp")
    lon_index = lax.axis_index("lon")
    fast = dp_count == 2 and lon_count == 2

    if fast:
        qkv_other = swap(w_qkv, "dp")
        dp_got = swap(jnp.concatenate([w_out, flat_grad], axis=0), "dp")
        w_out_other = dp_got[: w_out.shape[0]]
        cot_dp = dp_got[w_out.shape[0] :]
        cot_send = jnp.concatenate(
            [columns(flat_grad, 1 - lon_index, cols_block), columns(cot_dp, 1 - lon_index, cols_block)],
            axis=0,
        )
        cot_lon = swap(cot_send, "lon")
        cot_group = jnp.concatenate(
            [
                columns(flat_grad, lon_index, cols_block),
                columns(cot_dp, lon_index, cols_block),
                cot_lon,
            ],
            axis=0,
        )
        mine_part = lax.dot_general(flat_grad, w_out, TRANS_B, preferred_element_type=jnp.float32)
        other_part = lax.dot_general(
            flat_grad, w_out_other, TRANS_B, preferred_element_type=jnp.float32
        )
        mine_part = mine_part.astype(jnp.bfloat16)
        other_part = other_part.astype(jnp.bfloat16)
        grad_attn = jnp.where(
            dp_index == 0,
            jnp.concatenate([mine_part, other_part], axis=1),
            jnp.concatenate([other_part, mine_part], axis=1),
        )

        def project(rows, start, stop):
            own = jnp.dot(
                columns(rows, dp_index, rows_half), w_qkv[:, start:stop],
                preferred_element_type=jnp.float32,
            )
            other = jnp.dot(
                columns(rows, 1 - dp_index, rows_half), qkv_other[:, start:stop],
                preferred_element_type=jnp.float32,
            )
            return (own + other).astype(jnp.bfloat16)

        def back_project(grads):
            own = lax.dot_general(grads, w_qkv, TRANS_B, preferred_element_type=jnp.float32)
            other = lax.dot_general(grads, qkv_other, TRANS_B, preferred_element_type=jnp.float32)
            own = own.astype(jnp.bfloat16)
            other = other.astype(jnp.bfloat16)
            return jnp.where(
                dp_index == 0,
                jnp.concatenate([own, other], axis=1),
                jnp.concatenate([other, own], axis=1),
            )
    else:
        panels = lax.all_gather(w_qkv, "dp", axis=0, tiled=True)
        cot_blocks = flat_grad.reshape(token_count, lon_count, cols_block).transpose(1, 0, 2)
        cot_lon = exchange_blocks(cot_blocks, "lon")
        cot_group = gather_members(cot_lon, "dp").reshape(-1, cols_block)
        grad_attn = partner_rows_product(flat_grad, w_out, "dp")

        def project(rows, start, stop):
            out = jnp.dot(rows, panels[:, start:stop], preferred_element_type=jnp.float32)
            return out.astype(jnp.bfloat16)

        def back_project(grads):
            out = lax.dot_general(grads, panels, TRANS_B, preferred_element_type=jnp.float32)
            return out.astype(jnp.bfloat16)

    tok_ext = halo_gather(inputs_here, radius)
    tok_ext = jnp.pad(tok_ext, ((0, 0), (0, pad_cols - ext_cols), (0, 0)))
    tok_ext = tok_ext.reshape(key_count, width)

    query = project(flat_inputs, 0, width)
    key_values = project(tok_ext, width, 3 * width)

    wrapped = jnp.concatenate(
        [valid_cells[:, -radius:], valid_cells, valid_cells[:, :radius]], axis=1
    )
    framed = jnp.pad(wrapped, ((radius, radius), (0, 0)))
    valid_ext = lax.dynamic_slice(
        framed,
        (lax.axis_index("lat") * height, lon_index * breadth),
        (ext_rows, ext_cols),
    )
    valid_ext = jnp.pad(valid_ext, ((0, 0), (0, pad_cols - ext_cols))).reshape(1, key_count)
    query_pos = jnp.arange(token_count)
    key_pos = jnp.arange(key_count)
    delta_row = (key_pos // pad_cols)[None, :] - radius - (query_pos // breadth)[:, None]
    delta_col = (key_pos % pad_cols)[None, :] - radius - (query_pos % breadth)[:, None]
    inside = (jnp.abs(delta_row) <= radius) & (jnp.abs(delta_col) <= radius)
    itself = (delta_row == 0) & (delta_col == 0)
    allowed = (inside & ((valid_ext == 1) | itself)).astype(jnp.float32)

    attended, grad_query, grad_keys, grad_values = block_attention(
        query, key_values, grad_attn, allowed, HEADS
    )

    grad_k_ext = grad_keys.reshape(ext_rows, pad_cols, width)[:, :ext_cols]
    grad_v_ext = grad_values.reshape(ext_rows, pad_cols, width)[:, :ext_cols]
    grad_k_own, grad_v_own = halo_return([grad_k_ext, grad_v_ext], height, breadth, radius)

    if fast:
        own_att = columns(attended, dp_index, rows_half)
        att_from_dp = swap(columns(attended, 1 - dp_index, rows_half), "dp")
        att_dp = jnp.concatenate([own_att, att_from_dp], axis=0)
        att_group = jnp.concatenate([att_dp, swap(att_dp, "lon")], axis=0)
    else:
        att_blocks = attended.reshape(token_count, dp_count, rows_half).transpose(1, 0, 2)
        att_dp = exchange_blocks(att_blocks, "dp")
        att_group = gather_members(att_dp, "lon")
        att_group = att_group.transpose(1, 0, 2, 3).reshape(-1, rows_half)

    device_count = dp_count * lat_count * lon_count
    partial = lax.dot_general(
        att_group, cot_group, (((0,), (0,)), ((), ())), preferred_element_type=jnp.float32
    ) * (1.0 / device_count)
    spread = lax.all_to_all(partial.astype(jnp.bfloat16), "lat", 0, 0, tiled=True)
    d_w_out = spread.astype(jnp.float32).reshape(lat_count, rows_block, cols_block).sum(axis=0)

    grad_proj = jnp.concatenate(
        [
            grad_query,
            grad_k_own.astype(jnp.bfloat16).reshape(token_count, width),
            grad_v_own.astype(jnp.bfloat16).reshape(token_count, width),
        ],
        axis=1,
    )
    d_input = back_project(grad_proj).reshape(1, height, breadth, width)
    return (d_input, d_w_out)


def solution(mesh):
    in_specs = (
        P("dp", "lat", "lon", None),
        P("dp", "lat", "lon", None),
        P(),
        P("dp", None),
        P("dp", None),
    )
    out_specs = (P("dp", "lat", "lon", None), P(("dp", "lat"), "lon"))
    return jax.shard_map(shards, mesh=mesh, in_specs=in_specs, out_specs=out_specs, check_vma=False)
```

```python
import functools

import jax
import jax.numpy as jnp
from jax import lax
from jax.experimental import pallas as pl
from jax.sharding import PartitionSpec as P

HEADS = 16
RADIUS = 6

TRANS_B = (((1,), (1,)), ((), ()))


def passed_along(value, axis, steps):
    count = lax.axis_size(axis)
    pairs = [(source, (source + steps) % count) for source in range(count)]
    return lax.ppermute(value, axis, pairs)


def shifted(value, axis, by):
    count = lax.axis_size(axis)
    pairs = [(i, i + by) for i in range(count) if 0 <= i + by < count]
    return lax.ppermute(value, axis, pairs)


def extended(block, sides, width, periodic):
    for axis, dim in sides:
        count = lax.axis_size(axis)
        forward = [(i, i + 1) for i in range(count - 1)]
        if periodic:
            forward.append((count - 1, 0))
        backward = [(target, source) for source, target in forward]
        low = lax.ppermute(
            lax.slice_in_dim(block, block.shape[dim] - width, None, axis=dim), axis, forward
        )
        high = lax.ppermute(lax.slice_in_dim(block, 0, width, axis=dim), axis, backward)
        block = jnp.concatenate([low, block, high], axis=dim)
    return block


def attention_kernel(q_ref, kv_ref, g_ref, bias_ref, att_ref, gq_ref, gkv_ref, *, head_dim, scale):
    q = q_ref[...]
    g = g_ref[...]
    lanes = q.shape[1]
    kv = kv_ref[...]
    k = kv[:, :lanes]
    v = kv[:, lanes:]
    bias = bias_ref[...]
    lane = lax.broadcasted_iota(jnp.int32, (1, lanes), 1)
    q32 = q.astype(jnp.float32)
    g32 = g.astype(jnp.float32)
    att = jnp.zeros(q.shape, jnp.float32)
    gq = jnp.zeros(q.shape, jnp.float32)
    gk = jnp.zeros(k.shape, jnp.float32)
    gv = jnp.zeros(v.shape, jnp.float32)
    for j in range(lanes // head_dim):
        sel = (lane >= j * head_dim) & (lane < (j + 1) * head_dim)
        qj = jnp.where(sel, q32, 0.0).astype(jnp.bfloat16)
        gj = jnp.where(sel, g32, 0.0).astype(jnp.bfloat16)
        scores = lax.dot_general(qj, k, TRANS_B, preferred_element_type=jnp.float32) * scale
        masked = scores + bias
        peak = jnp.max(masked, axis=1, keepdims=True)
        weights = jnp.exp(masked - peak)
        probs = weights * (1.0 / jnp.sum(weights, axis=1, keepdims=True))
        probs_low = probs.astype(jnp.bfloat16)
        att_j = jnp.dot(probs_low, v, preferred_element_type=jnp.float32)
        grad_probs = lax.dot_general(gj, v, TRANS_B, preferred_element_type=jnp.float32)
        centre = jnp.sum(probs * grad_probs, axis=1, keepdims=True)
        grad_scores = (probs * (grad_probs - centre) * scale).astype(jnp.bfloat16)
        gq_j = jnp.dot(grad_scores, k, preferred_element_type=jnp.float32)
        scores_t = grad_scores.astype(jnp.float32).T.astype(jnp.bfloat16)
        probs_t = probs_low.astype(jnp.float32).T.astype(jnp.bfloat16)
        gk_j = jnp.dot(scores_t, q, preferred_element_type=jnp.float32)
        gv_j = jnp.dot(probs_t, g, preferred_element_type=jnp.float32)
        att = jnp.where(sel, att_j, att)
        gq = jnp.where(sel, gq_j, gq)
        gk = jnp.where(sel, gk_j, gk)
        gv = jnp.where(sel, gv_j, gv)
    att_ref[...] = att.astype(att_ref.dtype)
    gq_ref[...] = gq.astype(gq_ref.dtype)
    gkv_ref[:, :lanes] = gk
    gkv_ref[:, lanes:] = gv


def block_attention(query, key_values, grad_attn, bias, heads):
    queries, width = query.shape
    keys = key_values.shape[0]
    head_dim = width // heads
    lanes = 128
    pairs = width // lanes
    kernel = functools.partial(attention_kernel, head_dim=head_dim, scale=head_dim ** (-0.5))
    flops = 2 * queries * keys * width * 2 * 6
    cost = pl.CostEstimate(
        flops=flops,
        transcendentals=queries * keys * heads,
        bytes_accessed=2 * (2 * queries * width + 2 * keys * width + 2 * queries * width)
        + 4 * queries * keys + 4 * 2 * keys * width,
    )
    return pl.pallas_call(
        kernel,
        grid=(pairs,),
        in_specs=[
            pl.BlockSpec((queries, lanes), lambda h: (0, h)),
            pl.BlockSpec((keys, 2 * lanes), lambda h: (0, h)),
            pl.BlockSpec((queries, lanes), lambda h: (0, h)),
            pl.BlockSpec((queries, keys), lambda h: (0, 0)),
        ],
        out_specs=[
            pl.BlockSpec((queries, lanes), lambda h: (0, h)),
            pl.BlockSpec((queries, lanes), lambda h: (0, h)),
            pl.BlockSpec((keys, 2 * lanes), lambda h: (0, h)),
        ],
        out_shape=[
            jax.ShapeDtypeStruct((queries, width), jnp.bfloat16),
            jax.ShapeDtypeStruct((queries, width), jnp.bfloat16),
            jax.ShapeDtypeStruct((keys, 2 * width), jnp.float32),
        ],
        cost_estimate=cost,
        name="block_attention",
    )(query, key_values, grad_attn, bias)


def grid_pairs(delta_lat, delta_lon):
    lat_count = lax.axis_size("lat")
    lon_count = lax.axis_size("lon")
    pairs = []
    for la in range(lat_count):
        if 0 <= la + delta_lat < lat_count:
            for lo in range(lon_count):
                target = (la + delta_lat) * lon_count + (lo + delta_lon) % lon_count
                pairs.append((la * lon_count + lo, target))
    return pairs


def sent_to(value, delta_lat, delta_lon):
    return lax.ppermute(value, ("lat", "lon"), grid_pairs(delta_lat, delta_lon))


def part(count, radius, step, giving):
    if step == 0:
        return slice(0, count)
    if (step < 0) == giving:
        return slice(count - radius, count)
    return slice(0, radius)


def grouped_send(pieces):
    lon_count = lax.axis_size("lon")
    groups = {}
    for index, (dl, db, value) in enumerate(pieces):
        groups.setdefault((dl, db % lon_count), []).append(index)
    out = [None] * len(pieces)
    for (dl, db), members in groups.items():
        values = [pieces[i][2] for i in members]
        got = sent_to(jnp.concatenate(values, axis=1), dl, db)
        offset = 0
        for i, value in zip(members, values):
            out[i] = got[:, offset : offset + value.shape[1]]
            offset += value.shape[1]
    return out


def halo_gather(block, radius):
    height, breadth, lanes = block.shape
    spots = []
    pieces = []
    for da in (-1, 0, 1):
        for db in (-1, 0, 1):
            if da == 0 and db == 0:
                continue
            piece = block[part(height, radius, da, True), part(breadth, radius, db, True)]
            spots.append((da, db))
            pieces.append((-da, -db, piece))
    got = dict(zip(spots, grouped_send(pieces)))
    got[(0, 0)] = block
    rows = [jnp.concatenate([got[(da, db)] for db in (-1, 0, 1)], axis=1) for da in (-1, 0, 1)]
    return jnp.concatenate(rows, axis=0)


def halo_return(ext_list, height, breadth, radius):
    row_slices = {-1: slice(0, radius), 0: slice(radius, radius + height), 1: slice(radius + height, None)}
    col_slices = {-1: slice(0, radius), 0: slice(radius, radius + breadth), 1: slice(radius + breadth, None)}
    owns = [ext[row_slices[0], col_slices[0]] for ext in ext_list]
    widths = [ext.shape[-1] for ext in ext_list]
    spots = []
    pieces = []
    for da in (-1, 0, 1):
        for db in (-1, 0, 1):
            if da == 0 and db == 0:
                continue
            joined = jnp.concatenate(
                [ext[row_slices[da], col_slices[db]] for ext in ext_list], axis=-1
            ).astype(jnp.bfloat16)
            spots.append((da, db))
            pieces.append((da, db, joined))
    for (da, db), got in zip(spots, grouped_send(pieces)):
        rs = part(height, radius, da, True)
        cs = part(breadth, radius, db, True)
        pad_rows = (rs.start, height - rs.stop)
        pad_cols = (cs.start, breadth - cs.stop)
        offset = 0
        for index, width in enumerate(widths):
            piece = got[..., offset : offset + width].astype(jnp.float32)
            offset += width
            owns[index] = owns[index] + jnp.pad(piece, (pad_rows, pad_cols, (0, 0)))
    return owns


def partner_rows_product(lhs, weights, axis):
    count = lax.axis_size(axis)
    if count != 2:
        full = lax.all_gather(weights, axis, axis=0, tiled=True)
        return lax.dot_general(lhs, full, TRANS_B, preferred_element_type=jnp.float32).astype(
            jnp.bfloat16
        )
    other = lax.ppermute(weights, axis, [(0, 1), (1, 0)])
    mine_part = lax.dot_general(lhs, weights, TRANS_B, preferred_element_type=jnp.float32)
    other_part = lax.dot_general(lhs, other, TRANS_B, preferred_element_type=jnp.float32)
    mine_part = mine_part.astype(jnp.bfloat16)
    other_part = other_part.astype(jnp.bfloat16)
    first = lax.axis_index(axis) == 0
    return jnp.where(
        first,
        jnp.concatenate([mine_part, other_part], axis=1),
        jnp.concatenate([other_part, mine_part], axis=1),
    )


def exchange_blocks(blocks, axis):
    count = lax.axis_size(axis)
    if count == 2:
        me = lax.axis_index(axis)
        mine = lax.dynamic_index_in_dim(blocks, me, 0, keepdims=False)
        theirs = lax.dynamic_index_in_dim(blocks, 1 - me, 0, keepdims=False)
        got = lax.ppermute(theirs, axis, [(0, 1), (1, 0)])
        return jnp.where(me == 0, jnp.stack([mine, got]), jnp.stack([got, mine]))
    flat = blocks.reshape((-1,) + blocks.shape[2:])
    out = lax.all_to_all(flat, axis, 0, 0, tiled=True)
    return out.reshape(blocks.shape)


def gather_members(value, axis):
    count = lax.axis_size(axis)
    if count == 2:
        me = lax.axis_index(axis)
        got = lax.ppermute(value, axis, [(0, 1), (1, 0)])
        return jnp.where(me == 0, jnp.stack([value, got]), jnp.stack([got, value]))
    return lax.all_gather(value, axis, axis=0, tiled=False)


def arranged(weights, width):
    rows = weights.shape[0]
    lanes = 128
    pairs = width // lanes
    kv = weights[:, width:].reshape(rows, 2, pairs, lanes).transpose(0, 2, 1, 3)
    return weights[:, :width], kv.reshape(rows, 2 * width)


def swap(value, axis):
    return lax.ppermute(value, axis, [(0, 1), (1, 0)])


def columns(value, index, size):
    return lax.dynamic_slice_in_dim(value, index * size, size, axis=1)


def split_rows(joined, shapes):
    out = []
    offset = 0
    for shape in shapes:
        count = 1
        for extent in shape[:-1]:
            count *= extent
        count = count * shape[-1] // joined.shape[-1]
        out.append(joined[offset : offset + count].reshape(shape))
        offset += count
    return out


def join_rows(parts, lanes):
    return jnp.concatenate([p.reshape(-1, lanes) for p in parts], axis=0)


def lat_return(ext_list, height, radius):
    owns = []
    tops = join_rows([ext[:radius] for ext in ext_list], ext_list[0].shape[-1])
    bottoms = join_rows([ext[radius + height :] for ext in ext_list], ext_list[0].shape[-1])
    shapes = [ext[:radius].shape for ext in ext_list]
    from_below = split_rows(shifted(tops.astype(jnp.bfloat16), "lat", -1), shapes)
    from_above = split_rows(shifted(bottoms.astype(jnp.bfloat16), "lat", 1), shapes)
    for ext, below, above in zip(ext_list, from_below, from_above):
        middle = (
            ext[radius : radius + height]
            + jnp.pad(below.astype(jnp.float32), ((height - radius, 0), (0, 0), (0, 0)))
            + jnp.pad(above.astype(jnp.float32), ((0, height - radius), (0, 0), (0, 0)))
        )
        owns.append(middle)
    return owns


def add_lon_rims(mid_list, from_right, from_left, breadth, radius):
    owns = []
    for mid, right, left in zip(mid_list, from_right, from_left):
        owns.append(
            mid[:, radius : radius + breadth]
            + jnp.pad(right.astype(jnp.float32), ((0, 0), (breadth - radius, 0), (0, 0)))
            + jnp.pad(left.astype(jnp.float32), ((0, 0), (0, breadth - radius), (0, 0)))
        )
    return owns


def shards(tokens, cotangent, valid_cells, w_qkv, w_out):
    inputs_here = tokens[0]
    grad_here = cotangent[0]
    height, breadth, width = inputs_here.shape
    radius = RADIUS
    ext_rows = height + 2 * radius
    ext_cols = breadth + 2 * radius
    pad_cols = -(-ext_cols // 8) * 8
    token_count = height * breadth
    key_count = ext_rows * pad_cols
    flat_inputs = inputs_here.reshape(token_count, width)
    flat_grad = grad_here.reshape(token_count, width)
    dp_count = lax.axis_size("dp")
    lat_count = lax.axis_size("lat")
    lon_count = lax.axis_size("lon")
    rows_half = width // dp_count
    cols_block = width // lon_count
    rows_block = rows_half // lat_count
    dp_index = lax.axis_index("dp")
    lon_index = lax.axis_index("lon")
    fast = dp_count == 2 and lon_count == 2

    if fast:
        qkv_other = swap(w_qkv, "dp")
        dp_got = swap(jnp.concatenate([w_out, flat_grad], axis=0), "dp")
        w_out_other = dp_got[: w_out.shape[0]]
        cot_dp = dp_got[w_out.shape[0] :]
        cot_send = jnp.concatenate(
            [columns(flat_grad, 1 - lon_index, cols_block), columns(cot_dp, 1 - lon_index, cols_block)],
            axis=0,
        )
        cot_lon = swap(cot_send, "lon")
        cot_group = jnp.concatenate(
            [
                columns(flat_grad, lon_index, cols_block),
                columns(cot_dp, lon_index, cols_block),
                cot_lon,
            ],
            axis=0,
        )
        mine_part = lax.dot_general(flat_grad, w_out, TRANS_B, preferred_element_type=jnp.float32)
        other_part = lax.dot_general(
            flat_grad, w_out_other, TRANS_B, preferred_element_type=jnp.float32
        )
        mine_part = mine_part.astype(jnp.bfloat16)
        other_part = other_part.astype(jnp.bfloat16)
        grad_attn = jnp.where(
            dp_index == 0,
            jnp.concatenate([mine_part, other_part], axis=1),
            jnp.concatenate([other_part, mine_part], axis=1),
        )

        own_q, own_kv = arranged(w_qkv, width)
        other_q, other_kv = arranged(qkv_other, width)

        def project(rows, own_w, other_w):
            own = jnp.dot(
                columns(rows, dp_index, rows_half), own_w, preferred_element_type=jnp.float32
            )
            other = jnp.dot(
                columns(rows, 1 - dp_index, rows_half), other_w, preferred_element_type=jnp.float32
            )
            return (own + other).astype(jnp.bfloat16)

        def back_project(grad_q, grad_kv):
            own = lax.dot_general(grad_q, own_q, TRANS_B, preferred_element_type=jnp.float32)
            own = own + lax.dot_general(grad_kv, own_kv, TRANS_B, preferred_element_type=jnp.float32)
            other = lax.dot_general(grad_q, other_q, TRANS_B, preferred_element_type=jnp.float32)
            other = other + lax.dot_general(
                grad_kv, other_kv, TRANS_B, preferred_element_type=jnp.float32
            )
            own = own.astype(jnp.bfloat16)
            other = other.astype(jnp.bfloat16)
            return jnp.where(
                dp_index == 0,
                jnp.concatenate([own, other], axis=1),
                jnp.concatenate([other, own], axis=1),
            )

        query = project(flat_inputs, own_q, other_q)
        kv_weights = (own_kv, other_kv)
    else:
        panels = lax.all_gather(w_qkv, "dp", axis=0, tiled=True)
        cot_blocks = flat_grad.reshape(token_count, lon_count, cols_block).transpose(1, 0, 2)
        cot_lon = exchange_blocks(cot_blocks, "lon")
        cot_group = gather_members(cot_lon, "dp").reshape(-1, cols_block)
        grad_attn = partner_rows_product(flat_grad, w_out, "dp")

        full_q, full_kv = arranged(panels, width)

        def project(rows, weights, unused):
            out = jnp.dot(rows, weights, preferred_element_type=jnp.float32)
            return out.astype(jnp.bfloat16)

        def back_project(grad_q, grad_kv):
            out = lax.dot_general(grad_q, full_q, TRANS_B, preferred_element_type=jnp.float32)
            out = out + lax.dot_general(grad_kv, full_kv, TRANS_B, preferred_element_type=jnp.float32)
            return out.astype(jnp.bfloat16)

        query = project(flat_inputs, full_q, None)
        kv_weights = (full_kv, None)

    tok_ext = halo_gather(inputs_here, radius)
    tok_ext = jnp.pad(tok_ext, ((0, 0), (0, pad_cols - ext_cols), (0, 0)))
    tok_ext = tok_ext.reshape(key_count, width)

    key_values = project(tok_ext, *kv_weights)

    wrapped = jnp.concatenate(
        [valid_cells[:, -radius:], valid_cells, valid_cells[:, :radius]], axis=1
    )
    framed = jnp.pad(wrapped, ((radius, radius), (0, 0)))
    valid_ext = lax.dynamic_slice(
        framed,
        (lax.axis_index("lat") * height, lon_index * breadth),
        (ext_rows, ext_cols),
    )
    valid_ext = jnp.pad(valid_ext, ((0, 0), (0, pad_cols - ext_cols))).reshape(1, key_count)
    query_pos = jnp.arange(token_count)
    key_pos = jnp.arange(key_count)
    delta_row = (key_pos // pad_cols)[None, :] - radius - (query_pos // breadth)[:, None]
    delta_col = (key_pos % pad_cols)[None, :] - radius - (query_pos % breadth)[:, None]
    inside = (jnp.abs(delta_row) <= radius) & (jnp.abs(delta_col) <= radius)
    itself = (delta_row == 0) & (delta_col == 0)
    allowed = inside & ((valid_ext == 1) | itself)
    bias = jnp.where(allowed, 0.0, -jnp.inf).astype(jnp.float32)

    attended, grad_query, grad_kv = block_attention(query, key_values, grad_attn, bias, HEADS)

    grad_kv_ext = grad_kv.reshape(ext_rows, pad_cols, 2 * width)[:, :ext_cols]
    (grad_kv_own,) = halo_return([grad_kv_ext], height, breadth, radius)

    if fast:
        own_att = columns(attended, dp_index, rows_half)
        att_from_dp = swap(columns(attended, 1 - dp_index, rows_half), "dp")
        att_dp = jnp.concatenate([own_att, att_from_dp], axis=0)
        att_group = jnp.concatenate([att_dp, swap(att_dp, "lon")], axis=0)
    else:
        att_blocks = attended.reshape(token_count, dp_count, rows_half).transpose(1, 0, 2)
        att_dp = exchange_blocks(att_blocks, "dp")
        att_group = gather_members(att_dp, "lon")
        att_group = att_group.transpose(1, 0, 2, 3).reshape(-1, rows_half)

    device_count = dp_count * lat_count * lon_count
    partial = lax.dot_general(
        att_group, cot_group, (((0,), (0,)), ((), ())), preferred_element_type=jnp.float32
    ) * (1.0 / device_count)
    spread = lax.all_to_all(partial.astype(jnp.bfloat16), "lat", 0, 0, tiled=True)
    d_w_out = spread.astype(jnp.float32).reshape(lat_count, rows_block, cols_block).sum(axis=0)

    grad_kv_low = grad_kv_own.astype(jnp.bfloat16).reshape(token_count, 2 * width)
    d_input = back_project(grad_query, grad_kv_low).reshape(1, height, breadth, width)
    return (d_input, d_w_out)


def solution(mesh):
    in_specs = (
        P("dp", "lat", "lon", None),
        P("dp", "lat", "lon", None),
        P(),
        P("dp", None),
        P("dp", None),
    )
    out_specs = (P("dp", "lat", "lon", None), P(("dp", "lat"), "lon"))
    return jax.shard_map(shards, mesh=mesh, in_specs=in_specs, out_specs=out_specs, check_vma=False)
```

```python
import functools

import jax
import jax.numpy as jnp
from jax import lax
from jax.experimental import pallas as pl
from jax.sharding import PartitionSpec as P

HEADS = 16
RADIUS = 6

TRANS_B = (((1,), (1,)), ((), ()))


def passed_along(value, axis, steps):
    count = lax.axis_size(axis)
    pairs = [(source, (source + steps) % count) for source in range(count)]
    return lax.ppermute(value, axis, pairs)


def shifted(value, axis, by):
    count = lax.axis_size(axis)
    pairs = [(i, i + by) for i in range(count) if 0 <= i + by < count]
    return lax.ppermute(value, axis, pairs)


def extended(block, sides, width, periodic):
    for axis, dim in sides:
        count = lax.axis_size(axis)
        forward = [(i, i + 1) for i in range(count - 1)]
        if periodic:
            forward.append((count - 1, 0))
        backward = [(target, source) for source, target in forward]
        low = lax.ppermute(
            lax.slice_in_dim(block, block.shape[dim] - width, None, axis=dim), axis, forward
        )
        high = lax.ppermute(lax.slice_in_dim(block, 0, width, axis=dim), axis, backward)
        block = jnp.concatenate([low, block, high], axis=dim)
    return block


def attention_kernel(q_ref, k_ref, v_ref, g_ref, bias_ref, att_ref, gq_ref, gkv_ref, *, head_dim, scale):
    q = q_ref[...]
    g = g_ref[...]
    lanes = q.shape[1]
    k = k_ref[...]
    v = v_ref[...]
    bias = bias_ref[...]
    lane = lax.broadcasted_iota(jnp.int32, (1, lanes), 1)
    q32 = q.astype(jnp.float32)
    g32 = g.astype(jnp.float32)
    att = jnp.zeros(q.shape, jnp.float32)
    gq = jnp.zeros(q.shape, jnp.float32)
    gk = jnp.zeros(k.shape, jnp.float32)
    gv = jnp.zeros(v.shape, jnp.float32)
    for j in range(lanes // head_dim):
        sel = (lane >= j * head_dim) & (lane < (j + 1) * head_dim)
        qj = jnp.where(sel, q32, 0.0).astype(jnp.bfloat16)
        gj = jnp.where(sel, g32, 0.0).astype(jnp.bfloat16)
        scores = lax.dot_general(qj, k, TRANS_B, preferred_element_type=jnp.float32) * scale
        masked = scores + bias
        peak = jnp.max(masked, axis=1, keepdims=True)
        weights = jnp.exp(masked - peak)
        probs = weights * (1.0 / jnp.sum(weights, axis=1, keepdims=True))
        probs_low = probs.astype(jnp.bfloat16)
        att_j = jnp.dot(probs_low, v, preferred_element_type=jnp.float32)
        grad_probs = lax.dot_general(gj, v, TRANS_B, preferred_element_type=jnp.float32)
        centre = jnp.sum(probs * grad_probs, axis=1, keepdims=True)
        grad_scores = (probs * (grad_probs - centre) * scale).astype(jnp.bfloat16)
        gq_j = jnp.dot(grad_scores, k, preferred_element_type=jnp.float32)
        scores_t = grad_scores.astype(jnp.float32).T.astype(jnp.bfloat16)
        probs_t = probs_low.astype(jnp.float32).T.astype(jnp.bfloat16)
        gk_j = jnp.dot(scores_t, q, preferred_element_type=jnp.float32)
        gv_j = jnp.dot(probs_t, g, preferred_element_type=jnp.float32)
        att = jnp.where(sel, att_j, att)
        gq = jnp.where(sel, gq_j, gq)
        gk = jnp.where(sel, gk_j, gk)
        gv = jnp.where(sel, gv_j, gv)
    att_ref[...] = att.astype(att_ref.dtype)
    gq_ref[...] = gq.astype(gq_ref.dtype)
    gkv_ref[:, :lanes] = gk
    gkv_ref[:, lanes:] = gv


def block_attention(query, projected, grad_attn, bias, heads):
    queries, width = query.shape
    keys = projected.shape[0]
    head_dim = width // heads
    lanes = 128
    pairs = width // lanes
    kernel = functools.partial(attention_kernel, head_dim=head_dim, scale=head_dim ** (-0.5))
    flops = 2 * queries * keys * width * 2 * 6
    cost = pl.CostEstimate(
        flops=flops,
        transcendentals=queries * keys * heads,
        bytes_accessed=2 * (2 * queries * width + 2 * keys * width + 2 * queries * width)
        + 4 * queries * keys + 4 * 2 * keys * width,
    )
    return pl.pallas_call(
        kernel,
        grid=(pairs,),
        in_specs=[
            pl.BlockSpec((queries, lanes), lambda h: (0, h)),
            pl.BlockSpec((keys, lanes), lambda h: (0, h + pairs)),
            pl.BlockSpec((keys, lanes), lambda h: (0, h + 2 * pairs)),
            pl.BlockSpec((queries, lanes), lambda h: (0, h)),
            pl.BlockSpec((queries, keys), lambda h: (0, 0)),
        ],
        out_specs=[
            pl.BlockSpec((queries, lanes), lambda h: (0, h)),
            pl.BlockSpec((queries, lanes), lambda h: (0, h)),
            pl.BlockSpec((keys, 2 * lanes), lambda h: (0, h)),
        ],
        out_shape=[
            jax.ShapeDtypeStruct((queries, width), jnp.bfloat16),
            jax.ShapeDtypeStruct((queries, width), jnp.bfloat16),
            jax.ShapeDtypeStruct((keys, 2 * width), jnp.float32),
        ],
        cost_estimate=cost,
        name="block_attention",
    )(query, projected, projected, grad_attn, bias)


def grid_pairs(delta_lat, delta_lon):
    lat_count = lax.axis_size("lat")
    lon_count = lax.axis_size("lon")
    pairs = []
    for la in range(lat_count):
        if 0 <= la + delta_lat < lat_count:
            for lo in range(lon_count):
                target = (la + delta_lat) * lon_count + (lo + delta_lon) % lon_count
                pairs.append((la * lon_count + lo, target))
    return pairs


def sent_to(value, delta_lat, delta_lon):
    return lax.ppermute(value, ("lat", "lon"), grid_pairs(delta_lat, delta_lon))


def part(count, radius, step, giving):
    if step == 0:
        return slice(0, count)
    if (step < 0) == giving:
        return slice(count - radius, count)
    return slice(0, radius)


def grouped_send(pieces):
    lon_count = lax.axis_size("lon")
    groups = {}
    for index, (dl, db, value) in enumerate(pieces):
        groups.setdefault((dl, db % lon_count), []).append(index)
    out = [None] * len(pieces)
    for (dl, db), members in groups.items():
        values = [pieces[i][2] for i in members]
        got = sent_to(jnp.concatenate(values, axis=1), dl, db)
        offset = 0
        for i, value in zip(members, values):
            out[i] = got[:, offset : offset + value.shape[1]]
            offset += value.shape[1]
    return out


def halo_gather(block, radius):
    height, breadth, lanes = block.shape
    spots = []
    pieces = []
    for da in (-1, 0, 1):
        for db in (-1, 0, 1):
            if da == 0 and db == 0:
                continue
            piece = block[part(height, radius, da, True), part(breadth, radius, db, True)]
            spots.append((da, db))
            pieces.append((-da, -db, piece))
    got = dict(zip(spots, grouped_send(pieces)))
    got[(0, 0)] = block
    rows = [jnp.concatenate([got[(da, db)] for db in (-1, 0, 1)], axis=1) for da in (-1, 0, 1)]
    return jnp.concatenate(rows, axis=0)


def halo_return(ext_list, height, breadth, radius):
    row_slices = {-1: slice(0, radius), 0: slice(radius, radius + height), 1: slice(radius + height, None)}
    col_slices = {-1: slice(0, radius), 0: slice(radius, radius + breadth), 1: slice(radius + breadth, None)}
    owns = [ext[row_slices[0], col_slices[0]] for ext in ext_list]
    widths = [ext.shape[-1] for ext in ext_list]
    spots = []
    pieces = []
    for da in (-1, 0, 1):
        for db in (-1, 0, 1):
            if da == 0 and db == 0:
                continue
            joined = jnp.concatenate(
                [ext[row_slices[da], col_slices[db]] for ext in ext_list], axis=-1
            ).astype(jnp.bfloat16)
            spots.append((da, db))
            pieces.append((da, db, joined))
    for (da, db), got in zip(spots, grouped_send(pieces)):
        rs = part(height, radius, da, True)
        cs = part(breadth, radius, db, True)
        pad_rows = (rs.start, height - rs.stop)
        pad_cols = (cs.start, breadth - cs.stop)
        offset = 0
        for index, width in enumerate(widths):
            piece = got[..., offset : offset + width].astype(jnp.float32)
            offset += width
            owns[index] = owns[index] + jnp.pad(piece, (pad_rows, pad_cols, (0, 0)))
    return owns


def partner_rows_product(lhs, weights, axis):
    count = lax.axis_size(axis)
    if count != 2:
        full = lax.all_gather(weights, axis, axis=0, tiled=True)
        return lax.dot_general(lhs, full, TRANS_B, preferred_element_type=jnp.float32).astype(
            jnp.bfloat16
        )
    other = lax.ppermute(weights, axis, [(0, 1), (1, 0)])
    mine_part = lax.dot_general(lhs, weights, TRANS_B, preferred_element_type=jnp.float32)
    other_part = lax.dot_general(lhs, other, TRANS_B, preferred_element_type=jnp.float32)
    mine_part = mine_part.astype(jnp.bfloat16)
    other_part = other_part.astype(jnp.bfloat16)
    first = lax.axis_index(axis) == 0
    return jnp.where(
        first,
        jnp.concatenate([mine_part, other_part], axis=1),
        jnp.concatenate([other_part, mine_part], axis=1),
    )


def exchange_blocks(blocks, axis):
    count = lax.axis_size(axis)
    if count == 2:
        me = lax.axis_index(axis)
        mine = lax.dynamic_index_in_dim(blocks, me, 0, keepdims=False)
        theirs = lax.dynamic_index_in_dim(blocks, 1 - me, 0, keepdims=False)
        got = lax.ppermute(theirs, axis, [(0, 1), (1, 0)])
        return jnp.where(me == 0, jnp.stack([mine, got]), jnp.stack([got, mine]))
    flat = blocks.reshape((-1,) + blocks.shape[2:])
    out = lax.all_to_all(flat, axis, 0, 0, tiled=True)
    return out.reshape(blocks.shape)


def gather_members(value, axis):
    count = lax.axis_size(axis)
    if count == 2:
        me = lax.axis_index(axis)
        got = lax.ppermute(value, axis, [(0, 1), (1, 0)])
        return jnp.where(me == 0, jnp.stack([value, got]), jnp.stack([got, value]))
    return lax.all_gather(value, axis, axis=0, tiled=False)


def swap(value, axis):
    return lax.ppermute(value, axis, [(0, 1), (1, 0)])


def columns(value, index, size):
    return lax.dynamic_slice_in_dim(value, index * size, size, axis=1)


def split_rows(joined, shapes):
    out = []
    offset = 0
    for shape in shapes:
        count = 1
        for extent in shape[:-1]:
            count *= extent
        count = count * shape[-1] // joined.shape[-1]
        out.append(joined[offset : offset + count].reshape(shape))
        offset += count
    return out


def join_rows(parts, lanes):
    return jnp.concatenate([p.reshape(-1, lanes) for p in parts], axis=0)


def lat_return(ext_list, height, radius):
    owns = []
    tops = join_rows([ext[:radius] for ext in ext_list], ext_list[0].shape[-1])
    bottoms = join_rows([ext[radius + height :] for ext in ext_list], ext_list[0].shape[-1])
    shapes = [ext[:radius].shape for ext in ext_list]
    from_below = split_rows(shifted(tops.astype(jnp.bfloat16), "lat", -1), shapes)
    from_above = split_rows(shifted(bottoms.astype(jnp.bfloat16), "lat", 1), shapes)
    for ext, below, above in zip(ext_list, from_below, from_above):
        middle = (
            ext[radius : radius + height]
            + jnp.pad(below.astype(jnp.float32), ((height - radius, 0), (0, 0), (0, 0)))
            + jnp.pad(above.astype(jnp.float32), ((0, height - radius), (0, 0), (0, 0)))
        )
        owns.append(middle)
    return owns


def add_lon_rims(mid_list, from_right, from_left, breadth, radius):
    owns = []
    for mid, right, left in zip(mid_list, from_right, from_left):
        owns.append(
            mid[:, radius : radius + breadth]
            + jnp.pad(right.astype(jnp.float32), ((0, 0), (breadth - radius, 0), (0, 0)))
            + jnp.pad(left.astype(jnp.float32), ((0, 0), (0, breadth - radius), (0, 0)))
        )
    return owns


def shards(tokens, cotangent, valid_cells, w_qkv, w_out):
    inputs_here = tokens[0]
    grad_here = cotangent[0]
    height, breadth, width = inputs_here.shape
    radius = RADIUS
    ext_rows = height + 2 * radius
    ext_cols = breadth + 2 * radius
    pad_cols = -(-ext_cols // 8) * 8
    token_count = height * breadth
    key_count = ext_rows * pad_cols
    flat_inputs = inputs_here.reshape(token_count, width)
    flat_grad = grad_here.reshape(token_count, width)
    dp_count = lax.axis_size("dp")
    lat_count = lax.axis_size("lat")
    lon_count = lax.axis_size("lon")
    rows_half = width // dp_count
    cols_block = width // lon_count
    rows_block = rows_half // lat_count
    dp_index = lax.axis_index("dp")
    lon_index = lax.axis_index("lon")
    fast = dp_count == 2 and lon_count == 2

    if fast:
        qkv_other = swap(w_qkv, "dp")
        dp_got = swap(jnp.concatenate([w_out, flat_grad], axis=0), "dp")
        w_out_other = dp_got[: w_out.shape[0]]
        cot_dp = dp_got[w_out.shape[0] :]
        cot_send = jnp.concatenate(
            [columns(flat_grad, 1 - lon_index, cols_block), columns(cot_dp, 1 - lon_index, cols_block)],
            axis=0,
        )
        cot_lon = swap(cot_send, "lon")
        cot_group = jnp.concatenate(
            [
                columns(flat_grad, lon_index, cols_block),
                columns(cot_dp, lon_index, cols_block),
                cot_lon,
            ],
            axis=0,
        )
        mine_part = lax.dot_general(flat_grad, w_out, TRANS_B, preferred_element_type=jnp.float32)
        other_part = lax.dot_general(
            flat_grad, w_out_other, TRANS_B, preferred_element_type=jnp.float32
        )
        mine_part = mine_part.astype(jnp.bfloat16)
        other_part = other_part.astype(jnp.bfloat16)
        grad_attn = jnp.where(
            dp_index == 0,
            jnp.concatenate([mine_part, other_part], axis=1),
            jnp.concatenate([other_part, mine_part], axis=1),
        )

        def project(rows):
            own = jnp.dot(
                columns(rows, dp_index, rows_half), w_qkv, preferred_element_type=jnp.float32
            )
            other = jnp.dot(
                columns(rows, 1 - dp_index, rows_half), qkv_other, preferred_element_type=jnp.float32
            )
            return (own + other).astype(jnp.bfloat16)

        def back_project(grad_proj):
            own = lax.dot_general(grad_proj, w_qkv, TRANS_B, preferred_element_type=jnp.float32)
            other = lax.dot_general(grad_proj, qkv_other, TRANS_B, preferred_element_type=jnp.float32)
            own = own.astype(jnp.bfloat16)
            other = other.astype(jnp.bfloat16)
            return jnp.where(
                dp_index == 0,
                jnp.concatenate([own, other], axis=1),
                jnp.concatenate([other, own], axis=1),
            )
    else:
        panels = lax.all_gather(w_qkv, "dp", axis=0, tiled=True)
        cot_blocks = flat_grad.reshape(token_count, lon_count, cols_block).transpose(1, 0, 2)
        cot_lon = exchange_blocks(cot_blocks, "lon")
        cot_group = gather_members(cot_lon, "dp").reshape(-1, cols_block)
        grad_attn = partner_rows_product(flat_grad, w_out, "dp")


        def project(rows):
            out = jnp.dot(rows, panels, preferred_element_type=jnp.float32)
            return out.astype(jnp.bfloat16)

        def back_project(grad_proj):
            out = lax.dot_general(grad_proj, panels, TRANS_B, preferred_element_type=jnp.float32)
            return out.astype(jnp.bfloat16)

    tok_ext = halo_gather(inputs_here, radius)
    tok_ext = jnp.pad(tok_ext, ((0, 0), (0, pad_cols - ext_cols), (0, 0)))
    tok_ext = tok_ext.reshape(key_count, width)

    projected = project(tok_ext)
    query = projected.reshape(ext_rows, pad_cols, 3 * width)[
        radius : radius + height, radius : radius + breadth, :width
    ].reshape(token_count, width)

    wrapped = jnp.concatenate(
        [valid_cells[:, -radius:], valid_cells, valid_cells[:, :radius]], axis=1
    )
    framed = jnp.pad(wrapped, ((radius, radius), (0, 0)))
    valid_ext = lax.dynamic_slice(
        framed,
        (lax.axis_index("lat") * height, lon_index * breadth),
        (ext_rows, ext_cols),
    )
    valid_ext = jnp.pad(valid_ext, ((0, 0), (0, pad_cols - ext_cols))).reshape(1, key_count)
    query_pos = jnp.arange(token_count)
    key_pos = jnp.arange(key_count)
    delta_row = (key_pos // pad_cols)[None, :] - radius - (query_pos // breadth)[:, None]
    delta_col = (key_pos % pad_cols)[None, :] - radius - (query_pos % breadth)[:, None]
    inside = (jnp.abs(delta_row) <= radius) & (jnp.abs(delta_col) <= radius)
    itself = (delta_row == 0) & (delta_col == 0)
    allowed = inside & ((valid_ext == 1) | itself)
    bias = jnp.where(allowed, 0.0, -jnp.inf).astype(jnp.float32)

    attended, grad_query, grad_kv = block_attention(query, projected, grad_attn, bias, HEADS)

    grad_kv_ext = grad_kv.reshape(ext_rows, pad_cols, 2 * width)[:, :ext_cols]
    (grad_kv_own,) = halo_return([grad_kv_ext], height, breadth, radius)

    if fast:
        own_att = columns(attended, dp_index, rows_half)
        att_from_dp = swap(columns(attended, 1 - dp_index, rows_half), "dp")
        att_dp = jnp.concatenate([own_att, att_from_dp], axis=0)
        att_group = jnp.concatenate([att_dp, swap(att_dp, "lon")], axis=0)
    else:
        att_blocks = attended.reshape(token_count, dp_count, rows_half).transpose(1, 0, 2)
        att_dp = exchange_blocks(att_blocks, "dp")
        att_group = gather_members(att_dp, "lon")
        att_group = att_group.transpose(1, 0, 2, 3).reshape(-1, rows_half)

    device_count = dp_count * lat_count * lon_count
    partial = lax.dot_general(
        att_group, cot_group, (((0,), (0,)), ((), ())), preferred_element_type=jnp.float32
    ) * (1.0 / device_count)
    spread = lax.all_to_all(partial.astype(jnp.bfloat16), "lat", 0, 0, tiled=True)
    d_w_out = spread.astype(jnp.float32).reshape(lat_count, rows_block, cols_block).sum(axis=0)

    pairs = width // 128
    grad_kv_low = (
        grad_kv_own.astype(jnp.bfloat16)
        .reshape(token_count, pairs, 2, 128)
        .transpose(0, 2, 1, 3)
        .reshape(token_count, 2 * width)
    )
    grad_proj = jnp.concatenate([grad_query, grad_kv_low], axis=1)
    d_input = back_project(grad_proj).reshape(1, height, breadth, width)
    return (d_input, d_w_out)


def solution(mesh):
    in_specs = (
        P("dp", "lat", "lon", None),
        P("dp", "lat", "lon", None),
        P(),
        P("dp", None),
        P("dp", None),
    )
    out_specs = (P("dp", "lat", "lon", None), P(("dp", "lat"), "lon"))
    return jax.shard_map(shards, mesh=mesh, in_specs=in_specs, out_specs=out_specs, check_vma=False)
```

```python
import functools

import jax
import jax.numpy as jnp
from jax import lax
from jax.experimental import pallas as pl
from jax.sharding import PartitionSpec as P

HEADS = 16
RADIUS = 6

TRANS_B = (((1,), (1,)), ((), ()))


def passed_along(value, axis, steps):
    count = lax.axis_size(axis)
    pairs = [(source, (source + steps) % count) for source in range(count)]
    return lax.ppermute(value, axis, pairs)


def shifted(value, axis, by):
    count = lax.axis_size(axis)
    pairs = [(i, i + by) for i in range(count) if 0 <= i + by < count]
    return lax.ppermute(value, axis, pairs)


def extended(block, sides, width, periodic):
    for axis, dim in sides:
        count = lax.axis_size(axis)
        forward = [(i, i + 1) for i in range(count - 1)]
        if periodic:
            forward.append((count - 1, 0))
        backward = [(target, source) for source, target in forward]
        low = lax.ppermute(
            lax.slice_in_dim(block, block.shape[dim] - width, None, axis=dim), axis, forward
        )
        high = lax.ppermute(lax.slice_in_dim(block, 0, width, axis=dim), axis, backward)
        block = jnp.concatenate([low, block, high], axis=dim)
    return block


def attention_kernel(q_ref, k_ref, v_ref, g_ref, bias_ref, att_ref, gq_ref, gkv_ref, *, head_dim, scale):
    q = q_ref[...]
    g = g_ref[...]
    lanes = q.shape[1]
    k = k_ref[...]
    v = v_ref[...]
    bias = bias_ref[...]
    lane = lax.broadcasted_iota(jnp.int32, (1, lanes), 1)
    q32 = q.astype(jnp.float32)
    g32 = g.astype(jnp.float32)
    att = jnp.zeros(q.shape, jnp.float32)
    gq = jnp.zeros(q.shape, jnp.float32)
    gk = jnp.zeros(k.shape, jnp.float32)
    gv = jnp.zeros(v.shape, jnp.float32)
    for j in range(lanes // head_dim):
        sel = (lane >= j * head_dim) & (lane < (j + 1) * head_dim)
        qj = jnp.where(sel, q32, 0.0).astype(jnp.bfloat16)
        gj = jnp.where(sel, g32, 0.0).astype(jnp.bfloat16)
        scores = lax.dot_general(qj, k, TRANS_B, preferred_element_type=jnp.float32) * scale
        masked = scores + bias
        peak = jnp.max(masked, axis=1, keepdims=True)
        weights = jnp.exp(masked - peak)
        probs = weights * (1.0 / jnp.sum(weights, axis=1, keepdims=True))
        probs_low = probs.astype(jnp.bfloat16)
        att_j = jnp.dot(probs_low, v, preferred_element_type=jnp.float32)
        grad_probs = lax.dot_general(gj, v, TRANS_B, preferred_element_type=jnp.float32)
        centre = jnp.sum(probs * grad_probs, axis=1, keepdims=True)
        grad_scores = (probs * (grad_probs - centre) * scale).astype(jnp.bfloat16)
        gq_j = jnp.dot(grad_scores, k, preferred_element_type=jnp.float32)
        scores_t = grad_scores.astype(jnp.float32).T.astype(jnp.bfloat16)
        probs_t = probs_low.astype(jnp.float32).T.astype(jnp.bfloat16)
        gk_j = jnp.dot(scores_t, q, preferred_element_type=jnp.float32)
        gv_j = jnp.dot(probs_t, g, preferred_element_type=jnp.float32)
        att = jnp.where(sel, att_j, att)
        gq = jnp.where(sel, gq_j, gq)
        gk = jnp.where(sel, gk_j, gk)
        gv = jnp.where(sel, gv_j, gv)
    att_ref[...] = att.astype(att_ref.dtype)
    gq_ref[...] = gq.astype(gq_ref.dtype)
    gkv_ref[:, :lanes] = gk
    gkv_ref[:, lanes:] = gv


def block_attention(query, projected, grad_attn, bias, heads):
    queries, width = query.shape
    keys = projected.shape[0]
    head_dim = width // heads
    lanes = 128
    pairs = width // lanes
    kernel = functools.partial(attention_kernel, head_dim=head_dim, scale=head_dim ** (-0.5))
    flops = 2 * queries * keys * width * 2 * 6
    cost = pl.CostEstimate(
        flops=flops,
        transcendentals=queries * keys * heads,
        bytes_accessed=2 * (2 * queries * width + 2 * keys * width + 2 * queries * width)
        + 4 * queries * keys + 4 * 2 * keys * width,
    )
    return pl.pallas_call(
        kernel,
        grid=(pairs,),
        in_specs=[
            pl.BlockSpec((queries, lanes), lambda h: (0, h)),
            pl.BlockSpec((keys, lanes), lambda h: (0, h + pairs)),
            pl.BlockSpec((keys, lanes), lambda h: (0, h + 2 * pairs)),
            pl.BlockSpec((queries, lanes), lambda h: (0, h)),
            pl.BlockSpec((queries, keys), lambda h: (0, 0)),
        ],
        out_specs=[
            pl.BlockSpec((queries, lanes), lambda h: (0, h)),
            pl.BlockSpec((queries, lanes), lambda h: (0, h)),
            pl.BlockSpec((keys, 2 * lanes), lambda h: (0, h)),
        ],
        out_shape=[
            jax.ShapeDtypeStruct((queries, width), jnp.bfloat16),
            jax.ShapeDtypeStruct((queries, width), jnp.bfloat16),
            jax.ShapeDtypeStruct((keys, 2 * width), jnp.float32),
        ],
        cost_estimate=cost,
        name="block_attention",
    )(query, projected, projected, grad_attn, bias)


def grid_pairs(delta_lat, delta_lon):
    lat_count = lax.axis_size("lat")
    lon_count = lax.axis_size("lon")
    pairs = []
    for la in range(lat_count):
        if 0 <= la + delta_lat < lat_count:
            for lo in range(lon_count):
                target = (la + delta_lat) * lon_count + (lo + delta_lon) % lon_count
                pairs.append((la * lon_count + lo, target))
    return pairs


def sent_to(value, delta_lat, delta_lon):
    return lax.ppermute(value, ("lat", "lon"), grid_pairs(delta_lat, delta_lon))


def part(count, radius, step, giving):
    if step == 0:
        return slice(0, count)
    if (step < 0) == giving:
        return slice(count - radius, count)
    return slice(0, radius)


def grouped_send(pieces):
    lon_count = lax.axis_size("lon")
    groups = {}
    for index, (dl, db, value) in enumerate(pieces):
        groups.setdefault((dl, db % lon_count), []).append(index)
    out = [None] * len(pieces)
    for (dl, db), members in groups.items():
        values = [pieces[i][2] for i in members]
        got = sent_to(jnp.concatenate(values, axis=1), dl, db)
        offset = 0
        for i, value in zip(members, values):
            out[i] = got[:, offset : offset + value.shape[1]]
            offset += value.shape[1]
    return out


def halo_gather(block, radius):
    height, breadth, lanes = block.shape
    spots = []
    pieces = []
    for da in (-1, 0, 1):
        for db in (-1, 0, 1):
            if da == 0 and db == 0:
                continue
            piece = block[part(height, radius, da, True), part(breadth, radius, db, True)]
            spots.append((da, db))
            pieces.append((-da, -db, piece))
    got = dict(zip(spots, grouped_send(pieces)))
    got[(0, 0)] = block
    rows = [jnp.concatenate([got[(da, db)] for db in (-1, 0, 1)], axis=1) for da in (-1, 0, 1)]
    return jnp.concatenate(rows, axis=0)


def halo_return(ext_list, height, breadth, radius):
    row_slices = {-1: slice(0, radius), 0: slice(radius, radius + height), 1: slice(radius + height, None)}
    col_slices = {-1: slice(0, radius), 0: slice(radius, radius + breadth), 1: slice(radius + breadth, None)}
    owns = [ext[row_slices[0], col_slices[0]] for ext in ext_list]
    widths = [ext.shape[-1] for ext in ext_list]
    spots = []
    pieces = []
    for da in (-1, 0, 1):
        for db in (-1, 0, 1):
            if da == 0 and db == 0:
                continue
            joined = jnp.concatenate(
                [ext[row_slices[da], col_slices[db]] for ext in ext_list], axis=-1
            ).astype(jnp.bfloat16)
            spots.append((da, db))
            pieces.append((da, db, joined))
    for (da, db), got in zip(spots, grouped_send(pieces)):
        rs = part(height, radius, da, True)
        cs = part(breadth, radius, db, True)
        pad_rows = (rs.start, height - rs.stop)
        pad_cols = (cs.start, breadth - cs.stop)
        offset = 0
        for index, width in enumerate(widths):
            piece = got[..., offset : offset + width].astype(jnp.float32)
            offset += width
            owns[index] = owns[index] + jnp.pad(piece, (pad_rows, pad_cols, (0, 0)))
    return owns


def partner_rows_product(lhs, weights, axis):
    count = lax.axis_size(axis)
    if count != 2:
        full = lax.all_gather(weights, axis, axis=0, tiled=True)
        return lax.dot_general(lhs, full, TRANS_B, preferred_element_type=jnp.float32).astype(
            jnp.bfloat16
        )
    other = lax.ppermute(weights, axis, [(0, 1), (1, 0)])
    mine_part = lax.dot_general(lhs, weights, TRANS_B, preferred_element_type=jnp.float32)
    other_part = lax.dot_general(lhs, other, TRANS_B, preferred_element_type=jnp.float32)
    mine_part = mine_part.astype(jnp.bfloat16)
    other_part = other_part.astype(jnp.bfloat16)
    first = lax.axis_index(axis) == 0
    return jnp.where(
        first,
        jnp.concatenate([mine_part, other_part], axis=1),
        jnp.concatenate([other_part, mine_part], axis=1),
    )


def exchange_blocks(blocks, axis):
    count = lax.axis_size(axis)
    if count == 2:
        me = lax.axis_index(axis)
        mine = lax.dynamic_index_in_dim(blocks, me, 0, keepdims=False)
        theirs = lax.dynamic_index_in_dim(blocks, 1 - me, 0, keepdims=False)
        got = lax.ppermute(theirs, axis, [(0, 1), (1, 0)])
        return jnp.where(me == 0, jnp.stack([mine, got]), jnp.stack([got, mine]))
    flat = blocks.reshape((-1,) + blocks.shape[2:])
    out = lax.all_to_all(flat, axis, 0, 0, tiled=True)
    return out.reshape(blocks.shape)


def gather_members(value, axis):
    count = lax.axis_size(axis)
    if count == 2:
        me = lax.axis_index(axis)
        got = lax.ppermute(value, axis, [(0, 1), (1, 0)])
        return jnp.where(me == 0, jnp.stack([value, got]), jnp.stack([got, value]))
    return lax.all_gather(value, axis, axis=0, tiled=False)


def swap(value, axis):
    return lax.ppermute(value, axis, [(0, 1), (1, 0)])


def columns(value, index, size):
    return lax.dynamic_slice_in_dim(value, index * size, size, axis=1)


def split_rows(joined, shapes):
    out = []
    offset = 0
    for shape in shapes:
        count = 1
        for extent in shape[:-1]:
            count *= extent
        count = count * shape[-1] // joined.shape[-1]
        out.append(joined[offset : offset + count].reshape(shape))
        offset += count
    return out


def join_rows(parts, lanes):
    return jnp.concatenate([p.reshape(-1, lanes) for p in parts], axis=0)


def lat_return(ext_list, height, radius):
    owns = []
    tops = join_rows([ext[:radius] for ext in ext_list], ext_list[0].shape[-1])
    bottoms = join_rows([ext[radius + height :] for ext in ext_list], ext_list[0].shape[-1])
    shapes = [ext[:radius].shape for ext in ext_list]
    from_below = split_rows(shifted(tops.astype(jnp.bfloat16), "lat", -1), shapes)
    from_above = split_rows(shifted(bottoms.astype(jnp.bfloat16), "lat", 1), shapes)
    for ext, below, above in zip(ext_list, from_below, from_above):
        middle = (
            ext[radius : radius + height]
            + jnp.pad(below.astype(jnp.float32), ((height - radius, 0), (0, 0), (0, 0)))
            + jnp.pad(above.astype(jnp.float32), ((0, height - radius), (0, 0), (0, 0)))
        )
        owns.append(middle)
    return owns


def add_lon_rims(mid_list, from_right, from_left, breadth, radius):
    owns = []
    for mid, right, left in zip(mid_list, from_right, from_left):
        owns.append(
            mid[:, radius : radius + breadth]
            + jnp.pad(right.astype(jnp.float32), ((0, 0), (breadth - radius, 0), (0, 0)))
            + jnp.pad(left.astype(jnp.float32), ((0, 0), (0, breadth - radius), (0, 0)))
        )
    return owns


def shards(tokens, cotangent, valid_cells, w_qkv, w_out):
    inputs_here = tokens[0]
    grad_here = cotangent[0]
    height, breadth, width = inputs_here.shape
    radius = RADIUS
    ext_rows = height + 2 * radius
    ext_cols = breadth + 2 * radius
    pad_cols = -(-ext_cols // 8) * 8
    token_count = height * breadth
    key_count = ext_rows * pad_cols
    flat_inputs = inputs_here.reshape(token_count, width)
    flat_grad = grad_here.reshape(token_count, width)
    dp_count = lax.axis_size("dp")
    lat_count = lax.axis_size("lat")
    lon_count = lax.axis_size("lon")
    rows_half = width // dp_count
    cols_block = width // lon_count
    rows_block = rows_half // lat_count
    dp_index = lax.axis_index("dp")
    lon_index = lax.axis_index("lon")
    fast = dp_count == 2 and lon_count == 2

    if fast:
        panels = lax.all_gather(w_qkv, "dp", axis=0, tiled=True)
        dp_got = swap(jnp.concatenate([w_out, flat_grad], axis=0), "dp")
        w_out_other = dp_got[: w_out.shape[0]]
        cot_dp = dp_got[w_out.shape[0] :]
        cot_send = jnp.concatenate(
            [columns(flat_grad, 1 - lon_index, cols_block), columns(cot_dp, 1 - lon_index, cols_block)],
            axis=0,
        )
        cot_lon = swap(cot_send, "lon")
        cot_group = jnp.concatenate(
            [
                columns(flat_grad, lon_index, cols_block),
                columns(cot_dp, lon_index, cols_block),
                cot_lon,
            ],
            axis=0,
        )
        mine_part = lax.dot_general(flat_grad, w_out, TRANS_B, preferred_element_type=jnp.float32)
        other_part = lax.dot_general(
            flat_grad, w_out_other, TRANS_B, preferred_element_type=jnp.float32
        )
        mine_part = mine_part.astype(jnp.bfloat16)
        other_part = other_part.astype(jnp.bfloat16)
        grad_attn = jnp.where(
            dp_index == 0,
            jnp.concatenate([mine_part, other_part], axis=1),
            jnp.concatenate([other_part, mine_part], axis=1),
        )

        def project(rows):
            out = jnp.dot(rows, panels, preferred_element_type=jnp.float32)
            return out.astype(jnp.bfloat16)

        def back_project(grad_proj):
            out = lax.dot_general(grad_proj, panels, TRANS_B, preferred_element_type=jnp.float32)
            return out.astype(jnp.bfloat16)
    else:
        panels = lax.all_gather(w_qkv, "dp", axis=0, tiled=True)
        cot_blocks = flat_grad.reshape(token_count, lon_count, cols_block).transpose(1, 0, 2)
        cot_lon = exchange_blocks(cot_blocks, "lon")
        cot_group = gather_members(cot_lon, "dp").reshape(-1, cols_block)
        grad_attn = partner_rows_product(flat_grad, w_out, "dp")


        def project(rows):
            out = jnp.dot(rows, panels, preferred_element_type=jnp.float32)
            return out.astype(jnp.bfloat16)

        def back_project(grad_proj):
            out = lax.dot_general(grad_proj, panels, TRANS_B, preferred_element_type=jnp.float32)
            return out.astype(jnp.bfloat16)

    tok_ext = halo_gather(inputs_here, radius)
    tok_ext = jnp.pad(tok_ext, ((0, 0), (0, pad_cols - ext_cols), (0, 0)))
    tok_ext = tok_ext.reshape(key_count, width)

    projected = project(tok_ext)
    query = projected.reshape(ext_rows, pad_cols, 3 * width)[
        radius : radius + height, radius : radius + breadth, :width
    ].reshape(token_count, width)

    wrapped = jnp.concatenate(
        [valid_cells[:, -radius:], valid_cells, valid_cells[:, :radius]], axis=1
    )
    framed = jnp.pad(wrapped, ((radius, radius), (0, 0)))
    valid_ext = lax.dynamic_slice(
        framed,
        (lax.axis_index("lat") * height, lon_index * breadth),
        (ext_rows, ext_cols),
    )
    valid_ext = jnp.pad(valid_ext, ((0, 0), (0, pad_cols - ext_cols))).reshape(1, key_count)
    query_pos = jnp.arange(token_count)
    key_pos = jnp.arange(key_count)
    delta_row = (key_pos // pad_cols)[None, :] - radius - (query_pos // breadth)[:, None]
    delta_col = (key_pos % pad_cols)[None, :] - radius - (query_pos % breadth)[:, None]
    inside = (jnp.abs(delta_row) <= radius) & (jnp.abs(delta_col) <= radius)
    itself = (delta_row == 0) & (delta_col == 0)
    allowed = inside & ((valid_ext == 1) | itself)
    bias = jnp.where(allowed, 0.0, -jnp.inf).astype(jnp.float32)

    attended, grad_query, grad_kv = block_attention(query, projected, grad_attn, bias, HEADS)

    grad_kv_ext = grad_kv.reshape(ext_rows, pad_cols, 2 * width)[:, :ext_cols]
    (grad_kv_own,) = halo_return([grad_kv_ext], height, breadth, radius)

    if fast:
        own_att = columns(attended, dp_index, rows_half)
        att_from_dp = swap(columns(attended, 1 - dp_index, rows_half), "dp")
        att_dp = jnp.concatenate([own_att, att_from_dp], axis=0)
        att_group = jnp.concatenate([att_dp, swap(att_dp, "lon")], axis=0)
    else:
        att_blocks = attended.reshape(token_count, dp_count, rows_half).transpose(1, 0, 2)
        att_dp = exchange_blocks(att_blocks, "dp")
        att_group = gather_members(att_dp, "lon")
        att_group = att_group.transpose(1, 0, 2, 3).reshape(-1, rows_half)

    device_count = dp_count * lat_count * lon_count
    partial = lax.dot_general(
        att_group, cot_group, (((0,), (0,)), ((), ())), preferred_element_type=jnp.float32
    ) * (1.0 / device_count)
    d_w_out = lax.psum_scatter(partial, "lat", scatter_dimension=0, tiled=True)

    pairs = width // 128
    grad_kv_low = (
        grad_kv_own.astype(jnp.bfloat16)
        .reshape(token_count, pairs, 2, 128)
        .transpose(0, 2, 1, 3)
        .reshape(token_count, 2 * width)
    )
    grad_proj = jnp.concatenate([grad_query, grad_kv_low], axis=1)
    d_input = back_project(grad_proj).reshape(1, height, breadth, width)
    return (d_input, d_w_out)


def solution(mesh):
    in_specs = (
        P("dp", "lat", "lon", None),
        P("dp", "lat", "lon", None),
        P(),
        P("dp", None),
        P("dp", None),
    )
    out_specs = (P("dp", "lat", "lon", None), P(("dp", "lat"), "lon"))
    return jax.shard_map(shards, mesh=mesh, in_specs=in_specs, out_specs=out_specs, check_vma=False)
```

```python
import functools

import jax
import jax.numpy as jnp
from jax import lax
from jax.experimental import pallas as pl
from jax.sharding import PartitionSpec as P

HEADS = 16
RADIUS = 6

TRANS_B = (((1,), (1,)), ((), ()))


def passed_along(value, axis, steps):
    count = lax.axis_size(axis)
    pairs = [(source, (source + steps) % count) for source in range(count)]
    return lax.ppermute(value, axis, pairs)


def shifted(value, axis, by):
    count = lax.axis_size(axis)
    pairs = [(i, i + by) for i in range(count) if 0 <= i + by < count]
    return lax.ppermute(value, axis, pairs)


def extended(block, sides, width, periodic):
    for axis, dim in sides:
        count = lax.axis_size(axis)
        forward = [(i, i + 1) for i in range(count - 1)]
        if periodic:
            forward.append((count - 1, 0))
        backward = [(target, source) for source, target in forward]
        low = lax.ppermute(
            lax.slice_in_dim(block, block.shape[dim] - width, None, axis=dim), axis, forward
        )
        high = lax.ppermute(lax.slice_in_dim(block, 0, width, axis=dim), axis, backward)
        block = jnp.concatenate([low, block, high], axis=dim)
    return block


def attention_kernel(q_ref, k_ref, v_ref, g_ref, bias_ref, att_ref, gq_ref, gkv_ref, *, head_dim, scale):
    q = q_ref[...]
    g = g_ref[...]
    k = k_ref[...]
    v = v_ref[...]
    bias = bias_ref[...]
    lanes = q.shape[1]
    lane = lax.broadcasted_iota(jnp.int32, (1, lanes), 1)
    zero = jnp.zeros((), q.dtype)
    sels = [(lane >= j * head_dim) & (lane < (j + 1) * head_dim) for j in range(lanes // head_dim)]
    q_scaled = (q.astype(jnp.float32) * scale).astype(q.dtype)
    g_scaled = (g.astype(jnp.float32) * scale).astype(g.dtype)
    probs_list = []
    grads_list = []
    for sel in sels:
        qj = jnp.where(sel, q_scaled, zero)
        gj = jnp.where(sel, g_scaled, zero)
        masked = lax.dot_general(qj, k, TRANS_B, preferred_element_type=jnp.float32) + bias
        peak = jnp.max(masked, axis=1, keepdims=True)
        weights = jnp.exp(masked - peak)
        probs = weights * (1.0 / jnp.sum(weights, axis=1, keepdims=True))
        grad_probs = lax.dot_general(gj, v, TRANS_B, preferred_element_type=jnp.float32)
        centre = jnp.sum(probs * grad_probs, axis=1, keepdims=True)
        grads_list.append((probs * (grad_probs - centre)).astype(jnp.bfloat16))
        probs_list.append(probs.astype(jnp.bfloat16))
    k_sel = jnp.concatenate([jnp.where(sel, k, zero) for sel in sels], axis=0)
    v_sel = jnp.concatenate([jnp.where(sel, v, zero) for sel in sels], axis=0)
    q_sel = jnp.concatenate([jnp.where(sel, q, zero) for sel in sels], axis=0)
    g_sel = jnp.concatenate([jnp.where(sel, g, zero) for sel in sels], axis=0)
    probs_cat = jnp.concatenate(probs_list, axis=1)
    grads_cat = jnp.concatenate(grads_list, axis=1)
    att = jnp.dot(probs_cat, v_sel, preferred_element_type=jnp.float32)
    gq = jnp.dot(grads_cat, k_sel, preferred_element_type=jnp.float32)
    grads_t = jnp.concatenate(
        [x.astype(jnp.float32).T.astype(jnp.bfloat16) for x in grads_list], axis=1
    )
    probs_t = jnp.concatenate(
        [x.astype(jnp.float32).T.astype(jnp.bfloat16) for x in probs_list], axis=1
    )
    att_ref[...] = att.astype(att_ref.dtype)
    gq_ref[...] = gq.astype(gq_ref.dtype)
    gkv_ref[:, :lanes] = jnp.dot(grads_t, q_sel, preferred_element_type=jnp.float32)
    gkv_ref[:, lanes:] = jnp.dot(probs_t, g_sel, preferred_element_type=jnp.float32)


def block_attention(query, projected, grad_attn, bias, heads):
    queries, width = query.shape
    keys = projected.shape[0]
    head_dim = width // heads
    lanes = 128
    pairs = width // lanes
    kernel = functools.partial(attention_kernel, head_dim=head_dim, scale=head_dim ** (-0.5))
    flops = 2 * queries * keys * width * 2 * 6
    cost = pl.CostEstimate(
        flops=flops,
        transcendentals=queries * keys * heads,
        bytes_accessed=2 * (2 * queries * width + 2 * keys * width + 2 * queries * width)
        + 4 * queries * keys + 4 * 2 * keys * width,
    )
    return pl.pallas_call(
        kernel,
        grid=(pairs,),
        in_specs=[
            pl.BlockSpec((queries, lanes), lambda h: (0, h)),
            pl.BlockSpec((keys, lanes), lambda h: (0, h + pairs)),
            pl.BlockSpec((keys, lanes), lambda h: (0, h + 2 * pairs)),
            pl.BlockSpec((queries, lanes), lambda h: (0, h)),
            pl.BlockSpec((queries, keys), lambda h: (0, 0)),
        ],
        out_specs=[
            pl.BlockSpec((queries, lanes), lambda h: (0, h)),
            pl.BlockSpec((queries, lanes), lambda h: (0, h)),
            pl.BlockSpec((keys, 2 * lanes), lambda h: (0, h)),
        ],
        out_shape=[
            jax.ShapeDtypeStruct((queries, width), jnp.bfloat16),
            jax.ShapeDtypeStruct((queries, width), jnp.bfloat16),
            jax.ShapeDtypeStruct((keys, 2 * width), jnp.float32),
        ],
        cost_estimate=cost,
        name="block_attention",
    )(query, projected, projected, grad_attn, bias)


def grid_pairs(delta_lat, delta_lon):
    lat_count = lax.axis_size("lat")
    lon_count = lax.axis_size("lon")
    pairs = []
    for la in range(lat_count):
        if 0 <= la + delta_lat < lat_count:
            for lo in range(lon_count):
                target = (la + delta_lat) * lon_count + (lo + delta_lon) % lon_count
                pairs.append((la * lon_count + lo, target))
    return pairs


def sent_to(value, delta_lat, delta_lon):
    return lax.ppermute(value, ("lat", "lon"), grid_pairs(delta_lat, delta_lon))


def part(count, radius, step, giving):
    if step == 0:
        return slice(0, count)
    if (step < 0) == giving:
        return slice(count - radius, count)
    return slice(0, radius)


def grouped_send(pieces):
    lon_count = lax.axis_size("lon")
    groups = {}
    for index, (dl, db, value) in enumerate(pieces):
        groups.setdefault((dl, db % lon_count), []).append(index)
    out = [None] * len(pieces)
    for (dl, db), members in groups.items():
        values = [pieces[i][2] for i in members]
        got = sent_to(jnp.concatenate(values, axis=1), dl, db)
        offset = 0
        for i, value in zip(members, values):
            out[i] = got[:, offset : offset + value.shape[1]]
            offset += value.shape[1]
    return out


def halo_gather(block, radius):
    height, breadth, lanes = block.shape
    spots = []
    pieces = []
    for da in (-1, 0, 1):
        for db in (-1, 0, 1):
            if da == 0 and db == 0:
                continue
            piece = block[part(height, radius, da, True), part(breadth, radius, db, True)]
            spots.append((da, db))
            pieces.append((-da, -db, piece))
    got = dict(zip(spots, grouped_send(pieces)))
    got[(0, 0)] = block
    rows = [jnp.concatenate([got[(da, db)] for db in (-1, 0, 1)], axis=1) for da in (-1, 0, 1)]
    return jnp.concatenate(rows, axis=0)


def halo_return(ext_list, height, breadth, radius):
    row_slices = {-1: slice(0, radius), 0: slice(radius, radius + height), 1: slice(radius + height, None)}
    col_slices = {-1: slice(0, radius), 0: slice(radius, radius + breadth), 1: slice(radius + breadth, None)}
    owns = [ext[row_slices[0], col_slices[0]] for ext in ext_list]
    widths = [ext.shape[-1] for ext in ext_list]
    spots = []
    pieces = []
    for da in (-1, 0, 1):
        for db in (-1, 0, 1):
            if da == 0 and db == 0:
                continue
            joined = jnp.concatenate(
                [ext[row_slices[da], col_slices[db]] for ext in ext_list], axis=-1
            ).astype(jnp.bfloat16)
            spots.append((da, db))
            pieces.append((da, db, joined))
    for (da, db), got in zip(spots, grouped_send(pieces)):
        rs = part(height, radius, da, True)
        cs = part(breadth, radius, db, True)
        pad_rows = (rs.start, height - rs.stop)
        pad_cols = (cs.start, breadth - cs.stop)
        offset = 0
        for index, width in enumerate(widths):
            piece = got[..., offset : offset + width].astype(jnp.float32)
            offset += width
            owns[index] = owns[index] + jnp.pad(piece, (pad_rows, pad_cols, (0, 0)))
    return owns


def partner_rows_product(lhs, weights, axis):
    count = lax.axis_size(axis)
    if count != 2:
        full = lax.all_gather(weights, axis, axis=0, tiled=True)
        return lax.dot_general(lhs, full, TRANS_B, preferred_element_type=jnp.float32).astype(
            jnp.bfloat16
        )
    other = lax.ppermute(weights, axis, [(0, 1), (1, 0)])
    mine_part = lax.dot_general(lhs, weights, TRANS_B, preferred_element_type=jnp.float32)
    other_part = lax.dot_general(lhs, other, TRANS_B, preferred_element_type=jnp.float32)
    mine_part = mine_part.astype(jnp.bfloat16)
    other_part = other_part.astype(jnp.bfloat16)
    first = lax.axis_index(axis) == 0
    return jnp.where(
        first,
        jnp.concatenate([mine_part, other_part], axis=1),
        jnp.concatenate([other_part, mine_part], axis=1),
    )


def exchange_blocks(blocks, axis):
    count = lax.axis_size(axis)
    if count == 2:
        me = lax.axis_index(axis)
        mine = lax.dynamic_index_in_dim(blocks, me, 0, keepdims=False)
        theirs = lax.dynamic_index_in_dim(blocks, 1 - me, 0, keepdims=False)
        got = lax.ppermute(theirs, axis, [(0, 1), (1, 0)])
        return jnp.where(me == 0, jnp.stack([mine, got]), jnp.stack([got, mine]))
    flat = blocks.reshape((-1,) + blocks.shape[2:])
    out = lax.all_to_all(flat, axis, 0, 0, tiled=True)
    return out.reshape(blocks.shape)


def gather_members(value, axis):
    count = lax.axis_size(axis)
    if count == 2:
        me = lax.axis_index(axis)
        got = lax.ppermute(value, axis, [(0, 1), (1, 0)])
        return jnp.where(me == 0, jnp.stack([value, got]), jnp.stack([got, value]))
    return lax.all_gather(value, axis, axis=0, tiled=False)


def swap(value, axis):
    return lax.ppermute(value, axis, [(0, 1), (1, 0)])


def columns(value, index, size):
    return lax.dynamic_slice_in_dim(value, index * size, size, axis=1)


def split_rows(joined, shapes):
    out = []
    offset = 0
    for shape in shapes:
        count = 1
        for extent in shape[:-1]:
            count *= extent
        count = count * shape[-1] // joined.shape[-1]
        out.append(joined[offset : offset + count].reshape(shape))
        offset += count
    return out


def join_rows(parts, lanes):
    return jnp.concatenate([p.reshape(-1, lanes) for p in parts], axis=0)


def lat_return(ext_list, height, radius):
    owns = []
    tops = join_rows([ext[:radius] for ext in ext_list], ext_list[0].shape[-1])
    bottoms = join_rows([ext[radius + height :] for ext in ext_list], ext_list[0].shape[-1])
    shapes = [ext[:radius].shape for ext in ext_list]
    from_below = split_rows(shifted(tops.astype(jnp.bfloat16), "lat", -1), shapes)
    from_above = split_rows(shifted(bottoms.astype(jnp.bfloat16), "lat", 1), shapes)
    for ext, below, above in zip(ext_list, from_below, from_above):
        middle = (
            ext[radius : radius + height]
            + jnp.pad(below.astype(jnp.float32), ((height - radius, 0), (0, 0), (0, 0)))
            + jnp.pad(above.astype(jnp.float32), ((0, height - radius), (0, 0), (0, 0)))
        )
        owns.append(middle)
    return owns


def add_lon_rims(mid_list, from_right, from_left, breadth, radius):
    owns = []
    for mid, right, left in zip(mid_list, from_right, from_left):
        owns.append(
            mid[:, radius : radius + breadth]
            + jnp.pad(right.astype(jnp.float32), ((0, 0), (breadth - radius, 0), (0, 0)))
            + jnp.pad(left.astype(jnp.float32), ((0, 0), (0, breadth - radius), (0, 0)))
        )
    return owns


def shards(tokens, cotangent, valid_cells, w_qkv, w_out):
    inputs_here = tokens[0]
    grad_here = cotangent[0]
    height, breadth, width = inputs_here.shape
    radius = RADIUS
    ext_rows = height + 2 * radius
    ext_cols = breadth + 2 * radius
    pad_cols = -(-ext_cols // 8) * 8
    token_count = height * breadth
    key_count = ext_rows * pad_cols
    flat_inputs = inputs_here.reshape(token_count, width)
    flat_grad = grad_here.reshape(token_count, width)
    dp_count = lax.axis_size("dp")
    lat_count = lax.axis_size("lat")
    lon_count = lax.axis_size("lon")
    rows_half = width // dp_count
    cols_block = width // lon_count
    rows_block = rows_half // lat_count
    dp_index = lax.axis_index("dp")
    lon_index = lax.axis_index("lon")
    fast = dp_count == 2 and lon_count == 2

    if fast:
        qkv_other = swap(w_qkv, "dp")
        dp_got = swap(jnp.concatenate([w_out, flat_grad], axis=0), "dp")
        w_out_other = dp_got[: w_out.shape[0]]
        cot_dp = dp_got[w_out.shape[0] :]
        cot_send = jnp.concatenate(
            [columns(flat_grad, 1 - lon_index, cols_block), columns(cot_dp, 1 - lon_index, cols_block)],
            axis=0,
        )
        cot_lon = swap(cot_send, "lon")
        cot_group = jnp.concatenate(
            [
                columns(flat_grad, lon_index, cols_block),
                columns(cot_dp, lon_index, cols_block),
                cot_lon,
            ],
            axis=0,
        )
        mine_part = lax.dot_general(flat_grad, w_out, TRANS_B, preferred_element_type=jnp.float32)
        other_part = lax.dot_general(
            flat_grad, w_out_other, TRANS_B, preferred_element_type=jnp.float32
        )
        mine_part = mine_part.astype(jnp.bfloat16)
        other_part = other_part.astype(jnp.bfloat16)
        grad_attn = jnp.where(
            dp_index == 0,
            jnp.concatenate([mine_part, other_part], axis=1),
            jnp.concatenate([other_part, mine_part], axis=1),
        )

        def project(rows):
            own = jnp.dot(
                columns(rows, dp_index, rows_half), w_qkv, preferred_element_type=jnp.float32
            )
            other = jnp.dot(
                columns(rows, 1 - dp_index, rows_half), qkv_other, preferred_element_type=jnp.float32
            )
            return (own + other).astype(jnp.bfloat16)

        def back_project(grad_proj):
            own = lax.dot_general(grad_proj, w_qkv, TRANS_B, preferred_element_type=jnp.float32)
            other = lax.dot_general(grad_proj, qkv_other, TRANS_B, preferred_element_type=jnp.float32)
            own = own.astype(jnp.bfloat16)
            other = other.astype(jnp.bfloat16)
            return jnp.where(
                dp_index == 0,
                jnp.concatenate([own, other], axis=1),
                jnp.concatenate([other, own], axis=1),
            )
    else:
        panels = lax.all_gather(w_qkv, "dp", axis=0, tiled=True)
        cot_blocks = flat_grad.reshape(token_count, lon_count, cols_block).transpose(1, 0, 2)
        cot_lon = exchange_blocks(cot_blocks, "lon")
        cot_group = gather_members(cot_lon, "dp").reshape(-1, cols_block)
        grad_attn = partner_rows_product(flat_grad, w_out, "dp")


        def project(rows):
            out = jnp.dot(rows, panels, preferred_element_type=jnp.float32)
            return out.astype(jnp.bfloat16)

        def back_project(grad_proj):
            out = lax.dot_general(grad_proj, panels, TRANS_B, preferred_element_type=jnp.float32)
            return out.astype(jnp.bfloat16)

    tok_ext = halo_gather(inputs_here, radius)
    tok_ext = jnp.pad(tok_ext, ((0, 0), (0, pad_cols - ext_cols), (0, 0)))
    tok_ext = tok_ext.reshape(key_count, width)

    projected = project(tok_ext)
    query = projected.reshape(ext_rows, pad_cols, 3 * width)[
        radius : radius + height, radius : radius + breadth, :width
    ].reshape(token_count, width)

    wrapped = jnp.concatenate(
        [valid_cells[:, -radius:], valid_cells, valid_cells[:, :radius]], axis=1
    )
    framed = jnp.pad(wrapped, ((radius, radius), (0, 0)))
    valid_ext = lax.dynamic_slice(
        framed,
        (lax.axis_index("lat") * height, lon_index * breadth),
        (ext_rows, ext_cols),
    )
    valid_ext = jnp.pad(valid_ext, ((0, 0), (0, pad_cols - ext_cols))).reshape(1, key_count)
    query_pos = jnp.arange(token_count)
    key_pos = jnp.arange(key_count)
    delta_row = (key_pos // pad_cols)[None, :] - radius - (query_pos // breadth)[:, None]
    delta_col = (key_pos % pad_cols)[None, :] - radius - (query_pos % breadth)[:, None]
    inside = (jnp.abs(delta_row) <= radius) & (jnp.abs(delta_col) <= radius)
    itself = (delta_row == 0) & (delta_col == 0)
    allowed = inside & ((valid_ext == 1) | itself)
    bias = jnp.where(allowed, 0.0, -jnp.inf).astype(jnp.float32)

    attended, grad_query, grad_kv = block_attention(query, projected, grad_attn, bias, HEADS)

    grad_kv_ext = grad_kv.reshape(ext_rows, pad_cols, 2 * width)[:, :ext_cols]
    (grad_kv_own,) = halo_return([grad_kv_ext], height, breadth, radius)

    if fast:
        own_att = columns(attended, dp_index, rows_half)
        att_from_dp = swap(columns(attended, 1 - dp_index, rows_half), "dp")
        att_dp = jnp.concatenate([own_att, att_from_dp], axis=0)
        att_group = jnp.concatenate([att_dp, swap(att_dp, "lon")], axis=0)
    else:
        att_blocks = attended.reshape(token_count, dp_count, rows_half).transpose(1, 0, 2)
        att_dp = exchange_blocks(att_blocks, "dp")
        att_group = gather_members(att_dp, "lon")
        att_group = att_group.transpose(1, 0, 2, 3).reshape(-1, rows_half)

    device_count = dp_count * lat_count * lon_count
    partial = lax.dot_general(
        att_group, cot_group, (((0,), (0,)), ((), ())), preferred_element_type=jnp.float32
    ) * (1.0 / device_count)
    spread = lax.all_to_all(partial.astype(jnp.bfloat16), "lat", 0, 0, tiled=True)
    d_w_out = spread.astype(jnp.float32).reshape(lat_count, rows_block, cols_block).sum(axis=0)

    pairs = width // 128
    grad_kv_low = (
        grad_kv_own.astype(jnp.bfloat16)
        .reshape(token_count, pairs, 2, 128)
        .transpose(0, 2, 1, 3)
        .reshape(token_count, 2 * width)
    )
    grad_proj = jnp.concatenate([grad_query, grad_kv_low], axis=1)
    d_input = back_project(grad_proj).reshape(1, height, breadth, width)
    return (d_input, d_w_out)


def solution(mesh):
    in_specs = (
        P("dp", "lat", "lon", None),
        P("dp", "lat", "lon", None),
        P(),
        P("dp", None),
        P("dp", None),
    )
    out_specs = (P("dp", "lat", "lon", None), P(("dp", "lat"), "lon"))
    return jax.shard_map(shards, mesh=mesh, in_specs=in_specs, out_specs=out_specs, check_vma=False)
```

```python
import functools

import jax
import jax.numpy as jnp
from jax import lax
from jax.experimental import pallas as pl
from jax.sharding import PartitionSpec as P

HEADS = 16
RADIUS = 6

TRANS_B = (((1,), (1,)), ((), ()))


def passed_along(value, axis, steps):
    count = lax.axis_size(axis)
    pairs = [(source, (source + steps) % count) for source in range(count)]
    return lax.ppermute(value, axis, pairs)


def shifted(value, axis, by):
    count = lax.axis_size(axis)
    pairs = [(i, i + by) for i in range(count) if 0 <= i + by < count]
    return lax.ppermute(value, axis, pairs)


def extended(block, sides, width, periodic):
    for axis, dim in sides:
        count = lax.axis_size(axis)
        forward = [(i, i + 1) for i in range(count - 1)]
        if periodic:
            forward.append((count - 1, 0))
        backward = [(target, source) for source, target in forward]
        low = lax.ppermute(
            lax.slice_in_dim(block, block.shape[dim] - width, None, axis=dim), axis, forward
        )
        high = lax.ppermute(lax.slice_in_dim(block, 0, width, axis=dim), axis, backward)
        block = jnp.concatenate([low, block, high], axis=dim)
    return block


def attention_kernel(q_ref, k_ref, v_ref, g_ref, bias_ref, att_ref, gq_ref, gkv_ref, gkv_low_ref,
                     *, head_dim, scale):
    q = q_ref[...]
    g = g_ref[...]
    k = k_ref[...]
    v = v_ref[...]
    bias = bias_ref[...]
    lanes = q.shape[1]
    lane = lax.broadcasted_iota(jnp.int32, (1, lanes), 1)
    zero = jnp.zeros((), q.dtype)
    sels = [(lane >= j * head_dim) & (lane < (j + 1) * head_dim) for j in range(lanes // head_dim)]
    q_scaled = (q.astype(jnp.float32) * scale).astype(q.dtype)
    g_scaled = (g.astype(jnp.float32) * scale).astype(g.dtype)
    probs_list = []
    grads_list = []
    for sel in sels:
        qj = jnp.where(sel, q_scaled, zero)
        gj = jnp.where(sel, g_scaled, zero)
        masked = lax.dot_general(qj, k, TRANS_B, preferred_element_type=jnp.float32) + bias
        peak = jnp.max(masked, axis=1, keepdims=True)
        weights = jnp.exp(masked - peak)
        probs = weights * (1.0 / jnp.sum(weights, axis=1, keepdims=True))
        grad_probs = lax.dot_general(gj, v, TRANS_B, preferred_element_type=jnp.float32)
        centre = jnp.sum(probs * grad_probs, axis=1, keepdims=True)
        grads_list.append((probs * (grad_probs - centre)).astype(jnp.bfloat16))
        probs_list.append(probs.astype(jnp.bfloat16))
    k_sel = jnp.concatenate([jnp.where(sel, k, zero) for sel in sels], axis=0)
    v_sel = jnp.concatenate([jnp.where(sel, v, zero) for sel in sels], axis=0)
    q_sel = jnp.concatenate([jnp.where(sel, q, zero) for sel in sels], axis=0)
    g_sel = jnp.concatenate([jnp.where(sel, g, zero) for sel in sels], axis=0)
    probs_cat = jnp.concatenate(probs_list, axis=1)
    grads_cat = jnp.concatenate(grads_list, axis=1)
    att = jnp.dot(probs_cat, v_sel, preferred_element_type=jnp.float32)
    gq = jnp.dot(grads_cat, k_sel, preferred_element_type=jnp.float32)
    grads_t = jnp.concatenate(
        [x.astype(jnp.float32).T.astype(jnp.bfloat16) for x in grads_list], axis=1
    )
    probs_t = jnp.concatenate(
        [x.astype(jnp.float32).T.astype(jnp.bfloat16) for x in probs_list], axis=1
    )
    att_ref[...] = att.astype(att_ref.dtype)
    gq_ref[...] = gq.astype(gq_ref.dtype)
    grad_k = jnp.dot(grads_t, q_sel, preferred_element_type=jnp.float32)
    grad_v = jnp.dot(probs_t, g_sel, preferred_element_type=jnp.float32)
    gkv_ref[0] = grad_k
    gkv_ref[1] = grad_v
    gkv_low_ref[0] = grad_k.astype(gkv_low_ref.dtype)
    gkv_low_ref[1] = grad_v.astype(gkv_low_ref.dtype)


def block_attention(query, projected, grad_attn, bias, heads):
    queries, width = query.shape
    keys = projected.shape[0]
    head_dim = width // heads
    lanes = 128
    pairs = width // lanes
    kernel = functools.partial(attention_kernel, head_dim=head_dim, scale=head_dim ** (-0.5))
    flops = 2 * queries * keys * width * 2 * 6
    cost = pl.CostEstimate(
        flops=flops,
        transcendentals=queries * keys * heads,
        bytes_accessed=2 * (2 * queries * width + 2 * keys * width + 2 * queries * width)
        + 4 * queries * keys + 4 * 2 * keys * width,
    )
    return pl.pallas_call(
        kernel,
        grid=(pairs,),
        in_specs=[
            pl.BlockSpec((queries, lanes), lambda h: (0, h)),
            pl.BlockSpec((keys, lanes), lambda h: (0, h + pairs)),
            pl.BlockSpec((keys, lanes), lambda h: (0, h + 2 * pairs)),
            pl.BlockSpec((queries, lanes), lambda h: (0, h)),
            pl.BlockSpec((queries, keys), lambda h: (0, 0)),
        ],
        out_specs=[
            pl.BlockSpec((queries, lanes), lambda h: (0, h)),
            pl.BlockSpec((queries, lanes), lambda h: (0, h)),
            pl.BlockSpec((2, keys, lanes), lambda h: (0, 0, h)),
            pl.BlockSpec((2, keys, lanes), lambda h: (0, 0, h)),
        ],
        out_shape=[
            jax.ShapeDtypeStruct((queries, width), jnp.bfloat16),
            jax.ShapeDtypeStruct((queries, width), jnp.bfloat16),
            jax.ShapeDtypeStruct((2, keys, width), jnp.float32),
            jax.ShapeDtypeStruct((2, keys, width), jnp.bfloat16),
        ],
        cost_estimate=cost,
        name="block_attention",
    )(query, projected, projected, grad_attn, bias)


def grid_pairs(delta_lat, delta_lon):
    lat_count = lax.axis_size("lat")
    lon_count = lax.axis_size("lon")
    pairs = []
    for la in range(lat_count):
        if 0 <= la + delta_lat < lat_count:
            for lo in range(lon_count):
                target = (la + delta_lat) * lon_count + (lo + delta_lon) % lon_count
                pairs.append((la * lon_count + lo, target))
    return pairs


def sent_to(value, delta_lat, delta_lon):
    return lax.ppermute(value, ("lat", "lon"), grid_pairs(delta_lat, delta_lon))


def part(count, radius, step, giving):
    if step == 0:
        return slice(0, count)
    if (step < 0) == giving:
        return slice(count - radius, count)
    return slice(0, radius)


def grouped_send(pieces, axis):
    lon_count = lax.axis_size("lon")
    groups = {}
    for index, (dl, db, value) in enumerate(pieces):
        groups.setdefault((dl, db % lon_count), []).append(index)
    out = [None] * len(pieces)
    for (dl, db), members in groups.items():
        values = [pieces[i][2] for i in members]
        got = sent_to(jnp.concatenate(values, axis=axis), dl, db)
        offset = 0
        for i, value in zip(members, values):
            out[i] = lax.slice_in_dim(got, offset, offset + value.shape[axis], axis=axis)
            offset += value.shape[axis]
    return out


def halo_gather(block, radius):
    height, breadth, lanes = block.shape
    spots = []
    pieces = []
    for da in (-1, 0, 1):
        for db in (-1, 0, 1):
            if da == 0 and db == 0:
                continue
            piece = block[part(height, radius, da, True), part(breadth, radius, db, True)]
            spots.append((da, db))
            pieces.append((-da, -db, piece))
    got = dict(zip(spots, grouped_send(pieces, 1)))
    got[(0, 0)] = block
    rows = [jnp.concatenate([got[(da, db)] for db in (-1, 0, 1)], axis=1) for da in (-1, 0, 1)]
    return jnp.concatenate(rows, axis=0)


def halo_return(ext, ext_low, height, breadth, radius):
    row_slices = {-1: slice(0, radius), 0: slice(radius, radius + height), 1: slice(radius + height, None)}
    col_slices = {-1: slice(0, radius), 0: slice(radius, radius + breadth), 1: slice(radius + breadth, None)}
    own = ext[:, row_slices[0], col_slices[0]]
    spots = []
    pieces = []
    for da in (-1, 0, 1):
        for db in (-1, 0, 1):
            if da == 0 and db == 0:
                continue
            spots.append((da, db))
            pieces.append((da, db, ext_low[:, row_slices[da], col_slices[db]]))
    for (da, db), got in zip(spots, grouped_send(pieces, 2)):
        rs = part(height, radius, da, True)
        cs = part(breadth, radius, db, True)
        pad_rows = (rs.start, height - rs.stop)
        pad_cols = (cs.start, breadth - cs.stop)
        own = own + jnp.pad(got.astype(jnp.float32), ((0, 0), pad_rows, pad_cols, (0, 0)))
    return own


def partner_rows_product(lhs, weights, axis):
    count = lax.axis_size(axis)
    if count != 2:
        full = lax.all_gather(weights, axis, axis=0, tiled=True)
        return lax.dot_general(lhs, full, TRANS_B, preferred_element_type=jnp.float32).astype(
            jnp.bfloat16
        )
    other = lax.ppermute(weights, axis, [(0, 1), (1, 0)])
    mine_part = lax.dot_general(lhs, weights, TRANS_B, preferred_element_type=jnp.float32)
    other_part = lax.dot_general(lhs, other, TRANS_B, preferred_element_type=jnp.float32)
    mine_part = mine_part.astype(jnp.bfloat16)
    other_part = other_part.astype(jnp.bfloat16)
    first = lax.axis_index(axis) == 0
    return jnp.where(
        first,
        jnp.concatenate([mine_part, other_part], axis=1),
        jnp.concatenate([other_part, mine_part], axis=1),
    )


def exchange_blocks(blocks, axis):
    count = lax.axis_size(axis)
    if count == 2:
        me = lax.axis_index(axis)
        mine = lax.dynamic_index_in_dim(blocks, me, 0, keepdims=False)
        theirs = lax.dynamic_index_in_dim(blocks, 1 - me, 0, keepdims=False)
        got = lax.ppermute(theirs, axis, [(0, 1), (1, 0)])
        return jnp.where(me == 0, jnp.stack([mine, got]), jnp.stack([got, mine]))
    flat = blocks.reshape((-1,) + blocks.shape[2:])
    out = lax.all_to_all(flat, axis, 0, 0, tiled=True)
    return out.reshape(blocks.shape)


def gather_members(value, axis):
    count = lax.axis_size(axis)
    if count == 2:
        me = lax.axis_index(axis)
        got = lax.ppermute(value, axis, [(0, 1), (1, 0)])
        return jnp.where(me == 0, jnp.stack([value, got]), jnp.stack([got, value]))
    return lax.all_gather(value, axis, axis=0, tiled=False)


def swap(value, axis):
    return lax.ppermute(value, axis, [(0, 1), (1, 0)])


def columns(value, index, size):
    return lax.dynamic_slice_in_dim(value, index * size, size, axis=1)


def split_rows(joined, shapes):
    out = []
    offset = 0
    for shape in shapes:
        count = 1
        for extent in shape[:-1]:
            count *= extent
        count = count * shape[-1] // joined.shape[-1]
        out.append(joined[offset : offset + count].reshape(shape))
        offset += count
    return out


def join_rows(parts, lanes):
    return jnp.concatenate([p.reshape(-1, lanes) for p in parts], axis=0)


def lat_return(ext_list, height, radius):
    owns = []
    tops = join_rows([ext[:radius] for ext in ext_list], ext_list[0].shape[-1])
    bottoms = join_rows([ext[radius + height :] for ext in ext_list], ext_list[0].shape[-1])
    shapes = [ext[:radius].shape for ext in ext_list]
    from_below = split_rows(shifted(tops.astype(jnp.bfloat16), "lat", -1), shapes)
    from_above = split_rows(shifted(bottoms.astype(jnp.bfloat16), "lat", 1), shapes)
    for ext, below, above in zip(ext_list, from_below, from_above):
        middle = (
            ext[radius : radius + height]
            + jnp.pad(below.astype(jnp.float32), ((height - radius, 0), (0, 0), (0, 0)))
            + jnp.pad(above.astype(jnp.float32), ((0, height - radius), (0, 0), (0, 0)))
        )
        owns.append(middle)
    return owns


def add_lon_rims(mid_list, from_right, from_left, breadth, radius):
    owns = []
    for mid, right, left in zip(mid_list, from_right, from_left):
        owns.append(
            mid[:, radius : radius + breadth]
            + jnp.pad(right.astype(jnp.float32), ((0, 0), (breadth - radius, 0), (0, 0)))
            + jnp.pad(left.astype(jnp.float32), ((0, 0), (0, breadth - radius), (0, 0)))
        )
    return owns


def shards(tokens, cotangent, valid_cells, w_qkv, w_out):
    inputs_here = tokens[0]
    grad_here = cotangent[0]
    height, breadth, width = inputs_here.shape
    radius = RADIUS
    ext_rows = height + 2 * radius
    ext_cols = breadth + 2 * radius
    pad_cols = -(-ext_cols // 8) * 8
    token_count = height * breadth
    key_count = ext_rows * pad_cols
    flat_inputs = inputs_here.reshape(token_count, width)
    flat_grad = grad_here.reshape(token_count, width)
    dp_count = lax.axis_size("dp")
    lat_count = lax.axis_size("lat")
    lon_count = lax.axis_size("lon")
    rows_half = width // dp_count
    cols_block = width // lon_count
    rows_block = rows_half // lat_count
    dp_index = lax.axis_index("dp")
    lon_index = lax.axis_index("lon")
    fast = dp_count == 2 and lon_count == 2

    if fast:
        qkv_other = swap(w_qkv, "dp")
        dp_got = swap(jnp.concatenate([w_out, flat_grad], axis=0), "dp")
        w_out_other = dp_got[: w_out.shape[0]]
        cot_dp = dp_got[w_out.shape[0] :]
        cot_send = jnp.concatenate(
            [columns(flat_grad, 1 - lon_index, cols_block), columns(cot_dp, 1 - lon_index, cols_block)],
            axis=0,
        )
        cot_lon = swap(cot_send, "lon")
        cot_group = jnp.concatenate(
            [
                columns(flat_grad, lon_index, cols_block),
                columns(cot_dp, lon_index, cols_block),
                cot_lon,
            ],
            axis=0,
        )
        mine_part = lax.dot_general(flat_grad, w_out, TRANS_B, preferred_element_type=jnp.float32)
        other_part = lax.dot_general(
            flat_grad, w_out_other, TRANS_B, preferred_element_type=jnp.float32
        )
        mine_part = mine_part.astype(jnp.bfloat16)
        other_part = other_part.astype(jnp.bfloat16)
        grad_attn = jnp.where(
            dp_index == 0,
            jnp.concatenate([mine_part, other_part], axis=1),
            jnp.concatenate([other_part, mine_part], axis=1),
        )

        def project(rows):
            own = jnp.dot(
                columns(rows, dp_index, rows_half), w_qkv, preferred_element_type=jnp.float32
            )
            other = jnp.dot(
                columns(rows, 1 - dp_index, rows_half), qkv_other, preferred_element_type=jnp.float32
            )
            return (own + other).astype(jnp.bfloat16)

        def back_project(grad_proj):
            own = lax.dot_general(grad_proj, w_qkv, TRANS_B, preferred_element_type=jnp.float32)
            other = lax.dot_general(grad_proj, qkv_other, TRANS_B, preferred_element_type=jnp.float32)
            own = own.astype(jnp.bfloat16)
            other = other.astype(jnp.bfloat16)
            return jnp.where(
                dp_index == 0,
                jnp.concatenate([own, other], axis=1),
                jnp.concatenate([other, own], axis=1),
            )
    else:
        panels = lax.all_gather(w_qkv, "dp", axis=0, tiled=True)
        cot_blocks = flat_grad.reshape(token_count, lon_count, cols_block).transpose(1, 0, 2)
        cot_lon = exchange_blocks(cot_blocks, "lon")
        cot_group = gather_members(cot_lon, "dp").reshape(-1, cols_block)
        grad_attn = partner_rows_product(flat_grad, w_out, "dp")


        def project(rows):
            out = jnp.dot(rows, panels, preferred_element_type=jnp.float32)
            return out.astype(jnp.bfloat16)

        def back_project(grad_proj):
            out = lax.dot_general(grad_proj, panels, TRANS_B, preferred_element_type=jnp.float32)
            return out.astype(jnp.bfloat16)

    tok_ext = halo_gather(inputs_here, radius)
    tok_ext = jnp.pad(tok_ext, ((0, 0), (0, pad_cols - ext_cols), (0, 0)))
    tok_ext = tok_ext.reshape(key_count, width)

    projected = project(tok_ext)
    query = projected.reshape(ext_rows, pad_cols, 3 * width)[
        radius : radius + height, radius : radius + breadth, :width
    ].reshape(token_count, width)

    wrapped = jnp.concatenate(
        [valid_cells[:, -radius:], valid_cells, valid_cells[:, :radius]], axis=1
    )
    framed = jnp.pad(wrapped, ((radius, radius), (0, 0)))
    valid_ext = lax.dynamic_slice(
        framed,
        (lax.axis_index("lat") * height, lon_index * breadth),
        (ext_rows, ext_cols),
    )
    valid_ext = jnp.pad(valid_ext, ((0, 0), (0, pad_cols - ext_cols))).reshape(1, key_count)
    query_pos = jnp.arange(token_count)
    key_pos = jnp.arange(key_count)
    delta_row = (key_pos // pad_cols)[None, :] - radius - (query_pos // breadth)[:, None]
    delta_col = (key_pos % pad_cols)[None, :] - radius - (query_pos % breadth)[:, None]
    inside = (jnp.abs(delta_row) <= radius) & (jnp.abs(delta_col) <= radius)
    itself = (delta_row == 0) & (delta_col == 0)
    allowed = inside & ((valid_ext == 1) | itself)
    bias = jnp.where(allowed, 0.0, -jnp.inf).astype(jnp.float32)

    attended, grad_query, grad_kv, grad_kv_low = block_attention(
        query, projected, grad_attn, bias, HEADS
    )

    grad_kv_ext = grad_kv.reshape(2, ext_rows, pad_cols, width)[:, :, :ext_cols]
    grad_kv_low_ext = grad_kv_low.reshape(2, ext_rows, pad_cols, width)[:, :, :ext_cols]
    grad_kv_own = halo_return(grad_kv_ext, grad_kv_low_ext, height, breadth, radius)

    if fast:
        own_att = columns(attended, dp_index, rows_half)
        att_from_dp = swap(columns(attended, 1 - dp_index, rows_half), "dp")
        att_dp = jnp.concatenate([own_att, att_from_dp], axis=0)
        att_group = jnp.concatenate([att_dp, swap(att_dp, "lon")], axis=0)
    else:
        att_blocks = attended.reshape(token_count, dp_count, rows_half).transpose(1, 0, 2)
        att_dp = exchange_blocks(att_blocks, "dp")
        att_group = gather_members(att_dp, "lon")
        att_group = att_group.transpose(1, 0, 2, 3).reshape(-1, rows_half)

    device_count = dp_count * lat_count * lon_count
    partial = lax.dot_general(
        att_group, cot_group, (((0,), (0,)), ((), ())), preferred_element_type=jnp.float32
    ) * (1.0 / device_count)
    spread = lax.all_to_all(partial.astype(jnp.bfloat16), "lat", 0, 0, tiled=True)
    d_w_out = spread.astype(jnp.float32).reshape(lat_count, rows_block, cols_block).sum(axis=0)

    grad_kv_own = grad_kv_own.astype(jnp.bfloat16).reshape(2, token_count, width)
    grad_proj = jnp.concatenate([grad_query, grad_kv_own[0], grad_kv_own[1]], axis=1)
    d_input = back_project(grad_proj).reshape(1, height, breadth, width)
    return (d_input, d_w_out)


def solution(mesh):
    in_specs = (
        P("dp", "lat", "lon", None),
        P("dp", "lat", "lon", None),
        P(),
        P("dp", None),
        P("dp", None),
    )
    out_specs = (P("dp", "lat", "lon", None), P(("dp", "lat"), "lon"))
    return jax.shard_map(shards, mesh=mesh, in_specs=in_specs, out_specs=out_specs, check_vma=False)
```

```python
import functools

import jax
import jax.numpy as jnp
from jax import lax
from jax.experimental import pallas as pl
from jax.sharding import PartitionSpec as P

HEADS = 16
RADIUS = 6

TRANS_B = (((1,), (1,)), ((), ()))


def passed_along(value, axis, steps):
    count = lax.axis_size(axis)
    pairs = [(source, (source + steps) % count) for source in range(count)]
    return lax.ppermute(value, axis, pairs)


def shifted(value, axis, by):
    count = lax.axis_size(axis)
    pairs = [(i, i + by) for i in range(count) if 0 <= i + by < count]
    return lax.ppermute(value, axis, pairs)


def extended(block, sides, width, periodic):
    for axis, dim in sides:
        count = lax.axis_size(axis)
        forward = [(i, i + 1) for i in range(count - 1)]
        if periodic:
            forward.append((count - 1, 0))
        backward = [(target, source) for source, target in forward]
        low = lax.ppermute(
            lax.slice_in_dim(block, block.shape[dim] - width, None, axis=dim), axis, forward
        )
        high = lax.ppermute(lax.slice_in_dim(block, 0, width, axis=dim), axis, backward)
        block = jnp.concatenate([low, block, high], axis=dim)
    return block


def attention_kernel(q_ref, k_ref, v_ref, g_ref, bias_ref, att_ref, gq_ref, gkv_ref, gkv_low_ref,
                     *, head_dim, scale):
    q = q_ref[...]
    g = g_ref[...]
    k = k_ref[...]
    v = v_ref[...]
    bias = bias_ref[...]
    lanes = q.shape[1]
    lane = lax.broadcasted_iota(jnp.int32, (1, lanes), 1)
    zero = jnp.zeros((), q.dtype)
    sels = [(lane >= j * head_dim) & (lane < (j + 1) * head_dim) for j in range(lanes // head_dim)]
    q_scaled = (q.astype(jnp.float32) * scale).astype(q.dtype)
    g_scaled = (g.astype(jnp.float32) * scale).astype(g.dtype)
    probs_list = []
    grads_list = []
    for sel in sels:
        qj = jnp.where(sel, q_scaled, zero)
        gj = jnp.where(sel, g_scaled, zero)
        masked = lax.dot_general(qj, k, TRANS_B, preferred_element_type=jnp.float32) + bias
        peak = jnp.max(masked, axis=1, keepdims=True)
        weights = jnp.exp(masked - peak)
        probs = weights * (1.0 / jnp.sum(weights, axis=1, keepdims=True))
        grad_probs = lax.dot_general(gj, v, TRANS_B, preferred_element_type=jnp.float32)
        centre = jnp.sum(probs * grad_probs, axis=1, keepdims=True)
        grads_list.append((probs * (grad_probs - centre)).astype(jnp.bfloat16))
        probs_list.append(probs.astype(jnp.bfloat16))
    k_sel = jnp.concatenate([jnp.where(sel, k, zero) for sel in sels], axis=0)
    v_sel = jnp.concatenate([jnp.where(sel, v, zero) for sel in sels], axis=0)
    q_sel = jnp.concatenate([jnp.where(sel, q, zero) for sel in sels], axis=0)
    g_sel = jnp.concatenate([jnp.where(sel, g, zero) for sel in sels], axis=0)
    probs_cat = jnp.concatenate(probs_list, axis=1)
    grads_cat = jnp.concatenate(grads_list, axis=1)
    att = jnp.dot(probs_cat, v_sel, preferred_element_type=jnp.float32)
    gq = jnp.dot(grads_cat, k_sel, preferred_element_type=jnp.float32)
    grads_t = jnp.concatenate(
        [x.astype(jnp.float32).T.astype(jnp.bfloat16) for x in grads_list], axis=1
    )
    probs_t = jnp.concatenate(
        [x.astype(jnp.float32).T.astype(jnp.bfloat16) for x in probs_list], axis=1
    )
    att_ref[...] = att.astype(att_ref.dtype)
    gq_ref[...] = gq.astype(gq_ref.dtype)
    grad_k = jnp.dot(grads_t, q_sel, preferred_element_type=jnp.float32)
    grad_v = jnp.dot(probs_t, g_sel, preferred_element_type=jnp.float32)
    gkv_ref[0] = grad_k
    gkv_ref[1] = grad_v
    gkv_low_ref[0] = grad_k.astype(gkv_low_ref.dtype)
    gkv_low_ref[1] = grad_v.astype(gkv_low_ref.dtype)


def block_attention(query, projected, grad_attn, bias, heads):
    queries, width = query.shape
    keys = projected.shape[0]
    head_dim = width // heads
    lanes = 128
    pairs = width // lanes
    kernel = functools.partial(attention_kernel, head_dim=head_dim, scale=head_dim ** (-0.5))
    flops = 2 * queries * keys * width * 2 * 6
    cost = pl.CostEstimate(
        flops=flops,
        transcendentals=queries * keys * heads,
        bytes_accessed=2 * (2 * queries * width + 2 * keys * width + 2 * queries * width)
        + 4 * queries * keys + 4 * 2 * keys * width,
    )
    return pl.pallas_call(
        kernel,
        grid=(pairs,),
        in_specs=[
            pl.BlockSpec((queries, lanes), lambda h: (0, h)),
            pl.BlockSpec((keys, lanes), lambda h: (0, h + pairs)),
            pl.BlockSpec((keys, lanes), lambda h: (0, h + 2 * pairs)),
            pl.BlockSpec((queries, lanes), lambda h: (0, h)),
            pl.BlockSpec((queries, keys), lambda h: (0, 0)),
        ],
        out_specs=[
            pl.BlockSpec((queries, lanes), lambda h: (0, h)),
            pl.BlockSpec((queries, lanes), lambda h: (0, h)),
            pl.BlockSpec((2, keys, lanes), lambda h: (0, 0, h)),
            pl.BlockSpec((2, keys, lanes), lambda h: (0, 0, h)),
        ],
        out_shape=[
            jax.ShapeDtypeStruct((queries, width), jnp.bfloat16),
            jax.ShapeDtypeStruct((queries, width), jnp.bfloat16),
            jax.ShapeDtypeStruct((2, keys, width), jnp.float32),
            jax.ShapeDtypeStruct((2, keys, width), jnp.bfloat16),
        ],
        cost_estimate=cost,
        name="block_attention",
    )(query, projected, projected, grad_attn, bias)


def grid_pairs(delta_lat, delta_lon):
    lat_count = lax.axis_size("lat")
    lon_count = lax.axis_size("lon")
    pairs = []
    for la in range(lat_count):
        if 0 <= la + delta_lat < lat_count:
            for lo in range(lon_count):
                target = (la + delta_lat) * lon_count + (lo + delta_lon) % lon_count
                pairs.append((la * lon_count + lo, target))
    return pairs


def sent_to(value, delta_lat, delta_lon):
    return lax.ppermute(value, ("lat", "lon"), grid_pairs(delta_lat, delta_lon))


def part(count, radius, step, giving):
    if step == 0:
        return slice(0, count)
    if (step < 0) == giving:
        return slice(count - radius, count)
    return slice(0, radius)


def grouped_send(pieces, axis):
    lon_count = lax.axis_size("lon")
    groups = {}
    for index, (dl, db, value) in enumerate(pieces):
        groups.setdefault((dl, db % lon_count), []).append(index)
    out = [None] * len(pieces)
    for (dl, db), members in groups.items():
        values = [pieces[i][2] for i in members]
        got = sent_to(jnp.concatenate(values, axis=axis), dl, db)
        offset = 0
        for i, value in zip(members, values):
            out[i] = lax.slice_in_dim(got, offset, offset + value.shape[axis], axis=axis)
            offset += value.shape[axis]
    return out


def halo_gather(block, radius):
    height, breadth, lanes = block.shape
    spots = []
    pieces = []
    for da in (-1, 0, 1):
        for db in (-1, 0, 1):
            if da == 0 and db == 0:
                continue
            piece = block[part(height, radius, da, True), part(breadth, radius, db, True)]
            spots.append((da, db))
            pieces.append((-da, -db, piece))
    got = dict(zip(spots, grouped_send(pieces, 1)))
    got[(0, 0)] = block
    rows = [jnp.concatenate([got[(da, db)] for db in (-1, 0, 1)], axis=1) for da in (-1, 0, 1)]
    return jnp.concatenate(rows, axis=0)


def halo_return(ext, ext_low, height, breadth, radius):
    lon_count = lax.axis_size("lon")
    lefts = ext_low[:, :, :radius]
    rights = ext_low[:, :, radius + breadth :]
    if lon_count == 2:
        got = swap(jnp.concatenate([lefts, rights], axis=2), "lon")
        from_right = got[:, :, :radius]
        from_left = got[:, :, radius:]
    else:
        from_right = passed_along(lefts, "lon", -1)
        from_left = passed_along(rights, "lon", 1)
    middle = (
        ext[:, :, radius : radius + breadth]
        + jnp.pad(from_right.astype(jnp.float32), ((0, 0), (0, 0), (breadth - radius, 0), (0, 0)))
        + jnp.pad(from_left.astype(jnp.float32), ((0, 0), (0, 0), (0, breadth - radius), (0, 0)))
    )
    from_below = shifted(middle[:, :radius].astype(jnp.bfloat16), "lat", -1)
    from_above = shifted(middle[:, radius + height :].astype(jnp.bfloat16), "lat", 1)
    return (
        middle[:, radius : radius + height]
        + jnp.pad(from_below.astype(jnp.float32), ((0, 0), (height - radius, 0), (0, 0), (0, 0)))
        + jnp.pad(from_above.astype(jnp.float32), ((0, 0), (0, height - radius), (0, 0), (0, 0)))
    )


def halo_tokens(block, radius):
    breadth = block.shape[1]
    rows_ext = extended(block, (("lat", 0),), radius, False)
    if lax.axis_size("lon") != 2:
        return extended(rows_ext, (("lon", 1),), radius, True)
    got = swap(
        jnp.concatenate([rows_ext[:, breadth - radius :], rows_ext[:, :radius]], axis=1), "lon"
    )
    return jnp.concatenate([got[:, :radius], rows_ext, got[:, radius:]], axis=1)


def partner_rows_product(lhs, weights, axis):
    count = lax.axis_size(axis)
    if count != 2:
        full = lax.all_gather(weights, axis, axis=0, tiled=True)
        return lax.dot_general(lhs, full, TRANS_B, preferred_element_type=jnp.float32).astype(
            jnp.bfloat16
        )
    other = lax.ppermute(weights, axis, [(0, 1), (1, 0)])
    mine_part = lax.dot_general(lhs, weights, TRANS_B, preferred_element_type=jnp.float32)
    other_part = lax.dot_general(lhs, other, TRANS_B, preferred_element_type=jnp.float32)
    mine_part = mine_part.astype(jnp.bfloat16)
    other_part = other_part.astype(jnp.bfloat16)
    first = lax.axis_index(axis) == 0
    return jnp.where(
        first,
        jnp.concatenate([mine_part, other_part], axis=1),
        jnp.concatenate([other_part, mine_part], axis=1),
    )


def exchange_blocks(blocks, axis):
    count = lax.axis_size(axis)
    if count == 2:
        me = lax.axis_index(axis)
        mine = lax.dynamic_index_in_dim(blocks, me, 0, keepdims=False)
        theirs = lax.dynamic_index_in_dim(blocks, 1 - me, 0, keepdims=False)
        got = lax.ppermute(theirs, axis, [(0, 1), (1, 0)])
        return jnp.where(me == 0, jnp.stack([mine, got]), jnp.stack([got, mine]))
    flat = blocks.reshape((-1,) + blocks.shape[2:])
    out = lax.all_to_all(flat, axis, 0, 0, tiled=True)
    return out.reshape(blocks.shape)


def gather_members(value, axis):
    count = lax.axis_size(axis)
    if count == 2:
        me = lax.axis_index(axis)
        got = lax.ppermute(value, axis, [(0, 1), (1, 0)])
        return jnp.where(me == 0, jnp.stack([value, got]), jnp.stack([got, value]))
    return lax.all_gather(value, axis, axis=0, tiled=False)


def swap(value, axis):
    return lax.ppermute(value, axis, [(0, 1), (1, 0)])


def columns(value, index, size):
    return lax.dynamic_slice_in_dim(value, index * size, size, axis=1)


def split_rows(joined, shapes):
    out = []
    offset = 0
    for shape in shapes:
        count = 1
        for extent in shape[:-1]:
            count *= extent
        count = count * shape[-1] // joined.shape[-1]
        out.append(joined[offset : offset + count].reshape(shape))
        offset += count
    return out


def join_rows(parts, lanes):
    return jnp.concatenate([p.reshape(-1, lanes) for p in parts], axis=0)


def lat_return(ext_list, height, radius):
    owns = []
    tops = join_rows([ext[:radius] for ext in ext_list], ext_list[0].shape[-1])
    bottoms = join_rows([ext[radius + height :] for ext in ext_list], ext_list[0].shape[-1])
    shapes = [ext[:radius].shape for ext in ext_list]
    from_below = split_rows(shifted(tops.astype(jnp.bfloat16), "lat", -1), shapes)
    from_above = split_rows(shifted(bottoms.astype(jnp.bfloat16), "lat", 1), shapes)
    for ext, below, above in zip(ext_list, from_below, from_above):
        middle = (
            ext[radius : radius + height]
            + jnp.pad(below.astype(jnp.float32), ((height - radius, 0), (0, 0), (0, 0)))
            + jnp.pad(above.astype(jnp.float32), ((0, height - radius), (0, 0), (0, 0)))
        )
        owns.append(middle)
    return owns


def add_lon_rims(mid_list, from_right, from_left, breadth, radius):
    owns = []
    for mid, right, left in zip(mid_list, from_right, from_left):
        owns.append(
            mid[:, radius : radius + breadth]
            + jnp.pad(right.astype(jnp.float32), ((0, 0), (breadth - radius, 0), (0, 0)))
            + jnp.pad(left.astype(jnp.float32), ((0, 0), (0, breadth - radius), (0, 0)))
        )
    return owns


def shards(tokens, cotangent, valid_cells, w_qkv, w_out):
    inputs_here = tokens[0]
    grad_here = cotangent[0]
    height, breadth, width = inputs_here.shape
    radius = RADIUS
    ext_rows = height + 2 * radius
    ext_cols = breadth + 2 * radius
    pad_cols = -(-ext_cols // 8) * 8
    token_count = height * breadth
    key_count = ext_rows * pad_cols
    flat_inputs = inputs_here.reshape(token_count, width)
    flat_grad = grad_here.reshape(token_count, width)
    dp_count = lax.axis_size("dp")
    lat_count = lax.axis_size("lat")
    lon_count = lax.axis_size("lon")
    rows_half = width // dp_count
    cols_block = width // lon_count
    rows_block = rows_half // lat_count
    dp_index = lax.axis_index("dp")
    lon_index = lax.axis_index("lon")
    fast = dp_count == 2 and lon_count == 2

    if fast:
        qkv_other = swap(w_qkv, "dp")
        dp_got = swap(jnp.concatenate([w_out, flat_grad], axis=0), "dp")
        w_out_other = dp_got[: w_out.shape[0]]
        cot_dp = dp_got[w_out.shape[0] :]
        cot_send = jnp.concatenate(
            [columns(flat_grad, 1 - lon_index, cols_block), columns(cot_dp, 1 - lon_index, cols_block)],
            axis=0,
        )
        cot_lon = swap(cot_send, "lon")
        cot_group = jnp.concatenate(
            [
                columns(flat_grad, lon_index, cols_block),
                columns(cot_dp, lon_index, cols_block),
                cot_lon,
            ],
            axis=0,
        )
        mine_part = lax.dot_general(flat_grad, w_out, TRANS_B, preferred_element_type=jnp.float32)
        other_part = lax.dot_general(
            flat_grad, w_out_other, TRANS_B, preferred_element_type=jnp.float32
        )
        mine_part = mine_part.astype(jnp.bfloat16)
        other_part = other_part.astype(jnp.bfloat16)
        grad_attn = jnp.where(
            dp_index == 0,
            jnp.concatenate([mine_part, other_part], axis=1),
            jnp.concatenate([other_part, mine_part], axis=1),
        )

        def project(rows):
            own = jnp.dot(
                columns(rows, dp_index, rows_half), w_qkv, preferred_element_type=jnp.float32
            )
            other = jnp.dot(
                columns(rows, 1 - dp_index, rows_half), qkv_other, preferred_element_type=jnp.float32
            )
            return (own + other).astype(jnp.bfloat16)

        def back_project(grad_proj):
            own = lax.dot_general(grad_proj, w_qkv, TRANS_B, preferred_element_type=jnp.float32)
            other = lax.dot_general(grad_proj, qkv_other, TRANS_B, preferred_element_type=jnp.float32)
            own = own.astype(jnp.bfloat16)
            other = other.astype(jnp.bfloat16)
            return jnp.where(
                dp_index == 0,
                jnp.concatenate([own, other], axis=1),
                jnp.concatenate([other, own], axis=1),
            )
    else:
        panels = lax.all_gather(w_qkv, "dp", axis=0, tiled=True)
        cot_blocks = flat_grad.reshape(token_count, lon_count, cols_block).transpose(1, 0, 2)
        cot_lon = exchange_blocks(cot_blocks, "lon")
        cot_group = gather_members(cot_lon, "dp").reshape(-1, cols_block)
        grad_attn = partner_rows_product(flat_grad, w_out, "dp")


        def project(rows):
            out = jnp.dot(rows, panels, preferred_element_type=jnp.float32)
            return out.astype(jnp.bfloat16)

        def back_project(grad_proj):
            out = lax.dot_general(grad_proj, panels, TRANS_B, preferred_element_type=jnp.float32)
            return out.astype(jnp.bfloat16)

    tok_ext = halo_tokens(inputs_here, radius)
    tok_ext = jnp.pad(tok_ext, ((0, 0), (0, pad_cols - ext_cols), (0, 0)))
    tok_ext = tok_ext.reshape(key_count, width)

    projected = project(tok_ext)
    query = projected.reshape(ext_rows, pad_cols, 3 * width)[
        radius : radius + height, radius : radius + breadth, :width
    ].reshape(token_count, width)

    wrapped = jnp.concatenate(
        [valid_cells[:, -radius:], valid_cells, valid_cells[:, :radius]], axis=1
    )
    framed = jnp.pad(wrapped, ((radius, radius), (0, 0)))
    valid_ext = lax.dynamic_slice(
        framed,
        (lax.axis_index("lat") * height, lon_index * breadth),
        (ext_rows, ext_cols),
    )
    valid_ext = jnp.pad(valid_ext, ((0, 0), (0, pad_cols - ext_cols))).reshape(1, key_count)
    query_pos = jnp.arange(token_count)
    key_pos = jnp.arange(key_count)
    delta_row = (key_pos // pad_cols)[None, :] - radius - (query_pos // breadth)[:, None]
    delta_col = (key_pos % pad_cols)[None, :] - radius - (query_pos % breadth)[:, None]
    inside = (jnp.abs(delta_row) <= radius) & (jnp.abs(delta_col) <= radius)
    itself = (delta_row == 0) & (delta_col == 0)
    allowed = inside & ((valid_ext == 1) | itself)
    bias = jnp.where(allowed, 0.0, -jnp.inf).astype(jnp.float32)

    attended, grad_query, grad_kv, grad_kv_low = block_attention(
        query, projected, grad_attn, bias, HEADS
    )

    grad_kv_ext = grad_kv.reshape(2, ext_rows, pad_cols, width)[:, :, :ext_cols]
    grad_kv_low_ext = grad_kv_low.reshape(2, ext_rows, pad_cols, width)[:, :, :ext_cols]
    grad_kv_own = halo_return(grad_kv_ext, grad_kv_low_ext, height, breadth, radius)

    if fast:
        own_att = columns(attended, dp_index, rows_half)
        att_from_dp = swap(columns(attended, 1 - dp_index, rows_half), "dp")
        att_dp = jnp.concatenate([own_att, att_from_dp], axis=0)
        att_group = jnp.concatenate([att_dp, swap(att_dp, "lon")], axis=0)
    else:
        att_blocks = attended.reshape(token_count, dp_count, rows_half).transpose(1, 0, 2)
        att_dp = exchange_blocks(att_blocks, "dp")
        att_group = gather_members(att_dp, "lon")
        att_group = att_group.transpose(1, 0, 2, 3).reshape(-1, rows_half)

    device_count = dp_count * lat_count * lon_count
    partial = lax.dot_general(
        att_group, cot_group, (((0,), (0,)), ((), ())), preferred_element_type=jnp.float32
    ) * (1.0 / device_count)
    spread = lax.all_to_all(partial.astype(jnp.bfloat16), "lat", 0, 0, tiled=True)
    d_w_out = spread.astype(jnp.float32).reshape(lat_count, rows_block, cols_block).sum(axis=0)

    grad_kv_own = grad_kv_own.astype(jnp.bfloat16).reshape(2, token_count, width)
    grad_proj = jnp.concatenate([grad_query, grad_kv_own[0], grad_kv_own[1]], axis=1)
    d_input = back_project(grad_proj).reshape(1, height, breadth, width)
    return (d_input, d_w_out)


def solution(mesh):
    in_specs = (
        P("dp", "lat", "lon", None),
        P("dp", "lat", "lon", None),
        P(),
        P("dp", None),
        P("dp", None),
    )
    out_specs = (P("dp", "lat", "lon", None), P(("dp", "lat"), "lon"))
    return jax.shard_map(shards, mesh=mesh, in_specs=in_specs, out_specs=out_specs, check_vma=False)
```

```python
import functools

import jax
import jax.numpy as jnp
from jax import lax
from jax.experimental import pallas as pl
from jax.sharding import PartitionSpec as P

HEADS = 16
RADIUS = 6

TRANS_B = (((1,), (1,)), ((), ()))


def passed_along(value, axis, steps):
    count = lax.axis_size(axis)
    pairs = [(source, (source + steps) % count) for source in range(count)]
    return lax.ppermute(value, axis, pairs)


def shifted(value, axis, by):
    count = lax.axis_size(axis)
    pairs = [(i, i + by) for i in range(count) if 0 <= i + by < count]
    return lax.ppermute(value, axis, pairs)


def extended(block, sides, width, periodic):
    for axis, dim in sides:
        count = lax.axis_size(axis)
        forward = [(i, i + 1) for i in range(count - 1)]
        if periodic:
            forward.append((count - 1, 0))
        backward = [(target, source) for source, target in forward]
        low = lax.ppermute(
            lax.slice_in_dim(block, block.shape[dim] - width, None, axis=dim), axis, forward
        )
        high = lax.ppermute(lax.slice_in_dim(block, 0, width, axis=dim), axis, backward)
        block = jnp.concatenate([low, block, high], axis=dim)
    return block


def attention_kernel(q_ref, k_ref, v_ref, g_ref, bias_ref, att_ref, gq_ref, gkv_ref, gkv_low_ref,
                     *, head_dim, scale):
    q = q_ref[...]
    g = g_ref[...]
    k = k_ref[...]
    v = v_ref[...]
    bias = bias_ref[...]
    lanes = q.shape[1]
    lane = lax.broadcasted_iota(jnp.int32, (1, lanes), 1)
    zero = jnp.zeros((), q.dtype)
    sels = [(lane >= j * head_dim) & (lane < (j + 1) * head_dim) for j in range(lanes // head_dim)]
    q_scaled = (q.astype(jnp.float32) * scale).astype(q.dtype)
    g_scaled = (g.astype(jnp.float32) * scale).astype(g.dtype)
    probs_list = []
    grads_list = []
    for sel in sels:
        qj = jnp.where(sel, q_scaled, zero)
        gj = jnp.where(sel, g_scaled, zero)
        masked = lax.dot_general(qj, k, TRANS_B, preferred_element_type=jnp.float32) + bias
        peak = jnp.max(masked, axis=1, keepdims=True)
        weights = jnp.exp(masked - peak)
        probs = weights * (1.0 / jnp.sum(weights, axis=1, keepdims=True))
        grad_probs = lax.dot_general(gj, v, TRANS_B, preferred_element_type=jnp.float32)
        centre = jnp.sum(probs * grad_probs, axis=1, keepdims=True)
        grads_list.append((probs * (grad_probs - centre)).astype(jnp.bfloat16))
        probs_list.append(probs.astype(jnp.bfloat16))
    k_sel = jnp.concatenate([jnp.where(sel, k, zero) for sel in sels], axis=0)
    v_sel = jnp.concatenate([jnp.where(sel, v, zero) for sel in sels], axis=0)
    q_sel = jnp.concatenate([jnp.where(sel, q, zero) for sel in sels], axis=0)
    g_sel = jnp.concatenate([jnp.where(sel, g, zero) for sel in sels], axis=0)
    probs_cat = jnp.concatenate(probs_list, axis=1)
    grads_cat = jnp.concatenate(grads_list, axis=1)
    att = jnp.dot(probs_cat, v_sel, preferred_element_type=jnp.float32)
    gq = jnp.dot(grads_cat, k_sel, preferred_element_type=jnp.float32)
    grads_t = jnp.concatenate(
        [x.astype(jnp.float32).T.astype(jnp.bfloat16) for x in grads_list], axis=1
    )
    probs_t = jnp.concatenate(
        [x.astype(jnp.float32).T.astype(jnp.bfloat16) for x in probs_list], axis=1
    )
    att_ref[...] = att.astype(att_ref.dtype)
    gq_ref[...] = gq.astype(gq_ref.dtype)
    grad_k = jnp.dot(grads_t, q_sel, preferred_element_type=jnp.float32)
    grad_v = jnp.dot(probs_t, g_sel, preferred_element_type=jnp.float32)
    gkv_ref[0] = grad_k
    gkv_ref[1] = grad_v
    gkv_low_ref[0] = grad_k.astype(gkv_low_ref.dtype)
    gkv_low_ref[1] = grad_v.astype(gkv_low_ref.dtype)


def block_attention(query, projected, grad_attn, bias, heads):
    queries, width = query.shape
    keys = projected.shape[0]
    head_dim = width // heads
    lanes = 128
    pairs = width // lanes
    kernel = functools.partial(attention_kernel, head_dim=head_dim, scale=head_dim ** (-0.5))
    flops = 2 * queries * keys * width * 2 * 6
    cost = pl.CostEstimate(
        flops=flops,
        transcendentals=queries * keys * heads,
        bytes_accessed=2 * (2 * queries * width + 2 * keys * width + 2 * queries * width)
        + 4 * queries * keys + 4 * 2 * keys * width,
    )
    return pl.pallas_call(
        kernel,
        grid=(pairs,),
        in_specs=[
            pl.BlockSpec((queries, lanes), lambda h: (0, h)),
            pl.BlockSpec((keys, lanes), lambda h: (0, h + pairs)),
            pl.BlockSpec((keys, lanes), lambda h: (0, h + 2 * pairs)),
            pl.BlockSpec((queries, lanes), lambda h: (0, h)),
            pl.BlockSpec((queries, keys), lambda h: (0, 0)),
        ],
        out_specs=[
            pl.BlockSpec((queries, lanes), lambda h: (0, h)),
            pl.BlockSpec((queries, lanes), lambda h: (0, h)),
            pl.BlockSpec((2, keys, lanes), lambda h: (0, 0, h)),
            pl.BlockSpec((2, keys, lanes), lambda h: (0, 0, h)),
        ],
        out_shape=[
            jax.ShapeDtypeStruct((queries, width), jnp.bfloat16),
            jax.ShapeDtypeStruct((queries, width), jnp.bfloat16),
            jax.ShapeDtypeStruct((2, keys, width), jnp.float32),
            jax.ShapeDtypeStruct((2, keys, width), jnp.bfloat16),
        ],
        cost_estimate=cost,
        name="block_attention",
    )(query, projected, projected, grad_attn, bias)


def grid_pairs(delta_lat, delta_lon):
    lat_count = lax.axis_size("lat")
    lon_count = lax.axis_size("lon")
    pairs = []
    for la in range(lat_count):
        if 0 <= la + delta_lat < lat_count:
            for lo in range(lon_count):
                target = (la + delta_lat) * lon_count + (lo + delta_lon) % lon_count
                pairs.append((la * lon_count + lo, target))
    return pairs


def sent_to(value, delta_lat, delta_lon):
    return lax.ppermute(value, ("lat", "lon"), grid_pairs(delta_lat, delta_lon))


def part(count, radius, step, giving):
    if step == 0:
        return slice(0, count)
    if (step < 0) == giving:
        return slice(count - radius, count)
    return slice(0, radius)


def grouped_send(pieces, axis):
    lon_count = lax.axis_size("lon")
    groups = {}
    for index, (dl, db, value) in enumerate(pieces):
        groups.setdefault((dl, db % lon_count), []).append(index)
    out = [None] * len(pieces)
    for (dl, db), members in groups.items():
        values = [pieces[i][2] for i in members]
        got = sent_to(jnp.concatenate(values, axis=axis), dl, db)
        offset = 0
        for i, value in zip(members, values):
            out[i] = lax.slice_in_dim(got, offset, offset + value.shape[axis], axis=axis)
            offset += value.shape[axis]
    return out


def halo_gather(block, radius):
    height, breadth, lanes = block.shape
    spots = []
    pieces = []
    for da in (-1, 0, 1):
        for db in (-1, 0, 1):
            if da == 0 and db == 0:
                continue
            piece = block[part(height, radius, da, True), part(breadth, radius, db, True)]
            spots.append((da, db))
            pieces.append((-da, -db, piece))
    got = dict(zip(spots, grouped_send(pieces, 1)))
    got[(0, 0)] = block
    rows = [jnp.concatenate([got[(da, db)] for db in (-1, 0, 1)], axis=1) for da in (-1, 0, 1)]
    return jnp.concatenate(rows, axis=0)


def halo_return(ext, ext_low, height, breadth, radius, extra=None):
    row_slices = {-1: slice(0, radius), 0: slice(radius, radius + height), 1: slice(radius + height, None)}
    col_slices = {-1: slice(0, radius), 0: slice(radius, radius + breadth), 1: slice(radius + breadth, None)}
    own = ext[:, row_slices[0], col_slices[0]]
    spots = []
    pieces = []
    for da in (-1, 0, 1):
        for db in (-1, 0, 1):
            if da == 0 and db == 0:
                continue
            spots.append((da, db))
            pieces.append((da, db, ext_low[:, row_slices[da], col_slices[db]]))
    if extra is not None:
        spots.append(None)
        pieces.append((0, 1, extra))
    received = grouped_send(pieces, 2)
    extra_got = received[-1] if extra is not None else None
    for spot, got in zip(spots, received):
        if spot is None:
            continue
        da, db = spot
        rs = part(height, radius, da, True)
        cs = part(breadth, radius, db, True)
        pad_rows = (rs.start, height - rs.stop)
        pad_cols = (cs.start, breadth - cs.stop)
        own = own + jnp.pad(got.astype(jnp.float32), ((0, 0), pad_rows, pad_cols, (0, 0)))
    return own, extra_got


def partner_rows_product(lhs, weights, axis):
    count = lax.axis_size(axis)
    if count != 2:
        full = lax.all_gather(weights, axis, axis=0, tiled=True)
        return lax.dot_general(lhs, full, TRANS_B, preferred_element_type=jnp.float32).astype(
            jnp.bfloat16
        )
    other = lax.ppermute(weights, axis, [(0, 1), (1, 0)])
    mine_part = lax.dot_general(lhs, weights, TRANS_B, preferred_element_type=jnp.float32)
    other_part = lax.dot_general(lhs, other, TRANS_B, preferred_element_type=jnp.float32)
    mine_part = mine_part.astype(jnp.bfloat16)
    other_part = other_part.astype(jnp.bfloat16)
    first = lax.axis_index(axis) == 0
    return jnp.where(
        first,
        jnp.concatenate([mine_part, other_part], axis=1),
        jnp.concatenate([other_part, mine_part], axis=1),
    )


def exchange_blocks(blocks, axis):
    count = lax.axis_size(axis)
    if count == 2:
        me = lax.axis_index(axis)
        mine = lax.dynamic_index_in_dim(blocks, me, 0, keepdims=False)
        theirs = lax.dynamic_index_in_dim(blocks, 1 - me, 0, keepdims=False)
        got = lax.ppermute(theirs, axis, [(0, 1), (1, 0)])
        return jnp.where(me == 0, jnp.stack([mine, got]), jnp.stack([got, mine]))
    flat = blocks.reshape((-1,) + blocks.shape[2:])
    out = lax.all_to_all(flat, axis, 0, 0, tiled=True)
    return out.reshape(blocks.shape)


def gather_members(value, axis):
    count = lax.axis_size(axis)
    if count == 2:
        me = lax.axis_index(axis)
        got = lax.ppermute(value, axis, [(0, 1), (1, 0)])
        return jnp.where(me == 0, jnp.stack([value, got]), jnp.stack([got, value]))
    return lax.all_gather(value, axis, axis=0, tiled=False)


def swap(value, axis):
    return lax.ppermute(value, axis, [(0, 1), (1, 0)])


def columns(value, index, size):
    return lax.dynamic_slice_in_dim(value, index * size, size, axis=1)


def split_rows(joined, shapes):
    out = []
    offset = 0
    for shape in shapes:
        count = 1
        for extent in shape[:-1]:
            count *= extent
        count = count * shape[-1] // joined.shape[-1]
        out.append(joined[offset : offset + count].reshape(shape))
        offset += count
    return out


def join_rows(parts, lanes):
    return jnp.concatenate([p.reshape(-1, lanes) for p in parts], axis=0)


def lat_return(ext_list, height, radius):
    owns = []
    tops = join_rows([ext[:radius] for ext in ext_list], ext_list[0].shape[-1])
    bottoms = join_rows([ext[radius + height :] for ext in ext_list], ext_list[0].shape[-1])
    shapes = [ext[:radius].shape for ext in ext_list]
    from_below = split_rows(shifted(tops.astype(jnp.bfloat16), "lat", -1), shapes)
    from_above = split_rows(shifted(bottoms.astype(jnp.bfloat16), "lat", 1), shapes)
    for ext, below, above in zip(ext_list, from_below, from_above):
        middle = (
            ext[radius : radius + height]
            + jnp.pad(below.astype(jnp.float32), ((height - radius, 0), (0, 0), (0, 0)))
            + jnp.pad(above.astype(jnp.float32), ((0, height - radius), (0, 0), (0, 0)))
        )
        owns.append(middle)
    return owns


def add_lon_rims(mid_list, from_right, from_left, breadth, radius):
    owns = []
    for mid, right, left in zip(mid_list, from_right, from_left):
        owns.append(
            mid[:, radius : radius + breadth]
            + jnp.pad(right.astype(jnp.float32), ((0, 0), (breadth - radius, 0), (0, 0)))
            + jnp.pad(left.astype(jnp.float32), ((0, 0), (0, breadth - radius), (0, 0)))
        )
    return owns


def shards(tokens, cotangent, valid_cells, w_qkv, w_out):
    inputs_here = tokens[0]
    grad_here = cotangent[0]
    height, breadth, width = inputs_here.shape
    radius = RADIUS
    ext_rows = height + 2 * radius
    ext_cols = breadth + 2 * radius
    pad_cols = -(-ext_cols // 8) * 8
    token_count = height * breadth
    key_count = ext_rows * pad_cols
    flat_inputs = inputs_here.reshape(token_count, width)
    flat_grad = grad_here.reshape(token_count, width)
    dp_count = lax.axis_size("dp")
    lat_count = lax.axis_size("lat")
    lon_count = lax.axis_size("lon")
    rows_half = width // dp_count
    cols_block = width // lon_count
    rows_block = rows_half // lat_count
    dp_index = lax.axis_index("dp")
    lon_index = lax.axis_index("lon")
    fast = dp_count == 2 and lon_count == 2

    if fast:
        qkv_other = swap(w_qkv, "dp")
        dp_got = swap(jnp.concatenate([w_out, flat_grad], axis=0), "dp")
        w_out_other = dp_got[: w_out.shape[0]]
        cot_dp = dp_got[w_out.shape[0] :]
        cot_send = jnp.concatenate(
            [columns(flat_grad, 1 - lon_index, cols_block), columns(cot_dp, 1 - lon_index, cols_block)],
            axis=0,
        )
        cot_lon = swap(cot_send, "lon")
        cot_group = jnp.concatenate(
            [
                columns(flat_grad, lon_index, cols_block),
                columns(cot_dp, lon_index, cols_block),
                cot_lon,
            ],
            axis=0,
        )
        mine_part = lax.dot_general(flat_grad, w_out, TRANS_B, preferred_element_type=jnp.float32)
        other_part = lax.dot_general(
            flat_grad, w_out_other, TRANS_B, preferred_element_type=jnp.float32
        )
        mine_part = mine_part.astype(jnp.bfloat16)
        other_part = other_part.astype(jnp.bfloat16)
        grad_attn = jnp.where(
            dp_index == 0,
            jnp.concatenate([mine_part, other_part], axis=1),
            jnp.concatenate([other_part, mine_part], axis=1),
        )

        def project(rows):
            own = jnp.dot(
                columns(rows, dp_index, rows_half), w_qkv, preferred_element_type=jnp.float32
            )
            other = jnp.dot(
                columns(rows, 1 - dp_index, rows_half), qkv_other, preferred_element_type=jnp.float32
            )
            return (own + other).astype(jnp.bfloat16)

        def back_project(grad_proj):
            own = lax.dot_general(grad_proj, w_qkv, TRANS_B, preferred_element_type=jnp.float32)
            other = lax.dot_general(grad_proj, qkv_other, TRANS_B, preferred_element_type=jnp.float32)
            own = own.astype(jnp.bfloat16)
            other = other.astype(jnp.bfloat16)
            return jnp.where(
                dp_index == 0,
                jnp.concatenate([own, other], axis=1),
                jnp.concatenate([other, own], axis=1),
            )
    else:
        panels = lax.all_gather(w_qkv, "dp", axis=0, tiled=True)
        cot_blocks = flat_grad.reshape(token_count, lon_count, cols_block).transpose(1, 0, 2)
        cot_lon = exchange_blocks(cot_blocks, "lon")
        cot_group = gather_members(cot_lon, "dp").reshape(-1, cols_block)
        grad_attn = partner_rows_product(flat_grad, w_out, "dp")


        def project(rows):
            out = jnp.dot(rows, panels, preferred_element_type=jnp.float32)
            return out.astype(jnp.bfloat16)

        def back_project(grad_proj):
            out = lax.dot_general(grad_proj, panels, TRANS_B, preferred_element_type=jnp.float32)
            return out.astype(jnp.bfloat16)

    tok_ext = halo_gather(inputs_here, radius)
    tok_ext = jnp.pad(tok_ext, ((0, 0), (0, pad_cols - ext_cols), (0, 0)))
    tok_ext = tok_ext.reshape(key_count, width)

    projected = project(tok_ext)
    query = projected.reshape(ext_rows, pad_cols, 3 * width)[
        radius : radius + height, radius : radius + breadth, :width
    ].reshape(token_count, width)

    wrapped = jnp.concatenate(
        [valid_cells[:, -radius:], valid_cells, valid_cells[:, :radius]], axis=1
    )
    framed = jnp.pad(wrapped, ((radius, radius), (0, 0)))
    valid_ext = lax.dynamic_slice(
        framed,
        (lax.axis_index("lat") * height, lon_index * breadth),
        (ext_rows, ext_cols),
    )
    valid_ext = jnp.pad(valid_ext, ((0, 0), (0, pad_cols - ext_cols))).reshape(1, key_count)
    query_pos = jnp.arange(token_count)
    key_pos = jnp.arange(key_count)
    delta_row = (key_pos // pad_cols)[None, :] - radius - (query_pos // breadth)[:, None]
    delta_col = (key_pos % pad_cols)[None, :] - radius - (query_pos % breadth)[:, None]
    inside = (jnp.abs(delta_row) <= radius) & (jnp.abs(delta_col) <= radius)
    itself = (delta_row == 0) & (delta_col == 0)
    allowed = inside & ((valid_ext == 1) | itself)
    bias = jnp.where(allowed, 0.0, -jnp.inf).astype(jnp.float32)

    attended, grad_query, grad_kv, grad_kv_low = block_attention(
        query, projected, grad_attn, bias, HEADS
    )

    grad_kv_ext = grad_kv.reshape(2, ext_rows, pad_cols, width)[:, :, :ext_cols]
    grad_kv_low_ext = grad_kv_low.reshape(2, ext_rows, pad_cols, width)[:, :, :ext_cols]

    att_fits = (2 * token_count * rows_half) % (2 * height * width) == 0
    if fast and att_fits:
        own_att = columns(attended, dp_index, rows_half)
        att_from_dp = swap(columns(attended, 1 - dp_index, rows_half), "dp")
        att_dp = jnp.concatenate([own_att, att_from_dp], axis=0)
        carried = att_dp.reshape(2, height, -1, width)
        grad_kv_own, att_lon = halo_return(
            grad_kv_ext, grad_kv_low_ext, height, breadth, radius, carried
        )
        att_group = jnp.concatenate([att_dp, att_lon.reshape(att_dp.shape)], axis=0)
    else:
        grad_kv_own, _ = halo_return(grad_kv_ext, grad_kv_low_ext, height, breadth, radius)
        if fast:
            own_att = columns(attended, dp_index, rows_half)
            att_from_dp = swap(columns(attended, 1 - dp_index, rows_half), "dp")
            att_dp = jnp.concatenate([own_att, att_from_dp], axis=0)
            att_group = jnp.concatenate([att_dp, swap(att_dp, "lon")], axis=0)
        else:
            att_blocks = attended.reshape(token_count, dp_count, rows_half).transpose(1, 0, 2)
            att_dp = exchange_blocks(att_blocks, "dp")
            att_group = gather_members(att_dp, "lon")
            att_group = att_group.transpose(1, 0, 2, 3).reshape(-1, rows_half)

    device_count = dp_count * lat_count * lon_count
    partial = lax.dot_general(
        att_group, cot_group, (((0,), (0,)), ((), ())), preferred_element_type=jnp.float32
    ) * (1.0 / device_count)
    spread = lax.all_to_all(partial.astype(jnp.bfloat16), "lat", 0, 0, tiled=True)
    d_w_out = spread.astype(jnp.float32).reshape(lat_count, rows_block, cols_block).sum(axis=0)

    grad_kv_own = grad_kv_own.astype(jnp.bfloat16).reshape(2, token_count, width)
    grad_proj = jnp.concatenate([grad_query, grad_kv_own[0], grad_kv_own[1]], axis=1)
    d_input = back_project(grad_proj).reshape(1, height, breadth, width)
    return (d_input, d_w_out)


def solution(mesh):
    in_specs = (
        P("dp", "lat", "lon", None),
        P("dp", "lat", "lon", None),
        P(),
        P("dp", None),
        P("dp", None),
    )
    out_specs = (P("dp", "lat", "lon", None), P(("dp", "lat"), "lon"))
    return jax.shard_map(shards, mesh=mesh, in_specs=in_specs, out_specs=out_specs, check_vma=False)
```

```python
import functools

import jax
import jax.numpy as jnp
from jax import lax
from jax.experimental import pallas as pl
from jax.sharding import PartitionSpec as P

HEADS = 16
RADIUS = 6

TRANS_B = (((1,), (1,)), ((), ()))


def passed_along(value, axis, steps):
    count = lax.axis_size(axis)
    pairs = [(source, (source + steps) % count) for source in range(count)]
    return lax.ppermute(value, axis, pairs)


def shifted(value, axis, by):
    count = lax.axis_size(axis)
    pairs = [(i, i + by) for i in range(count) if 0 <= i + by < count]
    return lax.ppermute(value, axis, pairs)


def extended(block, sides, width, periodic):
    for axis, dim in sides:
        count = lax.axis_size(axis)
        forward = [(i, i + 1) for i in range(count - 1)]
        if periodic:
            forward.append((count - 1, 0))
        backward = [(target, source) for source, target in forward]
        low = lax.ppermute(
            lax.slice_in_dim(block, block.shape[dim] - width, None, axis=dim), axis, forward
        )
        high = lax.ppermute(lax.slice_in_dim(block, 0, width, axis=dim), axis, backward)
        block = jnp.concatenate([low, block, high], axis=dim)
    return block


def attention_kernel(q_ref, k_ref, v_ref, g_ref, bias_ref, att_ref, gq_ref, gkv_ref, gkv_low_ref,
                     *, head_dim, scale):
    q = q_ref[...]
    g = g_ref[...]
    k = k_ref[...]
    v = v_ref[...]
    bias = bias_ref[...]
    lanes = q.shape[1]
    lane = lax.broadcasted_iota(jnp.int32, (1, lanes), 1)
    zero = jnp.zeros((), q.dtype)
    sels = [(lane >= j * head_dim) & (lane < (j + 1) * head_dim) for j in range(lanes // head_dim)]
    q_scaled = (q.astype(jnp.float32) * scale).astype(q.dtype)
    g_scaled = (g.astype(jnp.float32) * scale).astype(g.dtype)
    probs_list = []
    grads_list = []
    for sel in sels:
        qj = jnp.where(sel, q_scaled, zero)
        gj = jnp.where(sel, g_scaled, zero)
        masked = lax.dot_general(qj, k, TRANS_B, preferred_element_type=jnp.float32) + bias
        peak = jnp.max(masked, axis=1, keepdims=True)
        weights = jnp.exp(masked - peak)
        probs = weights * (1.0 / jnp.sum(weights, axis=1, keepdims=True))
        grad_probs = lax.dot_general(gj, v, TRANS_B, preferred_element_type=jnp.float32)
        centre = jnp.sum(probs * grad_probs, axis=1, keepdims=True)
        grads_list.append((probs * (grad_probs - centre)).astype(jnp.bfloat16))
        probs_list.append(probs.astype(jnp.bfloat16))
    k_sel = jnp.concatenate([jnp.where(sel, k, zero) for sel in sels], axis=0)
    v_sel = jnp.concatenate([jnp.where(sel, v, zero) for sel in sels], axis=0)
    q_sel = jnp.concatenate([jnp.where(sel, q, zero) for sel in sels], axis=0)
    g_sel = jnp.concatenate([jnp.where(sel, g, zero) for sel in sels], axis=0)
    probs_cat = jnp.concatenate(probs_list, axis=1)
    grads_cat = jnp.concatenate(grads_list, axis=1)
    att = jnp.dot(probs_cat, v_sel, preferred_element_type=jnp.float32)
    gq = jnp.dot(grads_cat, k_sel, preferred_element_type=jnp.float32)
    grads_t = jnp.concatenate(
        [x.astype(jnp.float32).T.astype(jnp.bfloat16) for x in grads_list], axis=1
    )
    probs_t = jnp.concatenate(
        [x.astype(jnp.float32).T.astype(jnp.bfloat16) for x in probs_list], axis=1
    )
    att_ref[...] = att.astype(att_ref.dtype)
    gq_ref[...] = gq.astype(gq_ref.dtype)
    grad_k = jnp.dot(grads_t, q_sel, preferred_element_type=jnp.float32)
    grad_v = jnp.dot(probs_t, g_sel, preferred_element_type=jnp.float32)
    gkv_ref[0] = grad_k
    gkv_ref[1] = grad_v
    gkv_low_ref[0] = grad_k.astype(gkv_low_ref.dtype)
    gkv_low_ref[1] = grad_v.astype(gkv_low_ref.dtype)


def forward_kernel(q_ref, k_ref, v_ref, bias_ref, att_ref, *, head_dim, scale):
    q = q_ref[...]
    k = k_ref[...]
    v = v_ref[...]
    bias = bias_ref[...]
    lanes = q.shape[1]
    lane = lax.broadcasted_iota(jnp.int32, (1, lanes), 1)
    zero = jnp.zeros((), q.dtype)
    sels = [(lane >= j * head_dim) & (lane < (j + 1) * head_dim) for j in range(lanes // head_dim)]
    q_scaled = (q.astype(jnp.float32) * scale).astype(q.dtype)
    probs_list = []
    for sel in sels:
        qj = jnp.where(sel, q_scaled, zero)
        masked = lax.dot_general(qj, k, TRANS_B, preferred_element_type=jnp.float32) + bias
        peak = jnp.max(masked, axis=1, keepdims=True)
        weights = jnp.exp(masked - peak)
        probs = weights * (1.0 / jnp.sum(weights, axis=1, keepdims=True))
        probs_list.append(probs.astype(jnp.bfloat16))
    v_sel = jnp.concatenate([jnp.where(sel, v, zero) for sel in sels], axis=0)
    probs_cat = jnp.concatenate(probs_list, axis=1)
    att = jnp.dot(probs_cat, v_sel, preferred_element_type=jnp.float32)
    att_ref[...] = att.astype(att_ref.dtype)


def block_forward(query, projected, bias, heads):
    queries, width = query.shape
    keys = projected.shape[0]
    head_dim = width // heads
    lanes = 128
    pairs = width // lanes
    kernel = functools.partial(forward_kernel, head_dim=head_dim, scale=head_dim ** (-0.5))
    cost = pl.CostEstimate(
        flops=2 * queries * keys * width * 2 * 2,
        transcendentals=queries * keys * heads,
        bytes_accessed=2 * (2 * queries * width + 2 * keys * width) + 4 * queries * keys,
    )
    return pl.pallas_call(
        kernel,
        grid=(pairs,),
        in_specs=[
            pl.BlockSpec((queries, lanes), lambda h: (0, h)),
            pl.BlockSpec((keys, lanes), lambda h: (0, h + pairs)),
            pl.BlockSpec((keys, lanes), lambda h: (0, h + 2 * pairs)),
            pl.BlockSpec((queries, keys), lambda h: (0, 0)),
        ],
        out_specs=pl.BlockSpec((queries, lanes), lambda h: (0, h)),
        out_shape=jax.ShapeDtypeStruct((queries, width), jnp.bfloat16),
        cost_estimate=cost,
        name="block_forward",
    )(query, projected, projected, bias)


def block_attention(query, projected, grad_attn, bias, heads):
    queries, width = query.shape
    keys = projected.shape[0]
    head_dim = width // heads
    lanes = 128
    pairs = width // lanes
    kernel = functools.partial(attention_kernel, head_dim=head_dim, scale=head_dim ** (-0.5))
    flops = 2 * queries * keys * width * 2 * 6
    cost = pl.CostEstimate(
        flops=flops,
        transcendentals=queries * keys * heads,
        bytes_accessed=2 * (2 * queries * width + 2 * keys * width + 2 * queries * width)
        + 4 * queries * keys + 4 * 2 * keys * width,
    )
    return pl.pallas_call(
        kernel,
        grid=(pairs,),
        in_specs=[
            pl.BlockSpec((queries, lanes), lambda h: (0, h)),
            pl.BlockSpec((keys, lanes), lambda h: (0, h + pairs)),
            pl.BlockSpec((keys, lanes), lambda h: (0, h + 2 * pairs)),
            pl.BlockSpec((queries, lanes), lambda h: (0, h)),
            pl.BlockSpec((queries, keys), lambda h: (0, 0)),
        ],
        out_specs=[
            pl.BlockSpec((queries, lanes), lambda h: (0, h)),
            pl.BlockSpec((queries, lanes), lambda h: (0, h)),
            pl.BlockSpec((2, keys, lanes), lambda h: (0, 0, h)),
            pl.BlockSpec((2, keys, lanes), lambda h: (0, 0, h)),
        ],
        out_shape=[
            jax.ShapeDtypeStruct((queries, width), jnp.bfloat16),
            jax.ShapeDtypeStruct((queries, width), jnp.bfloat16),
            jax.ShapeDtypeStruct((2, keys, width), jnp.float32),
            jax.ShapeDtypeStruct((2, keys, width), jnp.bfloat16),
        ],
        cost_estimate=cost,
        name="block_attention",
    )(query, projected, projected, grad_attn, bias)


def grid_pairs(delta_lat, delta_lon):
    lat_count = lax.axis_size("lat")
    lon_count = lax.axis_size("lon")
    pairs = []
    for la in range(lat_count):
        if 0 <= la + delta_lat < lat_count:
            for lo in range(lon_count):
                target = (la + delta_lat) * lon_count + (lo + delta_lon) % lon_count
                pairs.append((la * lon_count + lo, target))
    return pairs


def sent_to(value, delta_lat, delta_lon):
    return lax.ppermute(value, ("lat", "lon"), grid_pairs(delta_lat, delta_lon))


def part(count, radius, step, giving):
    if step == 0:
        return slice(0, count)
    if (step < 0) == giving:
        return slice(count - radius, count)
    return slice(0, radius)


def grouped_send(pieces, axis):
    lon_count = lax.axis_size("lon")
    groups = {}
    for index, (dl, db, value) in enumerate(pieces):
        groups.setdefault((dl, db % lon_count), []).append(index)
    out = [None] * len(pieces)
    for (dl, db), members in groups.items():
        values = [pieces[i][2] for i in members]
        got = sent_to(jnp.concatenate(values, axis=axis), dl, db)
        offset = 0
        for i, value in zip(members, values):
            out[i] = lax.slice_in_dim(got, offset, offset + value.shape[axis], axis=axis)
            offset += value.shape[axis]
    return out


def halo_gather(block, radius):
    height, breadth, lanes = block.shape
    spots = []
    pieces = []
    for da in (-1, 0, 1):
        for db in (-1, 0, 1):
            if da == 0 and db == 0:
                continue
            piece = block[part(height, radius, da, True), part(breadth, radius, db, True)]
            spots.append((da, db))
            pieces.append((-da, -db, piece))
    got = dict(zip(spots, grouped_send(pieces, 1)))
    got[(0, 0)] = block
    rows = [jnp.concatenate([got[(da, db)] for db in (-1, 0, 1)], axis=1) for da in (-1, 0, 1)]
    return jnp.concatenate(rows, axis=0)


def halo_return(ext, ext_low, height, breadth, radius, extra=None):
    row_slices = {-1: slice(0, radius), 0: slice(radius, radius + height), 1: slice(radius + height, None)}
    col_slices = {-1: slice(0, radius), 0: slice(radius, radius + breadth), 1: slice(radius + breadth, None)}
    own = ext[:, row_slices[0], col_slices[0]]
    spots = []
    pieces = []
    for da in (-1, 0, 1):
        for db in (-1, 0, 1):
            if da == 0 and db == 0:
                continue
            spots.append((da, db))
            pieces.append((da, db, ext_low[:, row_slices[da], col_slices[db]]))
    if extra is not None:
        spots.append(None)
        pieces.append((0, 1, extra))
    received = grouped_send(pieces, 2)
    extra_got = received[-1] if extra is not None else None
    for spot, got in zip(spots, received):
        if spot is None:
            continue
        da, db = spot
        rs = part(height, radius, da, True)
        cs = part(breadth, radius, db, True)
        pad_rows = (rs.start, height - rs.stop)
        pad_cols = (cs.start, breadth - cs.stop)
        own = own + jnp.pad(got.astype(jnp.float32), ((0, 0), pad_rows, pad_cols, (0, 0)))
    return own, extra_got


def partner_rows_product(lhs, weights, axis):
    count = lax.axis_size(axis)
    if count != 2:
        full = lax.all_gather(weights, axis, axis=0, tiled=True)
        return lax.dot_general(lhs, full, TRANS_B, preferred_element_type=jnp.float32).astype(
            jnp.bfloat16
        )
    other = lax.ppermute(weights, axis, [(0, 1), (1, 0)])
    mine_part = lax.dot_general(lhs, weights, TRANS_B, preferred_element_type=jnp.float32)
    other_part = lax.dot_general(lhs, other, TRANS_B, preferred_element_type=jnp.float32)
    mine_part = mine_part.astype(jnp.bfloat16)
    other_part = other_part.astype(jnp.bfloat16)
    first = lax.axis_index(axis) == 0
    return jnp.where(
        first,
        jnp.concatenate([mine_part, other_part], axis=1),
        jnp.concatenate([other_part, mine_part], axis=1),
    )


def exchange_blocks(blocks, axis):
    count = lax.axis_size(axis)
    if count == 2:
        me = lax.axis_index(axis)
        mine = lax.dynamic_index_in_dim(blocks, me, 0, keepdims=False)
        theirs = lax.dynamic_index_in_dim(blocks, 1 - me, 0, keepdims=False)
        got = lax.ppermute(theirs, axis, [(0, 1), (1, 0)])
        return jnp.where(me == 0, jnp.stack([mine, got]), jnp.stack([got, mine]))
    flat = blocks.reshape((-1,) + blocks.shape[2:])
    out = lax.all_to_all(flat, axis, 0, 0, tiled=True)
    return out.reshape(blocks.shape)


def gather_members(value, axis):
    count = lax.axis_size(axis)
    if count == 2:
        me = lax.axis_index(axis)
        got = lax.ppermute(value, axis, [(0, 1), (1, 0)])
        return jnp.where(me == 0, jnp.stack([value, got]), jnp.stack([got, value]))
    return lax.all_gather(value, axis, axis=0, tiled=False)


def swap(value, axis):
    return lax.ppermute(value, axis, [(0, 1), (1, 0)])


def columns(value, index, size):
    return lax.dynamic_slice_in_dim(value, index * size, size, axis=1)


def split_rows(joined, shapes):
    out = []
    offset = 0
    for shape in shapes:
        count = 1
        for extent in shape[:-1]:
            count *= extent
        count = count * shape[-1] // joined.shape[-1]
        out.append(joined[offset : offset + count].reshape(shape))
        offset += count
    return out


def join_rows(parts, lanes):
    return jnp.concatenate([p.reshape(-1, lanes) for p in parts], axis=0)


def lat_return(ext_list, height, radius):
    owns = []
    tops = join_rows([ext[:radius] for ext in ext_list], ext_list[0].shape[-1])
    bottoms = join_rows([ext[radius + height :] for ext in ext_list], ext_list[0].shape[-1])
    shapes = [ext[:radius].shape for ext in ext_list]
    from_below = split_rows(shifted(tops.astype(jnp.bfloat16), "lat", -1), shapes)
    from_above = split_rows(shifted(bottoms.astype(jnp.bfloat16), "lat", 1), shapes)
    for ext, below, above in zip(ext_list, from_below, from_above):
        middle = (
            ext[radius : radius + height]
            + jnp.pad(below.astype(jnp.float32), ((height - radius, 0), (0, 0), (0, 0)))
            + jnp.pad(above.astype(jnp.float32), ((0, height - radius), (0, 0), (0, 0)))
        )
        owns.append(middle)
    return owns


def add_lon_rims(mid_list, from_right, from_left, breadth, radius):
    owns = []
    for mid, right, left in zip(mid_list, from_right, from_left):
        owns.append(
            mid[:, radius : radius + breadth]
            + jnp.pad(right.astype(jnp.float32), ((0, 0), (breadth - radius, 0), (0, 0)))
            + jnp.pad(left.astype(jnp.float32), ((0, 0), (0, breadth - radius), (0, 0)))
        )
    return owns


def shards(tokens, cotangent, valid_cells, w_qkv, w_out):
    inputs_here = tokens[0]
    grad_here = cotangent[0]
    height, breadth, width = inputs_here.shape
    radius = RADIUS
    ext_rows = height + 2 * radius
    ext_cols = breadth + 2 * radius
    pad_cols = -(-ext_cols // 8) * 8
    token_count = height * breadth
    key_count = ext_rows * pad_cols
    flat_inputs = inputs_here.reshape(token_count, width)
    flat_grad = grad_here.reshape(token_count, width)
    dp_count = lax.axis_size("dp")
    lat_count = lax.axis_size("lat")
    lon_count = lax.axis_size("lon")
    rows_half = width // dp_count
    cols_block = width // lon_count
    rows_block = rows_half // lat_count
    dp_index = lax.axis_index("dp")
    lon_index = lax.axis_index("lon")
    fast = dp_count == 2 and lon_count == 2

    if fast:
        qkv_other = swap(w_qkv, "dp")
        dp_got = swap(jnp.concatenate([w_out, flat_grad], axis=0), "dp")
        w_out_other = dp_got[: w_out.shape[0]]
        cot_dp = dp_got[w_out.shape[0] :]
        cot_send = jnp.concatenate(
            [columns(flat_grad, 1 - lon_index, cols_block), columns(cot_dp, 1 - lon_index, cols_block)],
            axis=0,
        )
        cot_lon = swap(cot_send, "lon")
        cot_group = jnp.concatenate(
            [
                columns(flat_grad, lon_index, cols_block),
                columns(cot_dp, lon_index, cols_block),
                cot_lon,
            ],
            axis=0,
        )
        mine_part = lax.dot_general(flat_grad, w_out, TRANS_B, preferred_element_type=jnp.float32)
        other_part = lax.dot_general(
            flat_grad, w_out_other, TRANS_B, preferred_element_type=jnp.float32
        )
        mine_part = mine_part.astype(jnp.bfloat16)
        other_part = other_part.astype(jnp.bfloat16)
        grad_attn = jnp.where(
            dp_index == 0,
            jnp.concatenate([mine_part, other_part], axis=1),
            jnp.concatenate([other_part, mine_part], axis=1),
        )

        def project(rows):
            own = jnp.dot(
                columns(rows, dp_index, rows_half), w_qkv, preferred_element_type=jnp.float32
            )
            other = jnp.dot(
                columns(rows, 1 - dp_index, rows_half), qkv_other, preferred_element_type=jnp.float32
            )
            return (own + other).astype(jnp.bfloat16)

        def back_project(grad_proj):
            own = lax.dot_general(grad_proj, w_qkv, TRANS_B, preferred_element_type=jnp.float32)
            other = lax.dot_general(grad_proj, qkv_other, TRANS_B, preferred_element_type=jnp.float32)
            own = own.astype(jnp.bfloat16)
            other = other.astype(jnp.bfloat16)
            return jnp.where(
                dp_index == 0,
                jnp.concatenate([own, other], axis=1),
                jnp.concatenate([other, own], axis=1),
            )
    else:
        panels = lax.all_gather(w_qkv, "dp", axis=0, tiled=True)
        cot_blocks = flat_grad.reshape(token_count, lon_count, cols_block).transpose(1, 0, 2)
        cot_lon = exchange_blocks(cot_blocks, "lon")
        cot_group = gather_members(cot_lon, "dp").reshape(-1, cols_block)
        grad_attn = partner_rows_product(flat_grad, w_out, "dp")


        def project(rows):
            out = jnp.dot(rows, panels, preferred_element_type=jnp.float32)
            return out.astype(jnp.bfloat16)

        def back_project(grad_proj):
            out = lax.dot_general(grad_proj, panels, TRANS_B, preferred_element_type=jnp.float32)
            return out.astype(jnp.bfloat16)

    tok_ext = halo_gather(inputs_here, radius)
    tok_ext = jnp.pad(tok_ext, ((0, 0), (0, pad_cols - ext_cols), (0, 0)))
    tok_ext = tok_ext.reshape(key_count, width)

    projected = project(tok_ext)
    query = projected.reshape(ext_rows, pad_cols, 3 * width)[
        radius : radius + height, radius : radius + breadth, :width
    ].reshape(token_count, width)

    wrapped = jnp.concatenate(
        [valid_cells[:, -radius:], valid_cells, valid_cells[:, :radius]], axis=1
    )
    framed = jnp.pad(wrapped, ((radius, radius), (0, 0)))
    valid_ext = lax.dynamic_slice(
        framed,
        (lax.axis_index("lat") * height, lon_index * breadth),
        (ext_rows, ext_cols),
    )
    valid_ext = jnp.pad(valid_ext, ((0, 0), (0, pad_cols - ext_cols))).reshape(1, key_count)
    query_pos = jnp.arange(token_count)
    key_pos = jnp.arange(key_count)
    delta_row = (key_pos // pad_cols)[None, :] - radius - (query_pos // breadth)[:, None]
    delta_col = (key_pos % pad_cols)[None, :] - radius - (query_pos % breadth)[:, None]
    inside = (jnp.abs(delta_row) <= radius) & (jnp.abs(delta_col) <= radius)
    itself = (delta_row == 0) & (delta_col == 0)
    allowed = inside & ((valid_ext == 1) | itself)
    bias = jnp.where(allowed, 0.0, -jnp.inf).astype(jnp.float32)

    attended = block_forward(query, projected, bias, HEADS)
    if fast:
        own_att = columns(attended, dp_index, rows_half)
        att_from_dp = swap(columns(attended, 1 - dp_index, rows_half), "dp")
        att_dp = jnp.concatenate([own_att, att_from_dp], axis=0)
        att_group = jnp.concatenate([att_dp, swap(att_dp, "lon")], axis=0)
    else:
        att_blocks = attended.reshape(token_count, dp_count, rows_half).transpose(1, 0, 2)
        att_dp = exchange_blocks(att_blocks, "dp")
        att_group = gather_members(att_dp, "lon")
        att_group = att_group.transpose(1, 0, 2, 3).reshape(-1, rows_half)

    device_count = dp_count * lat_count * lon_count
    partial = lax.dot_general(
        att_group, cot_group, (((0,), (0,)), ((), ())), preferred_element_type=jnp.float32
    ) * (1.0 / device_count)
    spread = lax.all_to_all(partial.astype(jnp.bfloat16), "lat", 0, 0, tiled=True)
    spread, query_after = lax.optimization_barrier((spread, query))

    _, grad_query, grad_kv, grad_kv_low = block_attention(
        query_after, projected, grad_attn, bias, HEADS
    )
    grad_kv_ext = grad_kv.reshape(2, ext_rows, pad_cols, width)[:, :, :ext_cols]
    grad_kv_low_ext = grad_kv_low.reshape(2, ext_rows, pad_cols, width)[:, :, :ext_cols]
    grad_kv_own, _ = halo_return(grad_kv_ext, grad_kv_low_ext, height, breadth, radius)

    d_w_out = spread.astype(jnp.float32).reshape(lat_count, rows_block, cols_block).sum(axis=0)

    grad_kv_own = grad_kv_own.astype(jnp.bfloat16).reshape(2, token_count, width)
    grad_proj = jnp.concatenate([grad_query, grad_kv_own[0], grad_kv_own[1]], axis=1)
    d_input = back_project(grad_proj).reshape(1, height, breadth, width)
    return (d_input, d_w_out)


def solution(mesh):
    in_specs = (
        P("dp", "lat", "lon", None),
        P("dp", "lat", "lon", None),
        P(),
        P("dp", None),
        P("dp", None),
    )
    out_specs = (P("dp", "lat", "lon", None), P(("dp", "lat"), "lon"))
    return jax.shard_map(shards, mesh=mesh, in_specs=in_specs, out_specs=out_specs, check_vma=False)
```

```python
import functools

import jax
import jax.numpy as jnp
from jax import lax
from jax.experimental import pallas as pl
from jax.sharding import PartitionSpec as P

HEADS = 16
RADIUS = 6

TRANS_B = (((1,), (1,)), ((), ()))


def passed_along(value, axis, steps):
    count = lax.axis_size(axis)
    pairs = [(source, (source + steps) % count) for source in range(count)]
    return lax.ppermute(value, axis, pairs)


def shifted(value, axis, by):
    count = lax.axis_size(axis)
    pairs = [(i, i + by) for i in range(count) if 0 <= i + by < count]
    return lax.ppermute(value, axis, pairs)


def extended(block, sides, width, periodic):
    for axis, dim in sides:
        count = lax.axis_size(axis)
        forward = [(i, i + 1) for i in range(count - 1)]
        if periodic:
            forward.append((count - 1, 0))
        backward = [(target, source) for source, target in forward]
        low = lax.ppermute(
            lax.slice_in_dim(block, block.shape[dim] - width, None, axis=dim), axis, forward
        )
        high = lax.ppermute(lax.slice_in_dim(block, 0, width, axis=dim), axis, backward)
        block = jnp.concatenate([low, block, high], axis=dim)
    return block


def attention_kernel(q_ref, k_ref, v_ref, g_ref, bias_ref, att_ref, gq_ref, gkv_ref, gkv_low_ref,
                     *, head_dim, scale):
    q = q_ref[...]
    g = g_ref[...]
    k = k_ref[...]
    v = v_ref[...]
    bias = bias_ref[...]
    lanes = q.shape[1]
    lane = lax.broadcasted_iota(jnp.int32, (1, lanes), 1)
    zero = jnp.zeros((), q.dtype)
    sels = [(lane >= j * head_dim) & (lane < (j + 1) * head_dim) for j in range(lanes // head_dim)]
    q_scaled = (q.astype(jnp.float32) * scale).astype(q.dtype)
    g_scaled = (g.astype(jnp.float32) * scale).astype(g.dtype)
    probs_list = []
    grads_list = []
    for sel in sels:
        qj = jnp.where(sel, q_scaled, zero)
        gj = jnp.where(sel, g_scaled, zero)
        masked = lax.dot_general(qj, k, TRANS_B, preferred_element_type=jnp.float32) + bias
        peak = jnp.max(masked, axis=1, keepdims=True)
        weights = jnp.exp(masked - peak)
        probs = weights * (1.0 / jnp.sum(weights, axis=1, keepdims=True))
        grad_probs = lax.dot_general(gj, v, TRANS_B, preferred_element_type=jnp.float32)
        centre = jnp.sum(probs * grad_probs, axis=1, keepdims=True)
        grads_list.append((probs * (grad_probs - centre)).astype(jnp.bfloat16))
        probs_list.append(probs.astype(jnp.bfloat16))
    k_sel = jnp.concatenate([jnp.where(sel, k, zero) for sel in sels], axis=0)
    v_sel = jnp.concatenate([jnp.where(sel, v, zero) for sel in sels], axis=0)
    q_sel = jnp.concatenate([jnp.where(sel, q, zero) for sel in sels], axis=0)
    g_sel = jnp.concatenate([jnp.where(sel, g, zero) for sel in sels], axis=0)
    probs_cat = jnp.concatenate(probs_list, axis=1)
    grads_cat = jnp.concatenate(grads_list, axis=1)
    att = jnp.dot(probs_cat, v_sel, preferred_element_type=jnp.float32)
    gq = jnp.dot(grads_cat, k_sel, preferred_element_type=jnp.float32)
    grads_t = jnp.concatenate(
        [x.astype(jnp.float32).T.astype(jnp.bfloat16) for x in grads_list], axis=1
    )
    probs_t = jnp.concatenate(
        [x.astype(jnp.float32).T.astype(jnp.bfloat16) for x in probs_list], axis=1
    )
    att_ref[...] = att.astype(att_ref.dtype)
    gq_ref[...] = gq.astype(gq_ref.dtype)
    grad_k = jnp.dot(grads_t, q_sel, preferred_element_type=jnp.float32)
    grad_v = jnp.dot(probs_t, g_sel, preferred_element_type=jnp.float32)
    gkv_ref[0] = grad_k
    gkv_ref[1] = grad_v
    gkv_low_ref[0] = grad_k.astype(gkv_low_ref.dtype)
    gkv_low_ref[1] = grad_v.astype(gkv_low_ref.dtype)


def block_attention(query, projected, grad_attn, bias, heads):
    queries, width = query.shape
    keys = projected.shape[0]
    head_dim = width // heads
    lanes = 128
    pairs = width // lanes
    kernel = functools.partial(attention_kernel, head_dim=head_dim, scale=head_dim ** (-0.5))
    flops = 2 * queries * keys * width * 2 * 6
    cost = pl.CostEstimate(
        flops=flops,
        transcendentals=queries * keys * heads,
        bytes_accessed=2 * (2 * queries * width + 2 * keys * width + 2 * queries * width)
        + 4 * queries * keys + 4 * 2 * keys * width,
    )
    return pl.pallas_call(
        kernel,
        grid=(pairs,),
        in_specs=[
            pl.BlockSpec((queries, lanes), lambda h: (0, h)),
            pl.BlockSpec((keys, lanes), lambda h: (0, h + pairs)),
            pl.BlockSpec((keys, lanes), lambda h: (0, h + 2 * pairs)),
            pl.BlockSpec((queries, lanes), lambda h: (0, h)),
            pl.BlockSpec((queries, keys), lambda h: (0, 0)),
        ],
        out_specs=[
            pl.BlockSpec((queries, lanes), lambda h: (0, h)),
            pl.BlockSpec((queries, lanes), lambda h: (0, h)),
            pl.BlockSpec((2, keys, lanes), lambda h: (0, 0, h)),
            pl.BlockSpec((2, keys, lanes), lambda h: (0, 0, h)),
        ],
        out_shape=[
            jax.ShapeDtypeStruct((queries, width), jnp.bfloat16),
            jax.ShapeDtypeStruct((queries, width), jnp.bfloat16),
            jax.ShapeDtypeStruct((2, keys, width), jnp.float32),
            jax.ShapeDtypeStruct((2, keys, width), jnp.bfloat16),
        ],
        cost_estimate=cost,
        name="block_attention",
    )(query, projected, projected, grad_attn, bias)


def grid_pairs(delta_lat, delta_lon):
    lat_count = lax.axis_size("lat")
    lon_count = lax.axis_size("lon")
    pairs = []
    for la in range(lat_count):
        if 0 <= la + delta_lat < lat_count:
            for lo in range(lon_count):
                target = (la + delta_lat) * lon_count + (lo + delta_lon) % lon_count
                pairs.append((la * lon_count + lo, target))
    return pairs


def sent_to(value, delta_lat, delta_lon):
    return lax.ppermute(value, ("lat", "lon"), grid_pairs(delta_lat, delta_lon))


def part(count, radius, step, giving):
    if step == 0:
        return slice(0, count)
    if (step < 0) == giving:
        return slice(count - radius, count)
    return slice(0, radius)


def grouped_send(pieces, axis):
    lon_count = lax.axis_size("lon")
    groups = {}
    for index, (dl, db, value) in enumerate(pieces):
        groups.setdefault((dl, db % lon_count), []).append(index)
    out = [None] * len(pieces)
    for (dl, db), members in groups.items():
        values = [pieces[i][2] for i in members]
        got = sent_to(jnp.concatenate(values, axis=axis), dl, db)
        offset = 0
        for i, value in zip(members, values):
            out[i] = lax.slice_in_dim(got, offset, offset + value.shape[axis], axis=axis)
            offset += value.shape[axis]
    return out


def halo_gather(block, radius):
    height, breadth, lanes = block.shape
    spots = []
    pieces = []
    for da in (-1, 0, 1):
        for db in (-1, 0, 1):
            if da == 0 and db == 0:
                continue
            piece = block[part(height, radius, da, True), part(breadth, radius, db, True)]
            spots.append((da, db))
            pieces.append((-da, -db, piece))
    got = dict(zip(spots, grouped_send(pieces, 1)))
    got[(0, 0)] = block
    rows = [jnp.concatenate([got[(da, db)] for db in (-1, 0, 1)], axis=1) for da in (-1, 0, 1)]
    return jnp.concatenate(rows, axis=0)


def halo_return(ext, ext_low, height, breadth, radius, extra=None):
    row_slices = {-1: slice(0, radius), 0: slice(radius, radius + height), 1: slice(radius + height, None)}
    col_slices = {-1: slice(0, radius), 0: slice(radius, radius + breadth), 1: slice(radius + breadth, None)}
    own = ext[:, row_slices[0], col_slices[0]]
    spots = []
    pieces = []
    for da in (-1, 0, 1):
        for db in (-1, 0, 1):
            if da == 0 and db == 0:
                continue
            spots.append((da, db))
            pieces.append((da, db, ext_low[:, row_slices[da], col_slices[db]]))
    if extra is not None:
        spots.append(None)
        pieces.append((0, 1, extra))
    received = grouped_send(pieces, 2)
    extra_got = received[-1] if extra is not None else None
    for spot, got in zip(spots, received):
        if spot is None:
            continue
        da, db = spot
        rs = part(height, radius, da, True)
        cs = part(breadth, radius, db, True)
        pad_rows = (rs.start, height - rs.stop)
        pad_cols = (cs.start, breadth - cs.stop)
        own = own + jnp.pad(got.astype(jnp.float32), ((0, 0), pad_rows, pad_cols, (0, 0)))
    return own, extra_got


def partner_rows_product(lhs, weights, axis):
    count = lax.axis_size(axis)
    if count != 2:
        full = lax.all_gather(weights, axis, axis=0, tiled=True)
        return lax.dot_general(lhs, full, TRANS_B, preferred_element_type=jnp.float32).astype(
            jnp.bfloat16
        )
    other = lax.ppermute(weights, axis, [(0, 1), (1, 0)])
    mine_part = lax.dot_general(lhs, weights, TRANS_B, preferred_element_type=jnp.float32)
    other_part = lax.dot_general(lhs, other, TRANS_B, preferred_element_type=jnp.float32)
    mine_part = mine_part.astype(jnp.bfloat16)
    other_part = other_part.astype(jnp.bfloat16)
    first = lax.axis_index(axis) == 0
    return jnp.where(
        first,
        jnp.concatenate([mine_part, other_part], axis=1),
        jnp.concatenate([other_part, mine_part], axis=1),
    )


def exchange_blocks(blocks, axis):
    count = lax.axis_size(axis)
    if count == 2:
        me = lax.axis_index(axis)
        mine = lax.dynamic_index_in_dim(blocks, me, 0, keepdims=False)
        theirs = lax.dynamic_index_in_dim(blocks, 1 - me, 0, keepdims=False)
        got = lax.ppermute(theirs, axis, [(0, 1), (1, 0)])
        return jnp.where(me == 0, jnp.stack([mine, got]), jnp.stack([got, mine]))
    flat = blocks.reshape((-1,) + blocks.shape[2:])
    out = lax.all_to_all(flat, axis, 0, 0, tiled=True)
    return out.reshape(blocks.shape)


def gather_members(value, axis):
    count = lax.axis_size(axis)
    if count == 2:
        me = lax.axis_index(axis)
        got = lax.ppermute(value, axis, [(0, 1), (1, 0)])
        return jnp.where(me == 0, jnp.stack([value, got]), jnp.stack([got, value]))
    return lax.all_gather(value, axis, axis=0, tiled=False)


def swap(value, axis):
    return lax.ppermute(value, axis, [(0, 1), (1, 0)])


def columns(value, index, size):
    return lax.dynamic_slice_in_dim(value, index * size, size, axis=1)


def split_rows(joined, shapes):
    out = []
    offset = 0
    for shape in shapes:
        count = 1
        for extent in shape[:-1]:
            count *= extent
        count = count * shape[-1] // joined.shape[-1]
        out.append(joined[offset : offset + count].reshape(shape))
        offset += count
    return out


def join_rows(parts, lanes):
    return jnp.concatenate([p.reshape(-1, lanes) for p in parts], axis=0)


def lat_return(ext_list, height, radius):
    owns = []
    tops = join_rows([ext[:radius] for ext in ext_list], ext_list[0].shape[-1])
    bottoms = join_rows([ext[radius + height :] for ext in ext_list], ext_list[0].shape[-1])
    shapes = [ext[:radius].shape for ext in ext_list]
    from_below = split_rows(shifted(tops.astype(jnp.bfloat16), "lat", -1), shapes)
    from_above = split_rows(shifted(bottoms.astype(jnp.bfloat16), "lat", 1), shapes)
    for ext, below, above in zip(ext_list, from_below, from_above):
        middle = (
            ext[radius : radius + height]
            + jnp.pad(below.astype(jnp.float32), ((height - radius, 0), (0, 0), (0, 0)))
            + jnp.pad(above.astype(jnp.float32), ((0, height - radius), (0, 0), (0, 0)))
        )
        owns.append(middle)
    return owns


def add_lon_rims(mid_list, from_right, from_left, breadth, radius):
    owns = []
    for mid, right, left in zip(mid_list, from_right, from_left):
        owns.append(
            mid[:, radius : radius + breadth]
            + jnp.pad(right.astype(jnp.float32), ((0, 0), (breadth - radius, 0), (0, 0)))
            + jnp.pad(left.astype(jnp.float32), ((0, 0), (0, breadth - radius), (0, 0)))
        )
    return owns


def shards(tokens, cotangent, valid_cells, w_qkv, w_out):
    inputs_here = tokens[0]
    grad_here = cotangent[0]
    height, breadth, width = inputs_here.shape
    radius = RADIUS
    ext_rows = height + 2 * radius
    ext_cols = breadth + 2 * radius
    pad_cols = -(-ext_cols // 8) * 8
    token_count = height * breadth
    key_count = ext_rows * pad_cols
    flat_inputs = inputs_here.reshape(token_count, width)
    flat_grad = grad_here.reshape(token_count, width)
    dp_count = lax.axis_size("dp")
    lat_count = lax.axis_size("lat")
    lon_count = lax.axis_size("lon")
    rows_half = width // dp_count
    cols_block = width // lon_count
    rows_block = rows_half // lat_count
    dp_index = lax.axis_index("dp")
    lon_index = lax.axis_index("lon")
    fast = dp_count == 2 and lon_count == 2

    if fast:
        qkv_other = swap(w_qkv, "dp")
        dp_got = swap(jnp.concatenate([w_out, flat_grad], axis=0), "dp")
        w_out_other = dp_got[: w_out.shape[0]]
        cot_dp = dp_got[w_out.shape[0] :]
        cot_send = jnp.concatenate(
            [columns(flat_grad, 1 - lon_index, cols_block), columns(cot_dp, 1 - lon_index, cols_block)],
            axis=0,
        )
        cot_later = cot_send
        cot_group = jnp.concatenate(
            [
                columns(flat_grad, lon_index, cols_block),
                columns(cot_dp, lon_index, cols_block),
            ],
            axis=0,
        )
        mine_part = lax.dot_general(flat_grad, w_out, TRANS_B, preferred_element_type=jnp.float32)
        other_part = lax.dot_general(
            flat_grad, w_out_other, TRANS_B, preferred_element_type=jnp.float32
        )
        mine_part = mine_part.astype(jnp.bfloat16)
        other_part = other_part.astype(jnp.bfloat16)
        grad_attn = jnp.where(
            dp_index == 0,
            jnp.concatenate([mine_part, other_part], axis=1),
            jnp.concatenate([other_part, mine_part], axis=1),
        )

        def project(rows):
            own = jnp.dot(
                columns(rows, dp_index, rows_half), w_qkv, preferred_element_type=jnp.float32
            )
            other = jnp.dot(
                columns(rows, 1 - dp_index, rows_half), qkv_other, preferred_element_type=jnp.float32
            )
            return (own + other).astype(jnp.bfloat16)

        def back_project(grad_proj):
            own = lax.dot_general(grad_proj, w_qkv, TRANS_B, preferred_element_type=jnp.float32)
            other = lax.dot_general(grad_proj, qkv_other, TRANS_B, preferred_element_type=jnp.float32)
            own = own.astype(jnp.bfloat16)
            other = other.astype(jnp.bfloat16)
            return jnp.where(
                dp_index == 0,
                jnp.concatenate([own, other], axis=1),
                jnp.concatenate([other, own], axis=1),
            )
    else:
        panels = lax.all_gather(w_qkv, "dp", axis=0, tiled=True)
        cot_blocks = flat_grad.reshape(token_count, lon_count, cols_block).transpose(1, 0, 2)
        cot_lon = exchange_blocks(cot_blocks, "lon")
        cot_group = gather_members(cot_lon, "dp").reshape(-1, cols_block)
        grad_attn = partner_rows_product(flat_grad, w_out, "dp")


        def project(rows):
            out = jnp.dot(rows, panels, preferred_element_type=jnp.float32)
            return out.astype(jnp.bfloat16)

        def back_project(grad_proj):
            out = lax.dot_general(grad_proj, panels, TRANS_B, preferred_element_type=jnp.float32)
            return out.astype(jnp.bfloat16)

    tok_ext = halo_gather(inputs_here, radius)
    tok_ext = jnp.pad(tok_ext, ((0, 0), (0, pad_cols - ext_cols), (0, 0)))
    tok_ext = tok_ext.reshape(key_count, width)

    projected = project(tok_ext)
    query = projected.reshape(ext_rows, pad_cols, 3 * width)[
        radius : radius + height, radius : radius + breadth, :width
    ].reshape(token_count, width)

    wrapped = jnp.concatenate(
        [valid_cells[:, -radius:], valid_cells, valid_cells[:, :radius]], axis=1
    )
    framed = jnp.pad(wrapped, ((radius, radius), (0, 0)))
    valid_ext = lax.dynamic_slice(
        framed,
        (lax.axis_index("lat") * height, lon_index * breadth),
        (ext_rows, ext_cols),
    )
    valid_ext = jnp.pad(valid_ext, ((0, 0), (0, pad_cols - ext_cols))).reshape(1, key_count)
    query_pos = jnp.arange(token_count)
    key_pos = jnp.arange(key_count)
    delta_row = (key_pos // pad_cols)[None, :] - radius - (query_pos // breadth)[:, None]
    delta_col = (key_pos % pad_cols)[None, :] - radius - (query_pos % breadth)[:, None]
    inside = (jnp.abs(delta_row) <= radius) & (jnp.abs(delta_col) <= radius)
    itself = (delta_row == 0) & (delta_col == 0)
    allowed = inside & ((valid_ext == 1) | itself)
    bias = jnp.where(allowed, 0.0, -jnp.inf).astype(jnp.float32)

    attended, grad_query, grad_kv, grad_kv_low = block_attention(
        query, projected, grad_attn, bias, HEADS
    )

    grad_kv_ext = grad_kv.reshape(2, ext_rows, pad_cols, width)[:, :, :ext_cols]
    grad_kv_low_ext = grad_kv_low.reshape(2, ext_rows, pad_cols, width)[:, :, :ext_cols]

    att_fits = (2 * token_count * rows_half) % (2 * height * width) == 0
    if fast and att_fits:
        own_att = columns(attended, dp_index, rows_half)
        att_from_dp = swap(columns(attended, 1 - dp_index, rows_half), "dp")
        att_dp = jnp.concatenate([own_att, att_from_dp], axis=0)
        carried = att_dp.reshape(2, height, -1, width)
        grad_kv_own, att_lon = halo_return(
            grad_kv_ext, grad_kv_low_ext, height, breadth, radius, carried
        )
        att_group = jnp.concatenate([att_dp, att_lon.reshape(att_dp.shape)], axis=0)
    else:
        grad_kv_own, _ = halo_return(grad_kv_ext, grad_kv_low_ext, height, breadth, radius)
        if fast:
            own_att = columns(attended, dp_index, rows_half)
            att_from_dp = swap(columns(attended, 1 - dp_index, rows_half), "dp")
            att_dp = jnp.concatenate([own_att, att_from_dp], axis=0)
            att_group = jnp.concatenate([att_dp, swap(att_dp, "lon")], axis=0)
        else:
            att_blocks = attended.reshape(token_count, dp_count, rows_half).transpose(1, 0, 2)
            att_dp = exchange_blocks(att_blocks, "dp")
            att_group = gather_members(att_dp, "lon")
            att_group = att_group.transpose(1, 0, 2, 3).reshape(-1, rows_half)

    if fast:
        cot_later, _ = lax.optimization_barrier((cot_later, attended))
        cot_group = jnp.concatenate([cot_group, swap(cot_later, "lon")], axis=0)

    device_count = dp_count * lat_count * lon_count
    partial = lax.dot_general(
        att_group, cot_group, (((0,), (0,)), ((), ())), preferred_element_type=jnp.float32
    ) * (1.0 / device_count)
    spread = lax.all_to_all(partial.astype(jnp.bfloat16), "lat", 0, 0, tiled=True)
    d_w_out = spread.astype(jnp.float32).reshape(lat_count, rows_block, cols_block).sum(axis=0)

    grad_kv_own = grad_kv_own.astype(jnp.bfloat16).reshape(2, token_count, width)
    grad_proj = jnp.concatenate([grad_query, grad_kv_own[0], grad_kv_own[1]], axis=1)
    d_input = back_project(grad_proj).reshape(1, height, breadth, width)
    return (d_input, d_w_out)


def solution(mesh):
    in_specs = (
        P("dp", "lat", "lon", None),
        P("dp", "lat", "lon", None),
        P(),
        P("dp", None),
        P("dp", None),
    )
    out_specs = (P("dp", "lat", "lon", None), P(("dp", "lat"), "lon"))
    return jax.shard_map(shards, mesh=mesh, in_specs=in_specs, out_specs=out_specs, check_vma=False)
```

```python
import functools

import jax
import jax.numpy as jnp
from jax import lax
from jax.experimental import pallas as pl
from jax.sharding import PartitionSpec as P

HEADS = 16
RADIUS = 6

TRANS_B = (((1,), (1,)), ((), ()))


def passed_along(value, axis, steps):
    count = lax.axis_size(axis)
    pairs = [(source, (source + steps) % count) for source in range(count)]
    return lax.ppermute(value, axis, pairs)


def shifted(value, axis, by):
    count = lax.axis_size(axis)
    pairs = [(i, i + by) for i in range(count) if 0 <= i + by < count]
    return lax.ppermute(value, axis, pairs)


def extended(block, sides, width, periodic):
    for axis, dim in sides:
        count = lax.axis_size(axis)
        forward = [(i, i + 1) for i in range(count - 1)]
        if periodic:
            forward.append((count - 1, 0))
        backward = [(target, source) for source, target in forward]
        low = lax.ppermute(
            lax.slice_in_dim(block, block.shape[dim] - width, None, axis=dim), axis, forward
        )
        high = lax.ppermute(lax.slice_in_dim(block, 0, width, axis=dim), axis, backward)
        block = jnp.concatenate([low, block, high], axis=dim)
    return block


def attention_kernel(q_ref, k_ref, v_ref, g_ref, bias_ref, att_ref, gq_ref, gkv_ref, gkv_low_ref,
                     *, head_dim, scale):
    q = q_ref[...]
    g = g_ref[...]
    k = k_ref[...]
    v = v_ref[...]
    bias = bias_ref[...]
    lanes = q.shape[1]
    lane = lax.broadcasted_iota(jnp.int32, (1, lanes), 1)
    zero = jnp.zeros((), q.dtype)
    sels = [(lane >= j * head_dim) & (lane < (j + 1) * head_dim) for j in range(lanes // head_dim)]
    q_scaled = (q.astype(jnp.float32) * scale).astype(q.dtype)
    g_scaled = (g.astype(jnp.float32) * scale).astype(g.dtype)
    probs_list = []
    grads_list = []
    for sel in sels:
        qj = jnp.where(sel, q_scaled, zero)
        gj = jnp.where(sel, g_scaled, zero)
        masked = lax.dot_general(qj, k, TRANS_B, preferred_element_type=jnp.float32) + bias
        peak = jnp.max(masked, axis=1, keepdims=True)
        weights = jnp.exp(masked - peak)
        probs = weights * (1.0 / jnp.sum(weights, axis=1, keepdims=True))
        grad_probs = lax.dot_general(gj, v, TRANS_B, preferred_element_type=jnp.float32)
        centre = jnp.sum(probs * grad_probs, axis=1, keepdims=True)
        grads_list.append((probs * (grad_probs - centre)).astype(jnp.bfloat16))
        probs_list.append(probs.astype(jnp.bfloat16))
    k_sel = jnp.concatenate([jnp.where(sel, k, zero) for sel in sels], axis=0)
    v_sel = jnp.concatenate([jnp.where(sel, v, zero) for sel in sels], axis=0)
    q_sel = jnp.concatenate([jnp.where(sel, q, zero) for sel in sels], axis=0)
    g_sel = jnp.concatenate([jnp.where(sel, g, zero) for sel in sels], axis=0)
    probs_cat = jnp.concatenate(probs_list, axis=1)
    grads_cat = jnp.concatenate(grads_list, axis=1)
    att = jnp.dot(probs_cat, v_sel, preferred_element_type=jnp.float32)
    gq = jnp.dot(grads_cat, k_sel, preferred_element_type=jnp.float32)
    grads_t = jnp.concatenate(
        [x.astype(jnp.float32).T.astype(jnp.bfloat16) for x in grads_list], axis=1
    )
    probs_t = jnp.concatenate(
        [x.astype(jnp.float32).T.astype(jnp.bfloat16) for x in probs_list], axis=1
    )
    att_ref[...] = att.astype(att_ref.dtype)
    gq_ref[...] = gq.astype(gq_ref.dtype)
    grad_k = jnp.dot(grads_t, q_sel, preferred_element_type=jnp.float32)
    grad_v = jnp.dot(probs_t, g_sel, preferred_element_type=jnp.float32)
    gkv_ref[0] = grad_k
    gkv_ref[1] = grad_v
    gkv_low_ref[0] = grad_k.astype(gkv_low_ref.dtype)
    gkv_low_ref[1] = grad_v.astype(gkv_low_ref.dtype)


def block_attention(query, projected, grad_attn, bias, heads):
    queries, width = query.shape
    keys = projected.shape[0]
    head_dim = width // heads
    lanes = 128
    pairs = width // lanes
    kernel = functools.partial(attention_kernel, head_dim=head_dim, scale=head_dim ** (-0.5))
    flops = 2 * queries * keys * width * 2 * 6
    cost = pl.CostEstimate(
        flops=flops,
        transcendentals=queries * keys * heads,
        bytes_accessed=2 * (2 * queries * width + 2 * keys * width + 2 * queries * width)
        + 4 * queries * keys + 4 * 2 * keys * width,
    )
    return pl.pallas_call(
        kernel,
        grid=(pairs,),
        in_specs=[
            pl.BlockSpec((queries, lanes), lambda h: (0, h)),
            pl.BlockSpec((keys, lanes), lambda h: (0, h + pairs)),
            pl.BlockSpec((keys, lanes), lambda h: (0, h + 2 * pairs)),
            pl.BlockSpec((queries, lanes), lambda h: (0, h)),
            pl.BlockSpec((queries, keys), lambda h: (0, 0)),
        ],
        out_specs=[
            pl.BlockSpec((queries, lanes), lambda h: (0, h)),
            pl.BlockSpec((queries, lanes), lambda h: (0, h)),
            pl.BlockSpec((2, keys, lanes), lambda h: (0, 0, h)),
            pl.BlockSpec((2, keys, lanes), lambda h: (0, 0, h)),
        ],
        out_shape=[
            jax.ShapeDtypeStruct((queries, width), jnp.bfloat16),
            jax.ShapeDtypeStruct((queries, width), jnp.bfloat16),
            jax.ShapeDtypeStruct((2, keys, width), jnp.float32),
            jax.ShapeDtypeStruct((2, keys, width), jnp.bfloat16),
        ],
        cost_estimate=cost,
        name="block_attention",
    )(query, projected, projected, grad_attn, bias)


def grid_pairs(delta_lat, delta_lon):
    lat_count = lax.axis_size("lat")
    lon_count = lax.axis_size("lon")
    pairs = []
    for la in range(lat_count):
        if 0 <= la + delta_lat < lat_count:
            for lo in range(lon_count):
                target = (la + delta_lat) * lon_count + (lo + delta_lon) % lon_count
                pairs.append((la * lon_count + lo, target))
    return pairs


def sent_to(value, delta_lat, delta_lon):
    return lax.ppermute(value, ("lat", "lon"), grid_pairs(delta_lat, delta_lon))


def part(count, radius, step, giving):
    if step == 0:
        return slice(0, count)
    if (step < 0) == giving:
        return slice(count - radius, count)
    return slice(0, radius)


def grouped_send(pieces, axis):
    lon_count = lax.axis_size("lon")
    groups = {}
    for index, (dl, db, value) in enumerate(pieces):
        groups.setdefault((dl, db % lon_count), []).append(index)
    out = [None] * len(pieces)
    for (dl, db), members in groups.items():
        values = [pieces[i][2] for i in members]
        got = sent_to(jnp.concatenate(values, axis=axis), dl, db)
        offset = 0
        for i, value in zip(members, values):
            out[i] = lax.slice_in_dim(got, offset, offset + value.shape[axis], axis=axis)
            offset += value.shape[axis]
    return out


def halo_gather(block, radius):
    height, breadth, lanes = block.shape
    spots = []
    pieces = []
    for da in (-1, 0, 1):
        for db in (-1, 0, 1):
            if da == 0 and db == 0:
                continue
            piece = block[part(height, radius, da, True), part(breadth, radius, db, True)]
            spots.append((da, db))
            pieces.append((-da, -db, piece))
    got = dict(zip(spots, grouped_send(pieces, 1)))
    got[(0, 0)] = block
    rows = [jnp.concatenate([got[(da, db)] for db in (-1, 0, 1)], axis=1) for da in (-1, 0, 1)]
    return jnp.concatenate(rows, axis=0)


def halo_return(ext, ext_low, height, breadth, radius, extra=None):
    row_slices = {-1: slice(0, radius), 0: slice(radius, radius + height), 1: slice(radius + height, None)}
    col_slices = {-1: slice(0, radius), 0: slice(radius, radius + breadth), 1: slice(radius + breadth, None)}
    own = ext[:, row_slices[0], col_slices[0]]
    spots = []
    pieces = []
    for da in (-1, 0, 1):
        for db in (-1, 0, 1):
            if da == 0 and db == 0:
                continue
            spots.append((da, db))
            pieces.append((da, db, ext_low[:, row_slices[da], col_slices[db]]))
    if extra is not None:
        spots.append(None)
        pieces.append((0, 1, extra))
    received = grouped_send(pieces, 2)
    extra_got = received[-1] if extra is not None else None
    for spot, got in zip(spots, received):
        if spot is None:
            continue
        da, db = spot
        rs = part(height, radius, da, True)
        cs = part(breadth, radius, db, True)
        pad_rows = (rs.start, height - rs.stop)
        pad_cols = (cs.start, breadth - cs.stop)
        own = own + jnp.pad(got.astype(jnp.float32), ((0, 0), pad_rows, pad_cols, (0, 0)))
    return own, extra_got


def partner_rows_product(lhs, weights, axis):
    count = lax.axis_size(axis)
    if count != 2:
        full = lax.all_gather(weights, axis, axis=0, tiled=True)
        return lax.dot_general(lhs, full, TRANS_B, preferred_element_type=jnp.float32).astype(
            jnp.bfloat16
        )
    other = lax.ppermute(weights, axis, [(0, 1), (1, 0)])
    mine_part = lax.dot_general(lhs, weights, TRANS_B, preferred_element_type=jnp.float32)
    other_part = lax.dot_general(lhs, other, TRANS_B, preferred_element_type=jnp.float32)
    mine_part = mine_part.astype(jnp.bfloat16)
    other_part = other_part.astype(jnp.bfloat16)
    first = lax.axis_index(axis) == 0
    return jnp.where(
        first,
        jnp.concatenate([mine_part, other_part], axis=1),
        jnp.concatenate([other_part, mine_part], axis=1),
    )


def exchange_blocks(blocks, axis):
    count = lax.axis_size(axis)
    if count == 2:
        me = lax.axis_index(axis)
        mine = lax.dynamic_index_in_dim(blocks, me, 0, keepdims=False)
        theirs = lax.dynamic_index_in_dim(blocks, 1 - me, 0, keepdims=False)
        got = lax.ppermute(theirs, axis, [(0, 1), (1, 0)])
        return jnp.where(me == 0, jnp.stack([mine, got]), jnp.stack([got, mine]))
    flat = blocks.reshape((-1,) + blocks.shape[2:])
    out = lax.all_to_all(flat, axis, 0, 0, tiled=True)
    return out.reshape(blocks.shape)


def gather_members(value, axis):
    count = lax.axis_size(axis)
    if count == 2:
        me = lax.axis_index(axis)
        got = lax.ppermute(value, axis, [(0, 1), (1, 0)])
        return jnp.where(me == 0, jnp.stack([value, got]), jnp.stack([got, value]))
    return lax.all_gather(value, axis, axis=0, tiled=False)


def swap(value, axis):
    return lax.ppermute(value, axis, [(0, 1), (1, 0)])


def columns(value, index, size):
    return lax.dynamic_slice_in_dim(value, index * size, size, axis=1)


def split_rows(joined, shapes):
    out = []
    offset = 0
    for shape in shapes:
        count = 1
        for extent in shape[:-1]:
            count *= extent
        count = count * shape[-1] // joined.shape[-1]
        out.append(joined[offset : offset + count].reshape(shape))
        offset += count
    return out


def join_rows(parts, lanes):
    return jnp.concatenate([p.reshape(-1, lanes) for p in parts], axis=0)


def lat_return(ext_list, height, radius):
    owns = []
    tops = join_rows([ext[:radius] for ext in ext_list], ext_list[0].shape[-1])
    bottoms = join_rows([ext[radius + height :] for ext in ext_list], ext_list[0].shape[-1])
    shapes = [ext[:radius].shape for ext in ext_list]
    from_below = split_rows(shifted(tops.astype(jnp.bfloat16), "lat", -1), shapes)
    from_above = split_rows(shifted(bottoms.astype(jnp.bfloat16), "lat", 1), shapes)
    for ext, below, above in zip(ext_list, from_below, from_above):
        middle = (
            ext[radius : radius + height]
            + jnp.pad(below.astype(jnp.float32), ((height - radius, 0), (0, 0), (0, 0)))
            + jnp.pad(above.astype(jnp.float32), ((0, height - radius), (0, 0), (0, 0)))
        )
        owns.append(middle)
    return owns


def add_lon_rims(mid_list, from_right, from_left, breadth, radius):
    owns = []
    for mid, right, left in zip(mid_list, from_right, from_left):
        owns.append(
            mid[:, radius : radius + breadth]
            + jnp.pad(right.astype(jnp.float32), ((0, 0), (breadth - radius, 0), (0, 0)))
            + jnp.pad(left.astype(jnp.float32), ((0, 0), (0, breadth - radius), (0, 0)))
        )
    return owns


def shards(tokens, cotangent, valid_cells, w_qkv, w_out):
    inputs_here = tokens[0]
    grad_here = cotangent[0]
    height, breadth, width = inputs_here.shape
    radius = RADIUS
    ext_rows = height + 2 * radius
    ext_cols = breadth + 2 * radius
    pad_cols = -(-ext_cols // 8) * 8
    token_count = height * breadth
    key_count = ext_rows * pad_cols
    flat_inputs = inputs_here.reshape(token_count, width)
    flat_grad = grad_here.reshape(token_count, width)
    dp_count = lax.axis_size("dp")
    lat_count = lax.axis_size("lat")
    lon_count = lax.axis_size("lon")
    rows_half = width // dp_count
    cols_block = width // lon_count
    rows_block = rows_half // lat_count
    dp_index = lax.axis_index("dp")
    lon_index = lax.axis_index("lon")
    fast = dp_count == 2 and lon_count == 2

    if fast:
        qkv_other = swap(w_qkv, "dp")
        dp_got = swap(jnp.concatenate([w_out, flat_grad], axis=0), "dp")
        w_out_other = dp_got[: w_out.shape[0]]
        cot_dp = dp_got[w_out.shape[0] :]
        cot_send = jnp.concatenate(
            [columns(flat_grad, 1 - lon_index, cols_block), columns(cot_dp, 1 - lon_index, cols_block)],
            axis=0,
        )
        cot_lon = swap(cot_send, "lon")
        cot_group = jnp.concatenate(
            [
                columns(flat_grad, lon_index, cols_block),
                columns(cot_dp, lon_index, cols_block),
                cot_lon,
            ],
            axis=0,
        )
        mine_part = lax.dot_general(flat_grad, w_out, TRANS_B, preferred_element_type=jnp.float32)
        other_part = lax.dot_general(
            flat_grad, w_out_other, TRANS_B, preferred_element_type=jnp.float32
        )
        mine_part = mine_part.astype(jnp.bfloat16)
        other_part = other_part.astype(jnp.bfloat16)
        grad_attn = jnp.where(
            dp_index == 0,
            jnp.concatenate([mine_part, other_part], axis=1),
            jnp.concatenate([other_part, mine_part], axis=1),
        )

        rows_first = jnp.concatenate([w_qkv, qkv_other], axis=0)

        def project(rows):
            ordered = jnp.concatenate(
                [columns(rows, dp_index, rows_half), columns(rows, 1 - dp_index, rows_half)], axis=1
            )
            out = jnp.dot(ordered, rows_first, preferred_element_type=jnp.float32)
            return out.astype(jnp.bfloat16)

        def back_project(grad_proj):
            out = lax.dot_general(grad_proj, rows_first, TRANS_B, preferred_element_type=jnp.float32)
            out = out.astype(jnp.bfloat16)
            swapped = jnp.concatenate([out[:, rows_half:], out[:, :rows_half]], axis=1)
            return jnp.where(dp_index == 0, out, swapped)
    else:
        panels = lax.all_gather(w_qkv, "dp", axis=0, tiled=True)
        cot_blocks = flat_grad.reshape(token_count, lon_count, cols_block).transpose(1, 0, 2)
        cot_lon = exchange_blocks(cot_blocks, "lon")
        cot_group = gather_members(cot_lon, "dp").reshape(-1, cols_block)
        grad_attn = partner_rows_product(flat_grad, w_out, "dp")


        def project(rows):
            out = jnp.dot(rows, panels, preferred_element_type=jnp.float32)
            return out.astype(jnp.bfloat16)

        def back_project(grad_proj):
            out = lax.dot_general(grad_proj, panels, TRANS_B, preferred_element_type=jnp.float32)
            return out.astype(jnp.bfloat16)

    tok_ext = halo_gather(inputs_here, radius)
    tok_ext = jnp.pad(tok_ext, ((0, 0), (0, pad_cols - ext_cols), (0, 0)))
    tok_ext = tok_ext.reshape(key_count, width)

    projected = project(tok_ext)
    query = projected.reshape(ext_rows, pad_cols, 3 * width)[
        radius : radius + height, radius : radius + breadth, :width
    ].reshape(token_count, width)

    wrapped = jnp.concatenate(
        [valid_cells[:, -radius:], valid_cells, valid_cells[:, :radius]], axis=1
    )
    framed = jnp.pad(wrapped, ((radius, radius), (0, 0)))
    valid_ext = lax.dynamic_slice(
        framed,
        (lax.axis_index("lat") * height, lon_index * breadth),
        (ext_rows, ext_cols),
    )
    valid_ext = jnp.pad(valid_ext, ((0, 0), (0, pad_cols - ext_cols))).reshape(1, key_count)
    query_pos = jnp.arange(token_count)
    key_pos = jnp.arange(key_count)
    delta_row = (key_pos // pad_cols)[None, :] - radius - (query_pos // breadth)[:, None]
    delta_col = (key_pos % pad_cols)[None, :] - radius - (query_pos % breadth)[:, None]
    inside = (jnp.abs(delta_row) <= radius) & (jnp.abs(delta_col) <= radius)
    itself = (delta_row == 0) & (delta_col == 0)
    allowed = inside & ((valid_ext == 1) | itself)
    bias = jnp.where(allowed, 0.0, -jnp.inf).astype(jnp.float32)

    attended, grad_query, grad_kv, grad_kv_low = block_attention(
        query, projected, grad_attn, bias, HEADS
    )

    grad_kv_ext = grad_kv.reshape(2, ext_rows, pad_cols, width)[:, :, :ext_cols]
    grad_kv_low_ext = grad_kv_low.reshape(2, ext_rows, pad_cols, width)[:, :, :ext_cols]

    att_fits = (2 * token_count * rows_half) % (2 * height * width) == 0
    if fast and att_fits:
        own_att = columns(attended, dp_index, rows_half)
        att_from_dp = swap(columns(attended, 1 - dp_index, rows_half), "dp")
        att_dp = jnp.concatenate([own_att, att_from_dp], axis=0)
        carried = att_dp.reshape(2, height, -1, width)
        grad_kv_own, att_lon = halo_return(
            grad_kv_ext, grad_kv_low_ext, height, breadth, radius, carried
        )
        att_group = jnp.concatenate([att_dp, att_lon.reshape(att_dp.shape)], axis=0)
    else:
        grad_kv_own, _ = halo_return(grad_kv_ext, grad_kv_low_ext, height, breadth, radius)
        if fast:
            own_att = columns(attended, dp_index, rows_half)
            att_from_dp = swap(columns(attended, 1 - dp_index, rows_half), "dp")
            att_dp = jnp.concatenate([own_att, att_from_dp], axis=0)
            att_group = jnp.concatenate([att_dp, swap(att_dp, "lon")], axis=0)
        else:
            att_blocks = attended.reshape(token_count, dp_count, rows_half).transpose(1, 0, 2)
            att_dp = exchange_blocks(att_blocks, "dp")
            att_group = gather_members(att_dp, "lon")
            att_group = att_group.transpose(1, 0, 2, 3).reshape(-1, rows_half)

    device_count = dp_count * lat_count * lon_count
    partial = lax.dot_general(
        att_group, cot_group, (((0,), (0,)), ((), ())), preferred_element_type=jnp.float32
    ) * (1.0 / device_count)
    spread = lax.all_to_all(partial.astype(jnp.bfloat16), "lat", 0, 0, tiled=True)
    d_w_out = spread.astype(jnp.float32).reshape(lat_count, rows_block, cols_block).sum(axis=0)

    grad_kv_own = grad_kv_own.astype(jnp.bfloat16).reshape(2, token_count, width)
    grad_proj = jnp.concatenate([grad_query, grad_kv_own[0], grad_kv_own[1]], axis=1)
    d_input = back_project(grad_proj).reshape(1, height, breadth, width)
    return (d_input, d_w_out)


def solution(mesh):
    in_specs = (
        P("dp", "lat", "lon", None),
        P("dp", "lat", "lon", None),
        P(),
        P("dp", None),
        P("dp", None),
    )
    out_specs = (P("dp", "lat", "lon", None), P(("dp", "lat"), "lon"))
    return jax.shard_map(shards, mesh=mesh, in_specs=in_specs, out_specs=out_specs, check_vma=False)
```

```python
import functools

import jax
import jax.numpy as jnp
from jax import lax
from jax.experimental import pallas as pl
from jax.experimental.pallas import tpu as pltpu
from jax.sharding import PartitionSpec as P

HEADS = 16
RADIUS = 6

TRANS_B = (((1,), (1,)), ((), ()))


def passed_along(value, axis, steps):
    count = lax.axis_size(axis)
    pairs = [(source, (source + steps) % count) for source in range(count)]
    return lax.ppermute(value, axis, pairs)


def shifted(value, axis, by):
    count = lax.axis_size(axis)
    pairs = [(i, i + by) for i in range(count) if 0 <= i + by < count]
    return lax.ppermute(value, axis, pairs)


def extended(block, sides, width, periodic):
    for axis, dim in sides:
        count = lax.axis_size(axis)
        forward = [(i, i + 1) for i in range(count - 1)]
        if periodic:
            forward.append((count - 1, 0))
        backward = [(target, source) for source, target in forward]
        low = lax.ppermute(
            lax.slice_in_dim(block, block.shape[dim] - width, None, axis=dim), axis, forward
        )
        high = lax.ppermute(lax.slice_in_dim(block, 0, width, axis=dim), axis, backward)
        block = jnp.concatenate([low, block, high], axis=dim)
    return block


def attention_kernel(q_ref, proj_ref, g_ref, bias_ref, att_ref, gq_ref, gkv_ref, gkv_low_ref,
                     *, head_dim, scale):
    q = q_ref[...]
    g = g_ref[...]
    lanes = q.shape[1]
    width = proj_ref.shape[1] // 3
    pair = pl.program_id(0)
    k = proj_ref[:, pl.ds(pl.multiple_of(width + pair * lanes, lanes), lanes)]
    v = proj_ref[:, pl.ds(pl.multiple_of(2 * width + pair * lanes, lanes), lanes)]
    bias = bias_ref[...]
    lane = lax.broadcasted_iota(jnp.int32, (1, lanes), 1)
    zero = jnp.zeros((), q.dtype)
    sels = [(lane >= j * head_dim) & (lane < (j + 1) * head_dim) for j in range(lanes // head_dim)]
    q_scaled = (q.astype(jnp.float32) * scale).astype(q.dtype)
    g_scaled = (g.astype(jnp.float32) * scale).astype(g.dtype)
    probs_list = []
    grads_list = []
    for sel in sels:
        qj = jnp.where(sel, q_scaled, zero)
        gj = jnp.where(sel, g_scaled, zero)
        masked = lax.dot_general(qj, k, TRANS_B, preferred_element_type=jnp.float32) + bias
        peak = jnp.max(masked, axis=1, keepdims=True)
        weights = jnp.exp(masked - peak)
        probs = weights * (1.0 / jnp.sum(weights, axis=1, keepdims=True))
        grad_probs = lax.dot_general(gj, v, TRANS_B, preferred_element_type=jnp.float32)
        centre = jnp.sum(probs * grad_probs, axis=1, keepdims=True)
        grads_list.append((probs * (grad_probs - centre)).astype(jnp.bfloat16))
        probs_list.append(probs.astype(jnp.bfloat16))
    k_sel = jnp.concatenate([jnp.where(sel, k, zero) for sel in sels], axis=0)
    v_sel = jnp.concatenate([jnp.where(sel, v, zero) for sel in sels], axis=0)
    q_sel = jnp.concatenate([jnp.where(sel, q, zero) for sel in sels], axis=0)
    g_sel = jnp.concatenate([jnp.where(sel, g, zero) for sel in sels], axis=0)
    probs_cat = jnp.concatenate(probs_list, axis=1)
    grads_cat = jnp.concatenate(grads_list, axis=1)
    att = jnp.dot(probs_cat, v_sel, preferred_element_type=jnp.float32)
    gq = jnp.dot(grads_cat, k_sel, preferred_element_type=jnp.float32)
    grads_t = jnp.concatenate(
        [x.astype(jnp.float32).T.astype(jnp.bfloat16) for x in grads_list], axis=1
    )
    probs_t = jnp.concatenate(
        [x.astype(jnp.float32).T.astype(jnp.bfloat16) for x in probs_list], axis=1
    )
    att_ref[...] = att.astype(att_ref.dtype)
    gq_ref[...] = gq.astype(gq_ref.dtype)
    grad_k = jnp.dot(grads_t, q_sel, preferred_element_type=jnp.float32)
    grad_v = jnp.dot(probs_t, g_sel, preferred_element_type=jnp.float32)
    gkv_ref[0] = grad_k
    gkv_ref[1] = grad_v
    gkv_low_ref[0] = grad_k.astype(gkv_low_ref.dtype)
    gkv_low_ref[1] = grad_v.astype(gkv_low_ref.dtype)


def block_attention(query, projected, grad_attn, bias, heads):
    queries, width = query.shape
    keys = projected.shape[0]
    head_dim = width // heads
    lanes = 128
    pairs = width // lanes
    kernel = functools.partial(attention_kernel, head_dim=head_dim, scale=head_dim ** (-0.5))
    flops = 2 * queries * keys * width * 2 * 6
    cost = pl.CostEstimate(
        flops=flops,
        transcendentals=queries * keys * heads,
        bytes_accessed=2 * (2 * queries * width + 2 * keys * width + 2 * queries * width)
        + 4 * queries * keys + 4 * 2 * keys * width,
    )
    return pl.pallas_call(
        kernel,
        grid=(pairs,),
        in_specs=[
            pl.BlockSpec((queries, lanes), lambda h: (0, h)),
            pl.BlockSpec(memory_space=pltpu.VMEM),
            pl.BlockSpec((queries, lanes), lambda h: (0, h)),
            pl.BlockSpec((queries, keys), lambda h: (0, 0)),
        ],
        out_specs=[
            pl.BlockSpec((queries, lanes), lambda h: (0, h)),
            pl.BlockSpec((queries, lanes), lambda h: (0, h)),
            pl.BlockSpec((2, keys, lanes), lambda h: (0, 0, h)),
            pl.BlockSpec((2, keys, lanes), lambda h: (0, 0, h)),
        ],
        out_shape=[
            jax.ShapeDtypeStruct((queries, width), jnp.bfloat16),
            jax.ShapeDtypeStruct((queries, width), jnp.bfloat16),
            jax.ShapeDtypeStruct((2, keys, width), jnp.float32),
            jax.ShapeDtypeStruct((2, keys, width), jnp.bfloat16),
        ],
        cost_estimate=cost,
        name="block_attention",
    )(query, projected, grad_attn, bias)


def grid_pairs(delta_lat, delta_lon):
    lat_count = lax.axis_size("lat")
    lon_count = lax.axis_size("lon")
    pairs = []
    for la in range(lat_count):
        if 0 <= la + delta_lat < lat_count:
            for lo in range(lon_count):
                target = (la + delta_lat) * lon_count + (lo + delta_lon) % lon_count
                pairs.append((la * lon_count + lo, target))
    return pairs


def sent_to(value, delta_lat, delta_lon):
    return lax.ppermute(value, ("lat", "lon"), grid_pairs(delta_lat, delta_lon))


def part(count, radius, step, giving):
    if step == 0:
        return slice(0, count)
    if (step < 0) == giving:
        return slice(count - radius, count)
    return slice(0, radius)


def grouped_send(pieces, axis):
    lon_count = lax.axis_size("lon")
    groups = {}
    for index, (dl, db, value) in enumerate(pieces):
        groups.setdefault((dl, db % lon_count), []).append(index)
    out = [None] * len(pieces)
    for (dl, db), members in groups.items():
        values = [pieces[i][2] for i in members]
        got = sent_to(jnp.concatenate(values, axis=axis), dl, db)
        offset = 0
        for i, value in zip(members, values):
            out[i] = lax.slice_in_dim(got, offset, offset + value.shape[axis], axis=axis)
            offset += value.shape[axis]
    return out


def halo_gather(block, radius):
    height, breadth, lanes = block.shape
    spots = []
    pieces = []
    for da in (-1, 0, 1):
        for db in (-1, 0, 1):
            if da == 0 and db == 0:
                continue
            piece = block[part(height, radius, da, True), part(breadth, radius, db, True)]
            spots.append((da, db))
            pieces.append((-da, -db, piece))
    got = dict(zip(spots, grouped_send(pieces, 1)))
    got[(0, 0)] = block
    rows = [jnp.concatenate([got[(da, db)] for db in (-1, 0, 1)], axis=1) for da in (-1, 0, 1)]
    return jnp.concatenate(rows, axis=0)


def halo_return(ext, ext_low, height, breadth, radius, extra=None):
    row_slices = {-1: slice(0, radius), 0: slice(radius, radius + height), 1: slice(radius + height, None)}
    col_slices = {-1: slice(0, radius), 0: slice(radius, radius + breadth), 1: slice(radius + breadth, None)}
    own = ext[:, row_slices[0], col_slices[0]]
    spots = []
    pieces = []
    for da in (-1, 0, 1):
        for db in (-1, 0, 1):
            if da == 0 and db == 0:
                continue
            spots.append((da, db))
            pieces.append((da, db, ext_low[:, row_slices[da], col_slices[db]]))
    if extra is not None:
        spots.append(None)
        pieces.append((0, 1, extra))
    received = grouped_send(pieces, 2)
    extra_got = received[-1] if extra is not None else None
    for spot, got in zip(spots, received):
        if spot is None:
            continue
        da, db = spot
        rs = part(height, radius, da, True)
        cs = part(breadth, radius, db, True)
        pad_rows = (rs.start, height - rs.stop)
        pad_cols = (cs.start, breadth - cs.stop)
        own = own + jnp.pad(got.astype(jnp.float32), ((0, 0), pad_rows, pad_cols, (0, 0)))
    return own, extra_got


def partner_rows_product(lhs, weights, axis):
    count = lax.axis_size(axis)
    if count != 2:
        full = lax.all_gather(weights, axis, axis=0, tiled=True)
        return lax.dot_general(lhs, full, TRANS_B, preferred_element_type=jnp.float32).astype(
            jnp.bfloat16
        )
    other = lax.ppermute(weights, axis, [(0, 1), (1, 0)])
    mine_part = lax.dot_general(lhs, weights, TRANS_B, preferred_element_type=jnp.float32)
    other_part = lax.dot_general(lhs, other, TRANS_B, preferred_element_type=jnp.float32)
    mine_part = mine_part.astype(jnp.bfloat16)
    other_part = other_part.astype(jnp.bfloat16)
    first = lax.axis_index(axis) == 0
    return jnp.where(
        first,
        jnp.concatenate([mine_part, other_part], axis=1),
        jnp.concatenate([other_part, mine_part], axis=1),
    )


def exchange_blocks(blocks, axis):
    count = lax.axis_size(axis)
    if count == 2:
        me = lax.axis_index(axis)
        mine = lax.dynamic_index_in_dim(blocks, me, 0, keepdims=False)
        theirs = lax.dynamic_index_in_dim(blocks, 1 - me, 0, keepdims=False)
        got = lax.ppermute(theirs, axis, [(0, 1), (1, 0)])
        return jnp.where(me == 0, jnp.stack([mine, got]), jnp.stack([got, mine]))
    flat = blocks.reshape((-1,) + blocks.shape[2:])
    out = lax.all_to_all(flat, axis, 0, 0, tiled=True)
    return out.reshape(blocks.shape)


def gather_members(value, axis):
    count = lax.axis_size(axis)
    if count == 2:
        me = lax.axis_index(axis)
        got = lax.ppermute(value, axis, [(0, 1), (1, 0)])
        return jnp.where(me == 0, jnp.stack([value, got]), jnp.stack([got, value]))
    return lax.all_gather(value, axis, axis=0, tiled=False)


def swap(value, axis):
    return lax.ppermute(value, axis, [(0, 1), (1, 0)])


def columns(value, index, size):
    return lax.dynamic_slice_in_dim(value, index * size, size, axis=1)


def split_rows(joined, shapes):
    out = []
    offset = 0
    for shape in shapes:
        count = 1
        for extent in shape[:-1]:
            count *= extent
        count = count * shape[-1] // joined.shape[-1]
        out.append(joined[offset : offset + count].reshape(shape))
        offset += count
    return out


def join_rows(parts, lanes):
    return jnp.concatenate([p.reshape(-1, lanes) for p in parts], axis=0)


def lat_return(ext_list, height, radius):
    owns = []
    tops = join_rows([ext[:radius] for ext in ext_list], ext_list[0].shape[-1])
    bottoms = join_rows([ext[radius + height :] for ext in ext_list], ext_list[0].shape[-1])
    shapes = [ext[:radius].shape for ext in ext_list]
    from_below = split_rows(shifted(tops.astype(jnp.bfloat16), "lat", -1), shapes)
    from_above = split_rows(shifted(bottoms.astype(jnp.bfloat16), "lat", 1), shapes)
    for ext, below, above in zip(ext_list, from_below, from_above):
        middle = (
            ext[radius : radius + height]
            + jnp.pad(below.astype(jnp.float32), ((height - radius, 0), (0, 0), (0, 0)))
            + jnp.pad(above.astype(jnp.float32), ((0, height - radius), (0, 0), (0, 0)))
        )
        owns.append(middle)
    return owns


def add_lon_rims(mid_list, from_right, from_left, breadth, radius):
    owns = []
    for mid, right, left in zip(mid_list, from_right, from_left):
        owns.append(
            mid[:, radius : radius + breadth]
            + jnp.pad(right.astype(jnp.float32), ((0, 0), (breadth - radius, 0), (0, 0)))
            + jnp.pad(left.astype(jnp.float32), ((0, 0), (0, breadth - radius), (0, 0)))
        )
    return owns


def shards(tokens, cotangent, valid_cells, w_qkv, w_out):
    inputs_here = tokens[0]
    grad_here = cotangent[0]
    height, breadth, width = inputs_here.shape
    radius = RADIUS
    ext_rows = height + 2 * radius
    ext_cols = breadth + 2 * radius
    pad_cols = -(-ext_cols // 8) * 8
    token_count = height * breadth
    key_count = ext_rows * pad_cols
    flat_inputs = inputs_here.reshape(token_count, width)
    flat_grad = grad_here.reshape(token_count, width)
    dp_count = lax.axis_size("dp")
    lat_count = lax.axis_size("lat")
    lon_count = lax.axis_size("lon")
    rows_half = width // dp_count
    cols_block = width // lon_count
    rows_block = rows_half // lat_count
    dp_index = lax.axis_index("dp")
    lon_index = lax.axis_index("lon")
    fast = dp_count == 2 and lon_count == 2

    if fast:
        qkv_other = swap(w_qkv, "dp")
        dp_got = swap(jnp.concatenate([w_out, flat_grad], axis=0), "dp")
        w_out_other = dp_got[: w_out.shape[0]]
        cot_dp = dp_got[w_out.shape[0] :]
        cot_send = jnp.concatenate(
            [columns(flat_grad, 1 - lon_index, cols_block), columns(cot_dp, 1 - lon_index, cols_block)],
            axis=0,
        )
        cot_lon = swap(cot_send, "lon")
        cot_group = jnp.concatenate(
            [
                columns(flat_grad, lon_index, cols_block),
                columns(cot_dp, lon_index, cols_block),
                cot_lon,
            ],
            axis=0,
        )
        mine_part = lax.dot_general(flat_grad, w_out, TRANS_B, preferred_element_type=jnp.float32)
        other_part = lax.dot_general(
            flat_grad, w_out_other, TRANS_B, preferred_element_type=jnp.float32
        )
        mine_part = mine_part.astype(jnp.bfloat16)
        other_part = other_part.astype(jnp.bfloat16)
        grad_attn = jnp.where(
            dp_index == 0,
            jnp.concatenate([mine_part, other_part], axis=1),
            jnp.concatenate([other_part, mine_part], axis=1),
        )

        def project(rows):
            own = jnp.dot(
                columns(rows, dp_index, rows_half), w_qkv, preferred_element_type=jnp.float32
            )
            other = jnp.dot(
                columns(rows, 1 - dp_index, rows_half), qkv_other, preferred_element_type=jnp.float32
            )
            return (own + other).astype(jnp.bfloat16)

        def back_project(grad_proj):
            own = lax.dot_general(grad_proj, w_qkv, TRANS_B, preferred_element_type=jnp.float32)
            other = lax.dot_general(grad_proj, qkv_other, TRANS_B, preferred_element_type=jnp.float32)
            own = own.astype(jnp.bfloat16)
            other = other.astype(jnp.bfloat16)
            return jnp.where(
                dp_index == 0,
                jnp.concatenate([own, other], axis=1),
                jnp.concatenate([other, own], axis=1),
            )
    else:
        panels = lax.all_gather(w_qkv, "dp", axis=0, tiled=True)
        cot_blocks = flat_grad.reshape(token_count, lon_count, cols_block).transpose(1, 0, 2)
        cot_lon = exchange_blocks(cot_blocks, "lon")
        cot_group = gather_members(cot_lon, "dp").reshape(-1, cols_block)
        grad_attn = partner_rows_product(flat_grad, w_out, "dp")


        def project(rows):
            out = jnp.dot(rows, panels, preferred_element_type=jnp.float32)
            return out.astype(jnp.bfloat16)

        def back_project(grad_proj):
            out = lax.dot_general(grad_proj, panels, TRANS_B, preferred_element_type=jnp.float32)
            return out.astype(jnp.bfloat16)

    tok_ext = halo_gather(inputs_here, radius)
    tok_ext = jnp.pad(tok_ext, ((0, 0), (0, pad_cols - ext_cols), (0, 0)))
    tok_ext = tok_ext.reshape(key_count, width)

    projected = project(tok_ext)
    query = projected.reshape(ext_rows, pad_cols, 3 * width)[
        radius : radius + height, radius : radius + breadth, :width
    ].reshape(token_count, width)

    wrapped = jnp.concatenate(
        [valid_cells[:, -radius:], valid_cells, valid_cells[:, :radius]], axis=1
    )
    framed = jnp.pad(wrapped, ((radius, radius), (0, 0)))
    valid_ext = lax.dynamic_slice(
        framed,
        (lax.axis_index("lat") * height, lon_index * breadth),
        (ext_rows, ext_cols),
    )
    valid_ext = jnp.pad(valid_ext, ((0, 0), (0, pad_cols - ext_cols))).reshape(1, key_count)
    query_pos = jnp.arange(token_count)
    key_pos = jnp.arange(key_count)
    delta_row = (key_pos // pad_cols)[None, :] - radius - (query_pos // breadth)[:, None]
    delta_col = (key_pos % pad_cols)[None, :] - radius - (query_pos % breadth)[:, None]
    inside = (jnp.abs(delta_row) <= radius) & (jnp.abs(delta_col) <= radius)
    itself = (delta_row == 0) & (delta_col == 0)
    allowed = inside & ((valid_ext == 1) | itself)
    bias = jnp.where(allowed, 0.0, -jnp.inf).astype(jnp.float32)

    attended, grad_query, grad_kv, grad_kv_low = block_attention(
        query, projected, grad_attn, bias, HEADS
    )

    grad_kv_ext = grad_kv.reshape(2, ext_rows, pad_cols, width)[:, :, :ext_cols]
    grad_kv_low_ext = grad_kv_low.reshape(2, ext_rows, pad_cols, width)[:, :, :ext_cols]

    att_fits = (2 * token_count * rows_half) % (2 * height * width) == 0
    if fast and att_fits:
        own_att = columns(attended, dp_index, rows_half)
        att_from_dp = swap(columns(attended, 1 - dp_index, rows_half), "dp")
        att_dp = jnp.concatenate([own_att, att_from_dp], axis=0)
        carried = att_dp.reshape(2, height, -1, width)
        grad_kv_own, att_lon = halo_return(
            grad_kv_ext, grad_kv_low_ext, height, breadth, radius, carried
        )
        att_group = jnp.concatenate([att_dp, att_lon.reshape(att_dp.shape)], axis=0)
    else:
        grad_kv_own, _ = halo_return(grad_kv_ext, grad_kv_low_ext, height, breadth, radius)
        if fast:
            own_att = columns(attended, dp_index, rows_half)
            att_from_dp = swap(columns(attended, 1 - dp_index, rows_half), "dp")
            att_dp = jnp.concatenate([own_att, att_from_dp], axis=0)
            att_group = jnp.concatenate([att_dp, swap(att_dp, "lon")], axis=0)
        else:
            att_blocks = attended.reshape(token_count, dp_count, rows_half).transpose(1, 0, 2)
            att_dp = exchange_blocks(att_blocks, "dp")
            att_group = gather_members(att_dp, "lon")
            att_group = att_group.transpose(1, 0, 2, 3).reshape(-1, rows_half)

    device_count = dp_count * lat_count * lon_count
    partial = lax.dot_general(
        att_group, cot_group, (((0,), (0,)), ((), ())), preferred_element_type=jnp.float32
    ) * (1.0 / device_count)
    spread = lax.all_to_all(partial.astype(jnp.bfloat16), "lat", 0, 0, tiled=True)
    d_w_out = spread.astype(jnp.float32).reshape(lat_count, rows_block, cols_block).sum(axis=0)

    grad_kv_own = grad_kv_own.astype(jnp.bfloat16).reshape(2, token_count, width)
    grad_proj = jnp.concatenate([grad_query, grad_kv_own[0], grad_kv_own[1]], axis=1)
    d_input = back_project(grad_proj).reshape(1, height, breadth, width)
    return (d_input, d_w_out)


def solution(mesh):
    in_specs = (
        P("dp", "lat", "lon", None),
        P("dp", "lat", "lon", None),
        P(),
        P("dp", None),
        P("dp", None),
    )
    out_specs = (P("dp", "lat", "lon", None), P(("dp", "lat"), "lon"))
    return jax.shard_map(shards, mesh=mesh, in_specs=in_specs, out_specs=out_specs, check_vma=False)
```

```python
import functools

import jax
import jax.numpy as jnp
from jax import lax
from jax.experimental import pallas as pl
from jax.sharding import PartitionSpec as P

HEADS = 16
RADIUS = 6

TRANS_B = (((1,), (1,)), ((), ()))


def passed_along(value, axis, steps):
    count = lax.axis_size(axis)
    pairs = [(source, (source + steps) % count) for source in range(count)]
    return lax.ppermute(value, axis, pairs)


def shifted(value, axis, by):
    count = lax.axis_size(axis)
    pairs = [(i, i + by) for i in range(count) if 0 <= i + by < count]
    return lax.ppermute(value, axis, pairs)


def extended(block, sides, width, periodic):
    for axis, dim in sides:
        count = lax.axis_size(axis)
        forward = [(i, i + 1) for i in range(count - 1)]
        if periodic:
            forward.append((count - 1, 0))
        backward = [(target, source) for source, target in forward]
        low = lax.ppermute(
            lax.slice_in_dim(block, block.shape[dim] - width, None, axis=dim), axis, forward
        )
        high = lax.ppermute(lax.slice_in_dim(block, 0, width, axis=dim), axis, backward)
        block = jnp.concatenate([low, block, high], axis=dim)
    return block


def attention_kernel(q_ref, k_ref, v_ref, g_ref, bias_ref, att_ref, gq_ref, gkv_ref, gkv_low_ref,
                     *, head_dim, scale):
    q = q_ref[...]
    g = g_ref[...]
    k = k_ref[...]
    v = v_ref[...]
    bias = bias_ref[...]
    lanes = q.shape[1]
    lane = lax.broadcasted_iota(jnp.int32, (1, lanes), 1)
    zero = jnp.zeros((), q.dtype)
    sels = [(lane >= j * head_dim) & (lane < (j + 1) * head_dim) for j in range(lanes // head_dim)]
    q_scaled = (q.astype(jnp.float32) * scale).astype(q.dtype)
    g_scaled = (g.astype(jnp.float32) * scale).astype(g.dtype)
    probs_list = []
    grads_list = []
    for sel in sels:
        qj = jnp.where(sel, q_scaled, zero)
        gj = jnp.where(sel, g_scaled, zero)
        masked = lax.dot_general(qj, k, TRANS_B, preferred_element_type=jnp.float32) + bias
        peak = jnp.max(masked, axis=1, keepdims=True)
        weights = jnp.exp(masked - peak)
        probs = weights * (1.0 / jnp.sum(weights, axis=1, keepdims=True))
        grad_probs = lax.dot_general(gj, v, TRANS_B, preferred_element_type=jnp.float32)
        centre = jnp.sum(probs * grad_probs, axis=1, keepdims=True)
        grads_list.append((probs * (grad_probs - centre)).astype(jnp.bfloat16))
        probs_list.append(probs.astype(jnp.bfloat16))
    k_sel = jnp.concatenate([jnp.where(sel, k, zero) for sel in sels], axis=0)
    v_sel = jnp.concatenate([jnp.where(sel, v, zero) for sel in sels], axis=0)
    q_sel = jnp.concatenate([jnp.where(sel, q, zero) for sel in sels], axis=0)
    g_sel = jnp.concatenate([jnp.where(sel, g, zero) for sel in sels], axis=0)
    probs_cat = jnp.concatenate(probs_list, axis=1)
    grads_cat = jnp.concatenate(grads_list, axis=1)
    att = jnp.dot(probs_cat, v_sel, preferred_element_type=jnp.float32)
    gq = jnp.dot(grads_cat, k_sel, preferred_element_type=jnp.float32)
    grads_t = jnp.concatenate(
        [x.astype(jnp.float32).T.astype(jnp.bfloat16) for x in grads_list], axis=1
    )
    probs_t = jnp.concatenate(
        [x.astype(jnp.float32).T.astype(jnp.bfloat16) for x in probs_list], axis=1
    )
    att_ref[...] = att.astype(att_ref.dtype)
    gq_ref[...] = gq.astype(gq_ref.dtype)
    grad_k = jnp.dot(grads_t, q_sel, preferred_element_type=jnp.float32)
    grad_v = jnp.dot(probs_t, g_sel, preferred_element_type=jnp.float32)
    gkv_ref[0] = grad_k
    gkv_ref[1] = grad_v
    gkv_low_ref[0] = grad_k.astype(gkv_low_ref.dtype)
    gkv_low_ref[1] = grad_v.astype(gkv_low_ref.dtype)


def block_attention(query, projected, grad_attn, bias, heads):
    queries, width = query.shape
    keys = projected.shape[0]
    head_dim = width // heads
    lanes = 128
    pairs = width // lanes
    kernel = functools.partial(attention_kernel, head_dim=head_dim, scale=head_dim ** (-0.5))
    flops = 2 * queries * keys * width * 2 * 6
    cost = pl.CostEstimate(
        flops=flops,
        transcendentals=queries * keys * heads,
        bytes_accessed=2 * (2 * queries * width + 2 * keys * width + 2 * queries * width)
        + 4 * queries * keys + 4 * 2 * keys * width,
    )
    return pl.pallas_call(
        kernel,
        grid=(pairs,),
        in_specs=[
            pl.BlockSpec((queries, lanes), lambda h: (0, h)),
            pl.BlockSpec((keys, lanes), lambda h: (0, h + pairs)),
            pl.BlockSpec((keys, lanes), lambda h: (0, h + 2 * pairs)),
            pl.BlockSpec((queries, lanes), lambda h: (0, h)),
            pl.BlockSpec((queries, keys), lambda h: (0, 0)),
        ],
        out_specs=[
            pl.BlockSpec((queries, lanes), lambda h: (0, h)),
            pl.BlockSpec((queries, lanes), lambda h: (0, h)),
            pl.BlockSpec((2, keys, lanes), lambda h: (0, 0, h)),
            pl.BlockSpec((2, keys, lanes), lambda h: (0, 0, h)),
        ],
        out_shape=[
            jax.ShapeDtypeStruct((queries, width), jnp.bfloat16),
            jax.ShapeDtypeStruct((queries, width), jnp.bfloat16),
            jax.ShapeDtypeStruct((2, keys, width), jnp.float32),
            jax.ShapeDtypeStruct((2, keys, width), jnp.bfloat16),
        ],
        cost_estimate=cost,
        name="block_attention",
    )(query, projected, projected, grad_attn, bias)


def grid_pairs(delta_lat, delta_lon):
    lat_count = lax.axis_size("lat")
    lon_count = lax.axis_size("lon")
    pairs = []
    for la in range(lat_count):
        if 0 <= la + delta_lat < lat_count:
            for lo in range(lon_count):
                target = (la + delta_lat) * lon_count + (lo + delta_lon) % lon_count
                pairs.append((la * lon_count + lo, target))
    return pairs


def sent_to(value, delta_lat, delta_lon):
    return lax.ppermute(value, ("lat", "lon"), grid_pairs(delta_lat, delta_lon))


def part(count, radius, step, giving):
    if step == 0:
        return slice(0, count)
    if (step < 0) == giving:
        return slice(count - radius, count)
    return slice(0, radius)


def grouped_send(pieces, axis):
    lon_count = lax.axis_size("lon")
    groups = {}
    for index, (dl, db, value) in enumerate(pieces):
        groups.setdefault((dl, db % lon_count), []).append(index)
    out = [None] * len(pieces)
    for (dl, db), members in groups.items():
        values = [pieces[i][2] for i in members]
        got = sent_to(jnp.concatenate(values, axis=axis), dl, db)
        offset = 0
        for i, value in zip(members, values):
            out[i] = lax.slice_in_dim(got, offset, offset + value.shape[axis], axis=axis)
            offset += value.shape[axis]
    return out


def halo_gather(block, radius):
    height, breadth, lanes = block.shape
    spots = []
    pieces = []
    for da in (-1, 0, 1):
        for db in (-1, 0, 1):
            if da == 0 and db == 0:
                continue
            piece = block[part(height, radius, da, True), part(breadth, radius, db, True)]
            spots.append((da, db))
            pieces.append((-da, -db, piece))
    got = dict(zip(spots, grouped_send(pieces, 1)))
    got[(0, 0)] = block
    rows = [jnp.concatenate([got[(da, db)] for db in (-1, 0, 1)], axis=1) for da in (-1, 0, 1)]
    return jnp.concatenate(rows, axis=0)


def halo_return(ext, ext_low, height, breadth, radius, extra=None):
    row_slices = {-1: slice(0, radius), 0: slice(radius, radius + height), 1: slice(radius + height, None)}
    col_slices = {-1: slice(0, radius), 0: slice(radius, radius + breadth), 1: slice(radius + breadth, None)}
    own = ext[:, row_slices[0], col_slices[0]]
    spots = []
    pieces = []
    for da in (-1, 0, 1):
        for db in (-1, 0, 1):
            if da == 0 and db == 0:
                continue
            spots.append((da, db))
            pieces.append((da, db, ext_low[:, row_slices[da], col_slices[db]]))
    if extra is not None:
        spots.append(None)
        pieces.append((0, 1, extra))
    received = grouped_send(pieces, 2)
    extra_got = received[-1] if extra is not None else None
    for spot, got in zip(spots, received):
        if spot is None:
            continue
        da, db = spot
        rs = part(height, radius, da, True)
        cs = part(breadth, radius, db, True)
        pad_rows = (rs.start, height - rs.stop)
        pad_cols = (cs.start, breadth - cs.stop)
        own = own + jnp.pad(got.astype(jnp.float32), ((0, 0), pad_rows, pad_cols, (0, 0)))
    return own, extra_got


def partner_rows_product(lhs, weights, axis):
    count = lax.axis_size(axis)
    if count != 2:
        full = lax.all_gather(weights, axis, axis=0, tiled=True)
        return lax.dot_general(lhs, full, TRANS_B, preferred_element_type=jnp.float32).astype(
            jnp.bfloat16
        )
    other = lax.ppermute(weights, axis, [(0, 1), (1, 0)])
    mine_part = lax.dot_general(lhs, weights, TRANS_B, preferred_element_type=jnp.float32)
    other_part = lax.dot_general(lhs, other, TRANS_B, preferred_element_type=jnp.float32)
    mine_part = mine_part.astype(jnp.bfloat16)
    other_part = other_part.astype(jnp.bfloat16)
    first = lax.axis_index(axis) == 0
    return jnp.where(
        first,
        jnp.concatenate([mine_part, other_part], axis=1),
        jnp.concatenate([other_part, mine_part], axis=1),
    )


def exchange_blocks(blocks, axis):
    count = lax.axis_size(axis)
    if count == 2:
        me = lax.axis_index(axis)
        mine = lax.dynamic_index_in_dim(blocks, me, 0, keepdims=False)
        theirs = lax.dynamic_index_in_dim(blocks, 1 - me, 0, keepdims=False)
        got = lax.ppermute(theirs, axis, [(0, 1), (1, 0)])
        return jnp.where(me == 0, jnp.stack([mine, got]), jnp.stack([got, mine]))
    flat = blocks.reshape((-1,) + blocks.shape[2:])
    out = lax.all_to_all(flat, axis, 0, 0, tiled=True)
    return out.reshape(blocks.shape)


def gather_members(value, axis):
    count = lax.axis_size(axis)
    if count == 2:
        me = lax.axis_index(axis)
        got = lax.ppermute(value, axis, [(0, 1), (1, 0)])
        return jnp.where(me == 0, jnp.stack([value, got]), jnp.stack([got, value]))
    return lax.all_gather(value, axis, axis=0, tiled=False)


def swap(value, axis):
    return lax.ppermute(value, axis, [(0, 1), (1, 0)])


def columns(value, index, size):
    return lax.dynamic_slice_in_dim(value, index * size, size, axis=1)


def split_rows(joined, shapes):
    out = []
    offset = 0
    for shape in shapes:
        count = 1
        for extent in shape[:-1]:
            count *= extent
        count = count * shape[-1] // joined.shape[-1]
        out.append(joined[offset : offset + count].reshape(shape))
        offset += count
    return out


def join_rows(parts, lanes):
    return jnp.concatenate([p.reshape(-1, lanes) for p in parts], axis=0)


def lat_return(ext_list, height, radius):
    owns = []
    tops = join_rows([ext[:radius] for ext in ext_list], ext_list[0].shape[-1])
    bottoms = join_rows([ext[radius + height :] for ext in ext_list], ext_list[0].shape[-1])
    shapes = [ext[:radius].shape for ext in ext_list]
    from_below = split_rows(shifted(tops.astype(jnp.bfloat16), "lat", -1), shapes)
    from_above = split_rows(shifted(bottoms.astype(jnp.bfloat16), "lat", 1), shapes)
    for ext, below, above in zip(ext_list, from_below, from_above):
        middle = (
            ext[radius : radius + height]
            + jnp.pad(below.astype(jnp.float32), ((height - radius, 0), (0, 0), (0, 0)))
            + jnp.pad(above.astype(jnp.float32), ((0, height - radius), (0, 0), (0, 0)))
        )
        owns.append(middle)
    return owns


def add_lon_rims(mid_list, from_right, from_left, breadth, radius):
    owns = []
    for mid, right, left in zip(mid_list, from_right, from_left):
        owns.append(
            mid[:, radius : radius + breadth]
            + jnp.pad(right.astype(jnp.float32), ((0, 0), (breadth - radius, 0), (0, 0)))
            + jnp.pad(left.astype(jnp.float32), ((0, 0), (0, breadth - radius), (0, 0)))
        )
    return owns


def shards(tokens, cotangent, valid_cells, w_qkv, w_out):
    inputs_here = tokens[0]
    grad_here = cotangent[0]
    height, breadth, width = inputs_here.shape
    radius = RADIUS
    ext_rows = height + 2 * radius
    ext_cols = breadth + 2 * radius
    pad_cols = -(-ext_cols // 8) * 8
    token_count = height * breadth
    key_count = ext_rows * pad_cols
    flat_inputs = inputs_here.reshape(token_count, width)
    flat_grad = grad_here.reshape(token_count, width)
    dp_count = lax.axis_size("dp")
    lat_count = lax.axis_size("lat")
    lon_count = lax.axis_size("lon")
    rows_half = width // dp_count
    cols_block = width // lon_count
    rows_block = rows_half // lat_count
    dp_index = lax.axis_index("dp")
    lon_index = lax.axis_index("lon")
    fast = dp_count == 2 and lon_count == 2

    if fast:
        qkv_other = swap(w_qkv, "dp")
        dp_all = lax.all_gather(jnp.concatenate([w_out, flat_grad], axis=0), "dp", axis=0)
        dp_got = lax.dynamic_index_in_dim(dp_all, 1 - dp_index, 0, keepdims=False)
        w_out_other = dp_got[: w_out.shape[0]]
        cot_dp = dp_got[w_out.shape[0] :]
        cot_send = jnp.concatenate(
            [columns(flat_grad, 1 - lon_index, cols_block), columns(cot_dp, 1 - lon_index, cols_block)],
            axis=0,
        )
        cot_lon = swap(cot_send, "lon")
        cot_group = jnp.concatenate(
            [
                columns(flat_grad, lon_index, cols_block),
                columns(cot_dp, lon_index, cols_block),
                cot_lon,
            ],
            axis=0,
        )
        mine_part = lax.dot_general(flat_grad, w_out, TRANS_B, preferred_element_type=jnp.float32)
        other_part = lax.dot_general(
            flat_grad, w_out_other, TRANS_B, preferred_element_type=jnp.float32
        )
        mine_part = mine_part.astype(jnp.bfloat16)
        other_part = other_part.astype(jnp.bfloat16)
        grad_attn = jnp.where(
            dp_index == 0,
            jnp.concatenate([mine_part, other_part], axis=1),
            jnp.concatenate([other_part, mine_part], axis=1),
        )

        def project(rows):
            own = jnp.dot(
                columns(rows, dp_index, rows_half), w_qkv, preferred_element_type=jnp.float32
            )
            other = jnp.dot(
                columns(rows, 1 - dp_index, rows_half), qkv_other, preferred_element_type=jnp.float32
            )
            return (own + other).astype(jnp.bfloat16)

        def back_project(grad_proj):
            own = lax.dot_general(grad_proj, w_qkv, TRANS_B, preferred_element_type=jnp.float32)
            other = lax.dot_general(grad_proj, qkv_other, TRANS_B, preferred_element_type=jnp.float32)
            own = own.astype(jnp.bfloat16)
            other = other.astype(jnp.bfloat16)
            return jnp.where(
                dp_index == 0,
                jnp.concatenate([own, other], axis=1),
                jnp.concatenate([other, own], axis=1),
            )
    else:
        panels = lax.all_gather(w_qkv, "dp", axis=0, tiled=True)
        cot_blocks = flat_grad.reshape(token_count, lon_count, cols_block).transpose(1, 0, 2)
        cot_lon = exchange_blocks(cot_blocks, "lon")
        cot_group = gather_members(cot_lon, "dp").reshape(-1, cols_block)
        grad_attn = partner_rows_product(flat_grad, w_out, "dp")


        def project(rows):
            out = jnp.dot(rows, panels, preferred_element_type=jnp.float32)
            return out.astype(jnp.bfloat16)

        def back_project(grad_proj):
            out = lax.dot_general(grad_proj, panels, TRANS_B, preferred_element_type=jnp.float32)
            return out.astype(jnp.bfloat16)

    tok_ext = halo_gather(inputs_here, radius)
    tok_ext = jnp.pad(tok_ext, ((0, 0), (0, pad_cols - ext_cols), (0, 0)))
    tok_ext = tok_ext.reshape(key_count, width)

    projected = project(tok_ext)
    query = projected.reshape(ext_rows, pad_cols, 3 * width)[
        radius : radius + height, radius : radius + breadth, :width
    ].reshape(token_count, width)

    wrapped = jnp.concatenate(
        [valid_cells[:, -radius:], valid_cells, valid_cells[:, :radius]], axis=1
    )
    framed = jnp.pad(wrapped, ((radius, radius), (0, 0)))
    valid_ext = lax.dynamic_slice(
        framed,
        (lax.axis_index("lat") * height, lon_index * breadth),
        (ext_rows, ext_cols),
    )
    valid_ext = jnp.pad(valid_ext, ((0, 0), (0, pad_cols - ext_cols))).reshape(1, key_count)
    query_pos = jnp.arange(token_count)
    key_pos = jnp.arange(key_count)
    delta_row = (key_pos // pad_cols)[None, :] - radius - (query_pos // breadth)[:, None]
    delta_col = (key_pos % pad_cols)[None, :] - radius - (query_pos % breadth)[:, None]
    inside = (jnp.abs(delta_row) <= radius) & (jnp.abs(delta_col) <= radius)
    itself = (delta_row == 0) & (delta_col == 0)
    allowed = inside & ((valid_ext == 1) | itself)
    bias = jnp.where(allowed, 0.0, -jnp.inf).astype(jnp.float32)

    attended, grad_query, grad_kv, grad_kv_low = block_attention(
        query, projected, grad_attn, bias, HEADS
    )

    grad_kv_ext = grad_kv.reshape(2, ext_rows, pad_cols, width)[:, :, :ext_cols]
    grad_kv_low_ext = grad_kv_low.reshape(2, ext_rows, pad_cols, width)[:, :, :ext_cols]

    att_fits = (2 * token_count * rows_half) % (2 * height * width) == 0
    if fast and att_fits:
        own_att = columns(attended, dp_index, rows_half)
        att_from_dp = swap(columns(attended, 1 - dp_index, rows_half), "dp")
        att_dp = jnp.concatenate([own_att, att_from_dp], axis=0)
        carried = att_dp.reshape(2, height, -1, width)
        grad_kv_own, att_lon = halo_return(
            grad_kv_ext, grad_kv_low_ext, height, breadth, radius, carried
        )
        att_group = jnp.concatenate([att_dp, att_lon.reshape(att_dp.shape)], axis=0)
    else:
        grad_kv_own, _ = halo_return(grad_kv_ext, grad_kv_low_ext, height, breadth, radius)
        if fast:
            own_att = columns(attended, dp_index, rows_half)
            att_from_dp = swap(columns(attended, 1 - dp_index, rows_half), "dp")
            att_dp = jnp.concatenate([own_att, att_from_dp], axis=0)
            att_group = jnp.concatenate([att_dp, swap(att_dp, "lon")], axis=0)
        else:
            att_blocks = attended.reshape(token_count, dp_count, rows_half).transpose(1, 0, 2)
            att_dp = exchange_blocks(att_blocks, "dp")
            att_group = gather_members(att_dp, "lon")
            att_group = att_group.transpose(1, 0, 2, 3).reshape(-1, rows_half)

    device_count = dp_count * lat_count * lon_count
    partial = lax.dot_general(
        att_group, cot_group, (((0,), (0,)), ((), ())), preferred_element_type=jnp.float32
    ) * (1.0 / device_count)
    spread = lax.all_to_all(partial.astype(jnp.bfloat16), "lat", 0, 0, tiled=True)
    d_w_out = spread.astype(jnp.float32).reshape(lat_count, rows_block, cols_block).sum(axis=0)

    grad_kv_own = grad_kv_own.astype(jnp.bfloat16).reshape(2, token_count, width)
    grad_proj = jnp.concatenate([grad_query, grad_kv_own[0], grad_kv_own[1]], axis=1)
    d_input = back_project(grad_proj).reshape(1, height, breadth, width)
    return (d_input, d_w_out)


def solution(mesh):
    in_specs = (
        P("dp", "lat", "lon", None),
        P("dp", "lat", "lon", None),
        P(),
        P("dp", None),
        P("dp", None),
    )
    out_specs = (P("dp", "lat", "lon", None), P(("dp", "lat"), "lon"))
    return jax.shard_map(shards, mesh=mesh, in_specs=in_specs, out_specs=out_specs, check_vma=False)
```

```python
import functools

import jax
import jax.numpy as jnp
from jax import lax
from jax.experimental import pallas as pl
from jax.sharding import PartitionSpec as P

HEADS = 16
RADIUS = 6

TRANS_B = (((1,), (1,)), ((), ()))


def passed_along(value, axis, steps):
    count = lax.axis_size(axis)
    pairs = [(source, (source + steps) % count) for source in range(count)]
    return lax.ppermute(value, axis, pairs)


def shifted(value, axis, by):
    count = lax.axis_size(axis)
    pairs = [(i, i + by) for i in range(count) if 0 <= i + by < count]
    return lax.ppermute(value, axis, pairs)


def extended(block, sides, width, periodic):
    for axis, dim in sides:
        count = lax.axis_size(axis)
        forward = [(i, i + 1) for i in range(count - 1)]
        if periodic:
            forward.append((count - 1, 0))
        backward = [(target, source) for source, target in forward]
        low = lax.ppermute(
            lax.slice_in_dim(block, block.shape[dim] - width, None, axis=dim), axis, forward
        )
        high = lax.ppermute(lax.slice_in_dim(block, 0, width, axis=dim), axis, backward)
        block = jnp.concatenate([low, block, high], axis=dim)
    return block


def pair_terms(q, k, v, g, bias, head_dim, scale):
    lanes = q.shape[1]
    lane = lax.broadcasted_iota(jnp.int32, (1, lanes), 1)
    zero = jnp.zeros((), q.dtype)
    sels = [(lane >= j * head_dim) & (lane < (j + 1) * head_dim) for j in range(lanes // head_dim)]
    q_scaled = (q.astype(jnp.float32) * scale).astype(q.dtype)
    g_scaled = (g.astype(jnp.float32) * scale).astype(g.dtype)
    probs_list = []
    grads_list = []
    for sel in sels:
        qj = jnp.where(sel, q_scaled, zero)
        gj = jnp.where(sel, g_scaled, zero)
        masked = lax.dot_general(qj, k, TRANS_B, preferred_element_type=jnp.float32) + bias
        peak = jnp.max(masked, axis=1, keepdims=True)
        weights = jnp.exp(masked - peak)
        probs = weights * (1.0 / jnp.sum(weights, axis=1, keepdims=True))
        grad_probs = lax.dot_general(gj, v, TRANS_B, preferred_element_type=jnp.float32)
        centre = jnp.sum(probs * grad_probs, axis=1, keepdims=True)
        grads_list.append((probs * (grad_probs - centre)).astype(jnp.bfloat16))
        probs_list.append(probs.astype(jnp.bfloat16))
    k_sel = jnp.concatenate([jnp.where(sel, k, zero) for sel in sels], axis=0)
    v_sel = jnp.concatenate([jnp.where(sel, v, zero) for sel in sels], axis=0)
    q_sel = jnp.concatenate([jnp.where(sel, q, zero) for sel in sels], axis=0)
    g_sel = jnp.concatenate([jnp.where(sel, g, zero) for sel in sels], axis=0)
    probs_cat = jnp.concatenate(probs_list, axis=1)
    grads_cat = jnp.concatenate(grads_list, axis=1)
    att = jnp.dot(probs_cat, v_sel, preferred_element_type=jnp.float32)
    gq = jnp.dot(grads_cat, k_sel, preferred_element_type=jnp.float32)
    grads_t = jnp.concatenate(
        [x.astype(jnp.float32).T.astype(jnp.bfloat16) for x in grads_list], axis=1
    )
    probs_t = jnp.concatenate(
        [x.astype(jnp.float32).T.astype(jnp.bfloat16) for x in probs_list], axis=1
    )
    grad_k = jnp.dot(grads_t, q_sel, preferred_element_type=jnp.float32)
    grad_v = jnp.dot(probs_t, g_sel, preferred_element_type=jnp.float32)
    return att, gq, grad_k, grad_v


def attention_kernel(q_ref, k_ref, v_ref, g_ref, bias_ref, att_ref, gq_ref, gkv_ref, gkv_low_ref,
                     *, head_dim, scale, lanes):
    bias = bias_ref[...]
    for sub in range(q_ref.shape[1] // lanes):
        cols = slice(sub * lanes, (sub + 1) * lanes)
        att, gq, grad_k, grad_v = pair_terms(
            q_ref[:, cols], k_ref[:, cols], v_ref[:, cols], g_ref[:, cols], bias, head_dim, scale
        )
        att_ref[:, cols] = att.astype(att_ref.dtype)
        gq_ref[:, cols] = gq.astype(gq_ref.dtype)
        gkv_ref[0, :, cols] = grad_k
        gkv_ref[1, :, cols] = grad_v
        gkv_low_ref[0, :, cols] = grad_k.astype(gkv_low_ref.dtype)
        gkv_low_ref[1, :, cols] = grad_v.astype(gkv_low_ref.dtype)


def block_attention(query, projected, grad_attn, bias, heads):
    queries, width = query.shape
    keys = projected.shape[0]
    head_dim = width // heads
    lanes = 256
    pairs = width // lanes
    kernel = functools.partial(
        attention_kernel, head_dim=head_dim, scale=head_dim ** (-0.5), lanes=128
    )
    flops = 2 * queries * keys * width * 2 * 6
    cost = pl.CostEstimate(
        flops=flops,
        transcendentals=queries * keys * heads,
        bytes_accessed=2 * (2 * queries * width + 2 * keys * width + 2 * queries * width)
        + 4 * queries * keys + 4 * 2 * keys * width,
    )
    return pl.pallas_call(
        kernel,
        grid=(pairs,),
        in_specs=[
            pl.BlockSpec((queries, lanes), lambda h: (0, h)),
            pl.BlockSpec((keys, lanes), lambda h: (0, h + pairs)),
            pl.BlockSpec((keys, lanes), lambda h: (0, h + 2 * pairs)),
            pl.BlockSpec((queries, lanes), lambda h: (0, h)),
            pl.BlockSpec((queries, keys), lambda h: (0, 0)),
        ],
        out_specs=[
            pl.BlockSpec((queries, lanes), lambda h: (0, h)),
            pl.BlockSpec((queries, lanes), lambda h: (0, h)),
            pl.BlockSpec((2, keys, lanes), lambda h: (0, 0, h)),
            pl.BlockSpec((2, keys, lanes), lambda h: (0, 0, h)),
        ],
        out_shape=[
            jax.ShapeDtypeStruct((queries, width), jnp.bfloat16),
            jax.ShapeDtypeStruct((queries, width), jnp.bfloat16),
            jax.ShapeDtypeStruct((2, keys, width), jnp.float32),
            jax.ShapeDtypeStruct((2, keys, width), jnp.bfloat16),
        ],
        cost_estimate=cost,
        name="block_attention",
    )(query, projected, projected, grad_attn, bias)


def grid_pairs(delta_lat, delta_lon):
    lat_count = lax.axis_size("lat")
    lon_count = lax.axis_size("lon")
    pairs = []
    for la in range(lat_count):
        if 0 <= la + delta_lat < lat_count:
            for lo in range(lon_count):
                target = (la + delta_lat) * lon_count + (lo + delta_lon) % lon_count
                pairs.append((la * lon_count + lo, target))
    return pairs


def sent_to(value, delta_lat, delta_lon):
    return lax.ppermute(value, ("lat", "lon"), grid_pairs(delta_lat, delta_lon))


def part(count, radius, step, giving):
    if step == 0:
        return slice(0, count)
    if (step < 0) == giving:
        return slice(count - radius, count)
    return slice(0, radius)


def grouped_send(pieces, axis):
    lon_count = lax.axis_size("lon")
    groups = {}
    for index, (dl, db, value) in enumerate(pieces):
        groups.setdefault((dl, db % lon_count), []).append(index)
    out = [None] * len(pieces)
    for (dl, db), members in groups.items():
        values = [pieces[i][2] for i in members]
        got = sent_to(jnp.concatenate(values, axis=axis), dl, db)
        offset = 0
        for i, value in zip(members, values):
            out[i] = lax.slice_in_dim(got, offset, offset + value.shape[axis], axis=axis)
            offset += value.shape[axis]
    return out


def halo_gather(block, radius):
    height, breadth, lanes = block.shape
    spots = []
    pieces = []
    for da in (-1, 0, 1):
        for db in (-1, 0, 1):
            if da == 0 and db == 0:
                continue
            piece = block[part(height, radius, da, True), part(breadth, radius, db, True)]
            spots.append((da, db))
            pieces.append((-da, -db, piece))
    got = dict(zip(spots, grouped_send(pieces, 1)))
    got[(0, 0)] = block
    rows = [jnp.concatenate([got[(da, db)] for db in (-1, 0, 1)], axis=1) for da in (-1, 0, 1)]
    return jnp.concatenate(rows, axis=0)


def halo_return(ext, ext_low, height, breadth, radius, extra=None):
    row_slices = {-1: slice(0, radius), 0: slice(radius, radius + height), 1: slice(radius + height, None)}
    col_slices = {-1: slice(0, radius), 0: slice(radius, radius + breadth), 1: slice(radius + breadth, None)}
    own = ext[:, row_slices[0], col_slices[0]]
    spots = []
    pieces = []
    for da in (-1, 0, 1):
        for db in (-1, 0, 1):
            if da == 0 and db == 0:
                continue
            spots.append((da, db))
            pieces.append((da, db, ext_low[:, row_slices[da], col_slices[db]]))
    if extra is not None:
        spots.append(None)
        pieces.append((0, 1, extra))
    received = grouped_send(pieces, 2)
    extra_got = received[-1] if extra is not None else None
    for spot, got in zip(spots, received):
        if spot is None:
            continue
        da, db = spot
        rs = part(height, radius, da, True)
        cs = part(breadth, radius, db, True)
        pad_rows = (rs.start, height - rs.stop)
        pad_cols = (cs.start, breadth - cs.stop)
        own = own + jnp.pad(got.astype(jnp.float32), ((0, 0), pad_rows, pad_cols, (0, 0)))
    return own, extra_got


def partner_rows_product(lhs, weights, axis):
    count = lax.axis_size(axis)
    if count != 2:
        full = lax.all_gather(weights, axis, axis=0, tiled=True)
        return lax.dot_general(lhs, full, TRANS_B, preferred_element_type=jnp.float32).astype(
            jnp.bfloat16
        )
    other = lax.ppermute(weights, axis, [(0, 1), (1, 0)])
    mine_part = lax.dot_general(lhs, weights, TRANS_B, preferred_element_type=jnp.float32)
    other_part = lax.dot_general(lhs, other, TRANS_B, preferred_element_type=jnp.float32)
    mine_part = mine_part.astype(jnp.bfloat16)
    other_part = other_part.astype(jnp.bfloat16)
    first = lax.axis_index(axis) == 0
    return jnp.where(
        first,
        jnp.concatenate([mine_part, other_part], axis=1),
        jnp.concatenate([other_part, mine_part], axis=1),
    )


def exchange_blocks(blocks, axis):
    count = lax.axis_size(axis)
    if count == 2:
        me = lax.axis_index(axis)
        mine = lax.dynamic_index_in_dim(blocks, me, 0, keepdims=False)
        theirs = lax.dynamic_index_in_dim(blocks, 1 - me, 0, keepdims=False)
        got = lax.ppermute(theirs, axis, [(0, 1), (1, 0)])
        return jnp.where(me == 0, jnp.stack([mine, got]), jnp.stack([got, mine]))
    flat = blocks.reshape((-1,) + blocks.shape[2:])
    out = lax.all_to_all(flat, axis, 0, 0, tiled=True)
    return out.reshape(blocks.shape)


def gather_members(value, axis):
    count = lax.axis_size(axis)
    if count == 2:
        me = lax.axis_index(axis)
        got = lax.ppermute(value, axis, [(0, 1), (1, 0)])
        return jnp.where(me == 0, jnp.stack([value, got]), jnp.stack([got, value]))
    return lax.all_gather(value, axis, axis=0, tiled=False)


def swap(value, axis):
    return lax.ppermute(value, axis, [(0, 1), (1, 0)])


def columns(value, index, size):
    return lax.dynamic_slice_in_dim(value, index * size, size, axis=1)


def split_rows(joined, shapes):
    out = []
    offset = 0
    for shape in shapes:
        count = 1
        for extent in shape[:-1]:
            count *= extent
        count = count * shape[-1] // joined.shape[-1]
        out.append(joined[offset : offset + count].reshape(shape))
        offset += count
    return out


def join_rows(parts, lanes):
    return jnp.concatenate([p.reshape(-1, lanes) for p in parts], axis=0)


def lat_return(ext_list, height, radius):
    owns = []
    tops = join_rows([ext[:radius] for ext in ext_list], ext_list[0].shape[-1])
    bottoms = join_rows([ext[radius + height :] for ext in ext_list], ext_list[0].shape[-1])
    shapes = [ext[:radius].shape for ext in ext_list]
    from_below = split_rows(shifted(tops.astype(jnp.bfloat16), "lat", -1), shapes)
    from_above = split_rows(shifted(bottoms.astype(jnp.bfloat16), "lat", 1), shapes)
    for ext, below, above in zip(ext_list, from_below, from_above):
        middle = (
            ext[radius : radius + height]
            + jnp.pad(below.astype(jnp.float32), ((height - radius, 0), (0, 0), (0, 0)))
            + jnp.pad(above.astype(jnp.float32), ((0, height - radius), (0, 0), (0, 0)))
        )
        owns.append(middle)
    return owns


def add_lon_rims(mid_list, from_right, from_left, breadth, radius):
    owns = []
    for mid, right, left in zip(mid_list, from_right, from_left):
        owns.append(
            mid[:, radius : radius + breadth]
            + jnp.pad(right.astype(jnp.float32), ((0, 0), (breadth - radius, 0), (0, 0)))
            + jnp.pad(left.astype(jnp.float32), ((0, 0), (0, breadth - radius), (0, 0)))
        )
    return owns


def shards(tokens, cotangent, valid_cells, w_qkv, w_out):
    inputs_here = tokens[0]
    grad_here = cotangent[0]
    height, breadth, width = inputs_here.shape
    radius = RADIUS
    ext_rows = height + 2 * radius
    ext_cols = breadth + 2 * radius
    pad_cols = -(-ext_cols // 8) * 8
    token_count = height * breadth
    key_count = ext_rows * pad_cols
    flat_inputs = inputs_here.reshape(token_count, width)
    flat_grad = grad_here.reshape(token_count, width)
    dp_count = lax.axis_size("dp")
    lat_count = lax.axis_size("lat")
    lon_count = lax.axis_size("lon")
    rows_half = width // dp_count
    cols_block = width // lon_count
    rows_block = rows_half // lat_count
    dp_index = lax.axis_index("dp")
    lon_index = lax.axis_index("lon")
    fast = dp_count == 2 and lon_count == 2

    if fast:
        qkv_other = swap(w_qkv, "dp")
        dp_got = swap(jnp.concatenate([w_out, flat_grad], axis=0), "dp")
        w_out_other = dp_got[: w_out.shape[0]]
        cot_dp = dp_got[w_out.shape[0] :]
        cot_send = jnp.concatenate(
            [columns(flat_grad, 1 - lon_index, cols_block), columns(cot_dp, 1 - lon_index, cols_block)],
            axis=0,
        )
        cot_lon = swap(cot_send, "lon")
        cot_group = jnp.concatenate(
            [
                columns(flat_grad, lon_index, cols_block),
                columns(cot_dp, lon_index, cols_block),
                cot_lon,
            ],
            axis=0,
        )
        mine_part = lax.dot_general(flat_grad, w_out, TRANS_B, preferred_element_type=jnp.float32)
        other_part = lax.dot_general(
            flat_grad, w_out_other, TRANS_B, preferred_element_type=jnp.float32
        )
        mine_part = mine_part.astype(jnp.bfloat16)
        other_part = other_part.astype(jnp.bfloat16)
        grad_attn = jnp.where(
            dp_index == 0,
            jnp.concatenate([mine_part, other_part], axis=1),
            jnp.concatenate([other_part, mine_part], axis=1),
        )

        def project(rows):
            own = jnp.dot(
                columns(rows, dp_index, rows_half), w_qkv, preferred_element_type=jnp.float32
            )
            other = jnp.dot(
                columns(rows, 1 - dp_index, rows_half), qkv_other, preferred_element_type=jnp.float32
            )
            return (own + other).astype(jnp.bfloat16)

        def back_project(grad_proj):
            own = lax.dot_general(grad_proj, w_qkv, TRANS_B, preferred_element_type=jnp.float32)
            other = lax.dot_general(grad_proj, qkv_other, TRANS_B, preferred_element_type=jnp.float32)
            own = own.astype(jnp.bfloat16)
            other = other.astype(jnp.bfloat16)
            return jnp.where(
                dp_index == 0,
                jnp.concatenate([own, other], axis=1),
                jnp.concatenate([other, own], axis=1),
            )
    else:
        panels = lax.all_gather(w_qkv, "dp", axis=0, tiled=True)
        cot_blocks = flat_grad.reshape(token_count, lon_count, cols_block).transpose(1, 0, 2)
        cot_lon = exchange_blocks(cot_blocks, "lon")
        cot_group = gather_members(cot_lon, "dp").reshape(-1, cols_block)
        grad_attn = partner_rows_product(flat_grad, w_out, "dp")


        def project(rows):
            out = jnp.dot(rows, panels, preferred_element_type=jnp.float32)
            return out.astype(jnp.bfloat16)

        def back_project(grad_proj):
            out = lax.dot_general(grad_proj, panels, TRANS_B, preferred_element_type=jnp.float32)
            return out.astype(jnp.bfloat16)

    tok_ext = halo_gather(inputs_here, radius)
    tok_ext = jnp.pad(tok_ext, ((0, 0), (0, pad_cols - ext_cols), (0, 0)))
    tok_ext = tok_ext.reshape(key_count, width)

    projected = project(tok_ext)
    query = projected.reshape(ext_rows, pad_cols, 3 * width)[
        radius : radius + height, radius : radius + breadth, :width
    ].reshape(token_count, width)

    wrapped = jnp.concatenate(
        [valid_cells[:, -radius:], valid_cells, valid_cells[:, :radius]], axis=1
    )
    framed = jnp.pad(wrapped, ((radius, radius), (0, 0)))
    valid_ext = lax.dynamic_slice(
        framed,
        (lax.axis_index("lat") * height, lon_index * breadth),
        (ext_rows, ext_cols),
    )
    valid_ext = jnp.pad(valid_ext, ((0, 0), (0, pad_cols - ext_cols))).reshape(1, key_count)
    query_pos = jnp.arange(token_count)
    key_pos = jnp.arange(key_count)
    delta_row = (key_pos // pad_cols)[None, :] - radius - (query_pos // breadth)[:, None]
    delta_col = (key_pos % pad_cols)[None, :] - radius - (query_pos % breadth)[:, None]
    inside = (jnp.abs(delta_row) <= radius) & (jnp.abs(delta_col) <= radius)
    itself = (delta_row == 0) & (delta_col == 0)
    allowed = inside & ((valid_ext == 1) | itself)
    bias = jnp.where(allowed, 0.0, -jnp.inf).astype(jnp.float32)

    attended, grad_query, grad_kv, grad_kv_low = block_attention(
        query, projected, grad_attn, bias, HEADS
    )

    grad_kv_ext = grad_kv.reshape(2, ext_rows, pad_cols, width)[:, :, :ext_cols]
    grad_kv_low_ext = grad_kv_low.reshape(2, ext_rows, pad_cols, width)[:, :, :ext_cols]

    att_fits = (2 * token_count * rows_half) % (2 * height * width) == 0
    if fast and att_fits:
        own_att = columns(attended, dp_index, rows_half)
        att_from_dp = swap(columns(attended, 1 - dp_index, rows_half), "dp")
        att_dp = jnp.concatenate([own_att, att_from_dp], axis=0)
        carried = att_dp.reshape(2, height, -1, width)
        grad_kv_own, att_lon = halo_return(
            grad_kv_ext, grad_kv_low_ext, height, breadth, radius, carried
        )
        att_group = jnp.concatenate([att_dp, att_lon.reshape(att_dp.shape)], axis=0)
    else:
        grad_kv_own, _ = halo_return(grad_kv_ext, grad_kv_low_ext, height, breadth, radius)
        if fast:
            own_att = columns(attended, dp_index, rows_half)
            att_from_dp = swap(columns(attended, 1 - dp_index, rows_half), "dp")
            att_dp = jnp.concatenate([own_att, att_from_dp], axis=0)
            att_group = jnp.concatenate([att_dp, swap(att_dp, "lon")], axis=0)
        else:
            att_blocks = attended.reshape(token_count, dp_count, rows_half).transpose(1, 0, 2)
            att_dp = exchange_blocks(att_blocks, "dp")
            att_group = gather_members(att_dp, "lon")
            att_group = att_group.transpose(1, 0, 2, 3).reshape(-1, rows_half)

    device_count = dp_count * lat_count * lon_count
    partial = lax.dot_general(
        att_group, cot_group, (((0,), (0,)), ((), ())), preferred_element_type=jnp.float32
    ) * (1.0 / device_count)
    spread = lax.all_to_all(partial.astype(jnp.bfloat16), "lat", 0, 0, tiled=True)
    d_w_out = spread.astype(jnp.float32).reshape(lat_count, rows_block, cols_block).sum(axis=0)

    grad_kv_own = grad_kv_own.astype(jnp.bfloat16).reshape(2, token_count, width)
    grad_proj = jnp.concatenate([grad_query, grad_kv_own[0], grad_kv_own[1]], axis=1)
    d_input = back_project(grad_proj).reshape(1, height, breadth, width)
    return (d_input, d_w_out)


def solution(mesh):
    in_specs = (
        P("dp", "lat", "lon", None),
        P("dp", "lat", "lon", None),
        P(),
        P("dp", None),
        P("dp", None),
    )
    out_specs = (P("dp", "lat", "lon", None), P(("dp", "lat"), "lon"))
    return jax.shard_map(shards, mesh=mesh, in_specs=in_specs, out_specs=out_specs, check_vma=False)
```

```python
import functools

import jax
import jax.numpy as jnp
from jax import lax
from jax.experimental import pallas as pl
from jax.sharding import PartitionSpec as P

HEADS = 16
RADIUS = 6

TRANS_B = (((1,), (1,)), ((), ()))


def passed_along(value, axis, steps):
    count = lax.axis_size(axis)
    pairs = [(source, (source + steps) % count) for source in range(count)]
    return lax.ppermute(value, axis, pairs)


def shifted(value, axis, by):
    count = lax.axis_size(axis)
    pairs = [(i, i + by) for i in range(count) if 0 <= i + by < count]
    return lax.ppermute(value, axis, pairs)


def extended(block, sides, width, periodic):
    for axis, dim in sides:
        count = lax.axis_size(axis)
        forward = [(i, i + 1) for i in range(count - 1)]
        if periodic:
            forward.append((count - 1, 0))
        backward = [(target, source) for source, target in forward]
        low = lax.ppermute(
            lax.slice_in_dim(block, block.shape[dim] - width, None, axis=dim), axis, forward
        )
        high = lax.ppermute(lax.slice_in_dim(block, 0, width, axis=dim), axis, backward)
        block = jnp.concatenate([low, block, high], axis=dim)
    return block


def pair_terms(q, k, v, g, bias, head_dim, scale):
    lanes = q.shape[1]
    lane = lax.broadcasted_iota(jnp.int32, (1, lanes), 1)
    zero = jnp.zeros((), q.dtype)
    sels = [(lane >= j * head_dim) & (lane < (j + 1) * head_dim) for j in range(lanes // head_dim)]
    q_scaled = (q.astype(jnp.float32) * scale).astype(q.dtype)
    g_scaled = (g.astype(jnp.float32) * scale).astype(g.dtype)
    probs_list = []
    grads_list = []
    for sel in sels:
        qj = jnp.where(sel, q_scaled, zero)
        gj = jnp.where(sel, g_scaled, zero)
        masked = lax.dot_general(qj, k, TRANS_B, preferred_element_type=jnp.float32) + bias
        peak = jnp.max(masked, axis=1, keepdims=True)
        weights = jnp.exp(masked - peak)
        probs = weights * (1.0 / jnp.sum(weights, axis=1, keepdims=True))
        grad_probs = lax.dot_general(gj, v, TRANS_B, preferred_element_type=jnp.float32)
        centre = jnp.sum(probs * grad_probs, axis=1, keepdims=True)
        grads_list.append((probs * (grad_probs - centre)).astype(jnp.bfloat16))
        probs_list.append(probs.astype(jnp.bfloat16))
    k_sel = jnp.concatenate([jnp.where(sel, k, zero) for sel in sels], axis=0)
    v_sel = jnp.concatenate([jnp.where(sel, v, zero) for sel in sels], axis=0)
    q_sel = jnp.concatenate([jnp.where(sel, q, zero) for sel in sels], axis=0)
    g_sel = jnp.concatenate([jnp.where(sel, g, zero) for sel in sels], axis=0)
    probs_cat = jnp.concatenate(probs_list, axis=1)
    grads_cat = jnp.concatenate(grads_list, axis=1)
    att = jnp.dot(probs_cat, v_sel, preferred_element_type=jnp.float32)
    gq = jnp.dot(grads_cat, k_sel, preferred_element_type=jnp.float32)
    grads_t = jnp.concatenate(
        [x.astype(jnp.float32).T.astype(jnp.bfloat16) for x in grads_list], axis=1
    )
    probs_t = jnp.concatenate(
        [x.astype(jnp.float32).T.astype(jnp.bfloat16) for x in probs_list], axis=1
    )
    grad_k = jnp.dot(grads_t, q_sel, preferred_element_type=jnp.float32)
    grad_v = jnp.dot(probs_t, g_sel, preferred_element_type=jnp.float32)
    return att, gq, grad_k, grad_v


def attention_kernel(q_ref, k_ref, v_ref, g_ref, bias_ref, att_ref, gq_ref, gkv_ref, gkv_low_ref,
                     *, head_dim, scale, lanes):
    bias = bias_ref[...]
    for sub in range(q_ref.shape[1] // lanes):
        cols = slice(sub * lanes, (sub + 1) * lanes)
        att, gq, grad_k, grad_v = pair_terms(
            q_ref[:, cols], k_ref[:, cols], v_ref[:, cols], g_ref[:, cols], bias, head_dim, scale
        )
        att_ref[:, cols] = att.astype(att_ref.dtype)
        gq_ref[:, cols] = gq.astype(gq_ref.dtype)
        gkv_ref[0, :, cols] = grad_k
        gkv_ref[1, :, cols] = grad_v
        gkv_low_ref[0, :, cols] = grad_k.astype(gkv_low_ref.dtype)
        gkv_low_ref[1, :, cols] = grad_v.astype(gkv_low_ref.dtype)


def block_attention(query, projected, grad_attn, bias, heads):
    queries, width = query.shape
    keys = projected.shape[0]
    head_dim = width // heads
    lanes = 512
    pairs = width // lanes
    kernel = functools.partial(
        attention_kernel, head_dim=head_dim, scale=head_dim ** (-0.5), lanes=128
    )
    flops = 2 * queries * keys * width * 2 * 6
    cost = pl.CostEstimate(
        flops=flops,
        transcendentals=queries * keys * heads,
        bytes_accessed=2 * (2 * queries * width + 2 * keys * width + 2 * queries * width)
        + 4 * queries * keys + 4 * 2 * keys * width,
    )
    return pl.pallas_call(
        kernel,
        grid=(pairs,),
        in_specs=[
            pl.BlockSpec((queries, lanes), lambda h: (0, h)),
            pl.BlockSpec((keys, lanes), lambda h: (0, h + pairs)),
            pl.BlockSpec((keys, lanes), lambda h: (0, h + 2 * pairs)),
            pl.BlockSpec((queries, lanes), lambda h: (0, h)),
            pl.BlockSpec((queries, keys), lambda h: (0, 0)),
        ],
        out_specs=[
            pl.BlockSpec((queries, lanes), lambda h: (0, h)),
            pl.BlockSpec((queries, lanes), lambda h: (0, h)),
            pl.BlockSpec((2, keys, lanes), lambda h: (0, 0, h)),
            pl.BlockSpec((2, keys, lanes), lambda h: (0, 0, h)),
        ],
        out_shape=[
            jax.ShapeDtypeStruct((queries, width), jnp.bfloat16),
            jax.ShapeDtypeStruct((queries, width), jnp.bfloat16),
            jax.ShapeDtypeStruct((2, keys, width), jnp.float32),
            jax.ShapeDtypeStruct((2, keys, width), jnp.bfloat16),
        ],
        cost_estimate=cost,
        name="block_attention",
    )(query, projected, projected, grad_attn, bias)


def grid_pairs(delta_lat, delta_lon):
    lat_count = lax.axis_size("lat")
    lon_count = lax.axis_size("lon")
    pairs = []
    for la in range(lat_count):
        if 0 <= la + delta_lat < lat_count:
            for lo in range(lon_count):
                target = (la + delta_lat) * lon_count + (lo + delta_lon) % lon_count
                pairs.append((la * lon_count + lo, target))
    return pairs


def sent_to(value, delta_lat, delta_lon):
    return lax.ppermute(value, ("lat", "lon"), grid_pairs(delta_lat, delta_lon))


def part(count, radius, step, giving):
    if step == 0:
        return slice(0, count)
    if (step < 0) == giving:
        return slice(count - radius, count)
    return slice(0, radius)


def grouped_send(pieces, axis):
    lon_count = lax.axis_size("lon")
    groups = {}
    for index, (dl, db, value) in enumerate(pieces):
        groups.setdefault((dl, db % lon_count), []).append(index)
    out = [None] * len(pieces)
    for (dl, db), members in groups.items():
        values = [pieces[i][2] for i in members]
        got = sent_to(jnp.concatenate(values, axis=axis), dl, db)
        offset = 0
        for i, value in zip(members, values):
            out[i] = lax.slice_in_dim(got, offset, offset + value.shape[axis], axis=axis)
            offset += value.shape[axis]
    return out


def halo_gather(block, radius):
    height, breadth, lanes = block.shape
    spots = []
    pieces = []
    for da in (-1, 0, 1):
        for db in (-1, 0, 1):
            if da == 0 and db == 0:
                continue
            piece = block[part(height, radius, da, True), part(breadth, radius, db, True)]
            spots.append((da, db))
            pieces.append((-da, -db, piece))
    got = dict(zip(spots, grouped_send(pieces, 1)))
    got[(0, 0)] = block
    rows = [jnp.concatenate([got[(da, db)] for db in (-1, 0, 1)], axis=1) for da in (-1, 0, 1)]
    return jnp.concatenate(rows, axis=0)


def halo_return(ext, ext_low, height, breadth, radius, extra=None):
    row_slices = {-1: slice(0, radius), 0: slice(radius, radius + height), 1: slice(radius + height, None)}
    col_slices = {-1: slice(0, radius), 0: slice(radius, radius + breadth), 1: slice(radius + breadth, None)}
    own = ext[:, row_slices[0], col_slices[0]]
    spots = []
    pieces = []
    for da in (-1, 0, 1):
        for db in (-1, 0, 1):
            if da == 0 and db == 0:
                continue
            spots.append((da, db))
            pieces.append((da, db, ext_low[:, row_slices[da], col_slices[db]]))
    if extra is not None:
        spots.append(None)
        pieces.append((0, 1, extra))
    received = grouped_send(pieces, 2)
    extra_got = received[-1] if extra is not None else None
    for spot, got in zip(spots, received):
        if spot is None:
            continue
        da, db = spot
        rs = part(height, radius, da, True)
        cs = part(breadth, radius, db, True)
        pad_rows = (rs.start, height - rs.stop)
        pad_cols = (cs.start, breadth - cs.stop)
        own = own + jnp.pad(got.astype(jnp.float32), ((0, 0), pad_rows, pad_cols, (0, 0)))
    return own, extra_got


def partner_rows_product(lhs, weights, axis):
    count = lax.axis_size(axis)
    if count != 2:
        full = lax.all_gather(weights, axis, axis=0, tiled=True)
        return lax.dot_general(lhs, full, TRANS_B, preferred_element_type=jnp.float32).astype(
            jnp.bfloat16
        )
    other = lax.ppermute(weights, axis, [(0, 1), (1, 0)])
    mine_part = lax.dot_general(lhs, weights, TRANS_B, preferred_element_type=jnp.float32)
    other_part = lax.dot_general(lhs, other, TRANS_B, preferred_element_type=jnp.float32)
    mine_part = mine_part.astype(jnp.bfloat16)
    other_part = other_part.astype(jnp.bfloat16)
    first = lax.axis_index(axis) == 0
    return jnp.where(
        first,
        jnp.concatenate([mine_part, other_part], axis=1),
        jnp.concatenate([other_part, mine_part], axis=1),
    )


def exchange_blocks(blocks, axis):
    count = lax.axis_size(axis)
    if count == 2:
        me = lax.axis_index(axis)
        mine = lax.dynamic_index_in_dim(blocks, me, 0, keepdims=False)
        theirs = lax.dynamic_index_in_dim(blocks, 1 - me, 0, keepdims=False)
        got = lax.ppermute(theirs, axis, [(0, 1), (1, 0)])
        return jnp.where(me == 0, jnp.stack([mine, got]), jnp.stack([got, mine]))
    flat = blocks.reshape((-1,) + blocks.shape[2:])
    out = lax.all_to_all(flat, axis, 0, 0, tiled=True)
    return out.reshape(blocks.shape)


def gather_members(value, axis):
    count = lax.axis_size(axis)
    if count == 2:
        me = lax.axis_index(axis)
        got = lax.ppermute(value, axis, [(0, 1), (1, 0)])
        return jnp.where(me == 0, jnp.stack([value, got]), jnp.stack([got, value]))
    return lax.all_gather(value, axis, axis=0, tiled=False)


def swap(value, axis):
    return lax.ppermute(value, axis, [(0, 1), (1, 0)])


def columns(value, index, size):
    return lax.dynamic_slice_in_dim(value, index * size, size, axis=1)


def split_rows(joined, shapes):
    out = []
    offset = 0
    for shape in shapes:
        count = 1
        for extent in shape[:-1]:
            count *= extent
        count = count * shape[-1] // joined.shape[-1]
        out.append(joined[offset : offset + count].reshape(shape))
        offset += count
    return out


def join_rows(parts, lanes):
    return jnp.concatenate([p.reshape(-1, lanes) for p in parts], axis=0)


def lat_return(ext_list, height, radius):
    owns = []
    tops = join_rows([ext[:radius] for ext in ext_list], ext_list[0].shape[-1])
    bottoms = join_rows([ext[radius + height :] for ext in ext_list], ext_list[0].shape[-1])
    shapes = [ext[:radius].shape for ext in ext_list]
    from_below = split_rows(shifted(tops.astype(jnp.bfloat16), "lat", -1), shapes)
    from_above = split_rows(shifted(bottoms.astype(jnp.bfloat16), "lat", 1), shapes)
    for ext, below, above in zip(ext_list, from_below, from_above):
        middle = (
            ext[radius : radius + height]
            + jnp.pad(below.astype(jnp.float32), ((height - radius, 0), (0, 0), (0, 0)))
            + jnp.pad(above.astype(jnp.float32), ((0, height - radius), (0, 0), (0, 0)))
        )
        owns.append(middle)
    return owns


def add_lon_rims(mid_list, from_right, from_left, breadth, radius):
    owns = []
    for mid, right, left in zip(mid_list, from_right, from_left):
        owns.append(
            mid[:, radius : radius + breadth]
            + jnp.pad(right.astype(jnp.float32), ((0, 0), (breadth - radius, 0), (0, 0)))
            + jnp.pad(left.astype(jnp.float32), ((0, 0), (0, breadth - radius), (0, 0)))
        )
    return owns


def shards(tokens, cotangent, valid_cells, w_qkv, w_out):
    inputs_here = tokens[0]
    grad_here = cotangent[0]
    height, breadth, width = inputs_here.shape
    radius = RADIUS
    ext_rows = height + 2 * radius
    ext_cols = breadth + 2 * radius
    pad_cols = -(-ext_cols // 8) * 8
    token_count = height * breadth
    key_count = ext_rows * pad_cols
    flat_inputs = inputs_here.reshape(token_count, width)
    flat_grad = grad_here.reshape(token_count, width)
    dp_count = lax.axis_size("dp")
    lat_count = lax.axis_size("lat")
    lon_count = lax.axis_size("lon")
    rows_half = width // dp_count
    cols_block = width // lon_count
    rows_block = rows_half // lat_count
    dp_index = lax.axis_index("dp")
    lon_index = lax.axis_index("lon")
    fast = dp_count == 2 and lon_count == 2

    if fast:
        qkv_other = swap(w_qkv, "dp")
        dp_got = swap(jnp.concatenate([w_out, flat_grad], axis=0), "dp")
        w_out_other = dp_got[: w_out.shape[0]]
        cot_dp = dp_got[w_out.shape[0] :]
        cot_send = jnp.concatenate(
            [columns(flat_grad, 1 - lon_index, cols_block), columns(cot_dp, 1 - lon_index, cols_block)],
            axis=0,
        )
        cot_lon = swap(cot_send, "lon")
        cot_group = jnp.concatenate(
            [
                columns(flat_grad, lon_index, cols_block),
                columns(cot_dp, lon_index, cols_block),
                cot_lon,
            ],
            axis=0,
        )
        mine_part = lax.dot_general(flat_grad, w_out, TRANS_B, preferred_element_type=jnp.float32)
        other_part = lax.dot_general(
            flat_grad, w_out_other, TRANS_B, preferred_element_type=jnp.float32
        )
        mine_part = mine_part.astype(jnp.bfloat16)
        other_part = other_part.astype(jnp.bfloat16)
        grad_attn = jnp.where(
            dp_index == 0,
            jnp.concatenate([mine_part, other_part], axis=1),
            jnp.concatenate([other_part, mine_part], axis=1),
        )

        def project(rows):
            own = jnp.dot(
                columns(rows, dp_index, rows_half), w_qkv, preferred_element_type=jnp.float32
            )
            other = jnp.dot(
                columns(rows, 1 - dp_index, rows_half), qkv_other, preferred_element_type=jnp.float32
            )
            return (own + other).astype(jnp.bfloat16)

        def back_project(grad_proj):
            own = lax.dot_general(grad_proj, w_qkv, TRANS_B, preferred_element_type=jnp.float32)
            other = lax.dot_general(grad_proj, qkv_other, TRANS_B, preferred_element_type=jnp.float32)
            own = own.astype(jnp.bfloat16)
            other = other.astype(jnp.bfloat16)
            return jnp.where(
                dp_index == 0,
                jnp.concatenate([own, other], axis=1),
                jnp.concatenate([other, own], axis=1),
            )
    else:
        panels = lax.all_gather(w_qkv, "dp", axis=0, tiled=True)
        cot_blocks = flat_grad.reshape(token_count, lon_count, cols_block).transpose(1, 0, 2)
        cot_lon = exchange_blocks(cot_blocks, "lon")
        cot_group = gather_members(cot_lon, "dp").reshape(-1, cols_block)
        grad_attn = partner_rows_product(flat_grad, w_out, "dp")


        def project(rows):
            out = jnp.dot(rows, panels, preferred_element_type=jnp.float32)
            return out.astype(jnp.bfloat16)

        def back_project(grad_proj):
            out = lax.dot_general(grad_proj, panels, TRANS_B, preferred_element_type=jnp.float32)
            return out.astype(jnp.bfloat16)

    tok_ext = halo_gather(inputs_here, radius)
    tok_ext = jnp.pad(tok_ext, ((0, 0), (0, pad_cols - ext_cols), (0, 0)))
    tok_ext = tok_ext.reshape(key_count, width)

    projected = project(tok_ext)
    query = projected.reshape(ext_rows, pad_cols, 3 * width)[
        radius : radius + height, radius : radius + breadth, :width
    ].reshape(token_count, width)

    wrapped = jnp.concatenate(
        [valid_cells[:, -radius:], valid_cells, valid_cells[:, :radius]], axis=1
    )
    framed = jnp.pad(wrapped, ((radius, radius), (0, 0)))
    valid_ext = lax.dynamic_slice(
        framed,
        (lax.axis_index("lat") * height, lon_index * breadth),
        (ext_rows, ext_cols),
    )
    valid_ext = jnp.pad(valid_ext, ((0, 0), (0, pad_cols - ext_cols))).reshape(1, key_count)
    query_pos = jnp.arange(token_count)
    key_pos = jnp.arange(key_count)
    delta_row = (key_pos // pad_cols)[None, :] - radius - (query_pos // breadth)[:, None]
    delta_col = (key_pos % pad_cols)[None, :] - radius - (query_pos % breadth)[:, None]
    inside = (jnp.abs(delta_row) <= radius) & (jnp.abs(delta_col) <= radius)
    itself = (delta_row == 0) & (delta_col == 0)
    allowed = inside & ((valid_ext == 1) | itself)
    bias = jnp.where(allowed, 0.0, -jnp.inf).astype(jnp.float32)

    attended, grad_query, grad_kv, grad_kv_low = block_attention(
        query, projected, grad_attn, bias, HEADS
    )

    grad_kv_ext = grad_kv.reshape(2, ext_rows, pad_cols, width)[:, :, :ext_cols]
    grad_kv_low_ext = grad_kv_low.reshape(2, ext_rows, pad_cols, width)[:, :, :ext_cols]

    att_fits = (2 * token_count * rows_half) % (2 * height * width) == 0
    if fast and att_fits:
        own_att = columns(attended, dp_index, rows_half)
        att_from_dp = swap(columns(attended, 1 - dp_index, rows_half), "dp")
        att_dp = jnp.concatenate([own_att, att_from_dp], axis=0)
        carried = att_dp.reshape(2, height, -1, width)
        grad_kv_own, att_lon = halo_return(
            grad_kv_ext, grad_kv_low_ext, height, breadth, radius, carried
        )
        att_group = jnp.concatenate([att_dp, att_lon.reshape(att_dp.shape)], axis=0)
    else:
        grad_kv_own, _ = halo_return(grad_kv_ext, grad_kv_low_ext, height, breadth, radius)
        if fast:
            own_att = columns(attended, dp_index, rows_half)
            att_from_dp = swap(columns(attended, 1 - dp_index, rows_half), "dp")
            att_dp = jnp.concatenate([own_att, att_from_dp], axis=0)
            att_group = jnp.concatenate([att_dp, swap(att_dp, "lon")], axis=0)
        else:
            att_blocks = attended.reshape(token_count, dp_count, rows_half).transpose(1, 0, 2)
            att_dp = exchange_blocks(att_blocks, "dp")
            att_group = gather_members(att_dp, "lon")
            att_group = att_group.transpose(1, 0, 2, 3).reshape(-1, rows_half)

    device_count = dp_count * lat_count * lon_count
    partial = lax.dot_general(
        att_group, cot_group, (((0,), (0,)), ((), ())), preferred_element_type=jnp.float32
    ) * (1.0 / device_count)
    spread = lax.all_to_all(partial.astype(jnp.bfloat16), "lat", 0, 0, tiled=True)
    d_w_out = spread.astype(jnp.float32).reshape(lat_count, rows_block, cols_block).sum(axis=0)

    grad_kv_own = grad_kv_own.astype(jnp.bfloat16).reshape(2, token_count, width)
    grad_proj = jnp.concatenate([grad_query, grad_kv_own[0], grad_kv_own[1]], axis=1)
    d_input = back_project(grad_proj).reshape(1, height, breadth, width)
    return (d_input, d_w_out)


def solution(mesh):
    in_specs = (
        P("dp", "lat", "lon", None),
        P("dp", "lat", "lon", None),
        P(),
        P("dp", None),
        P("dp", None),
    )
    out_specs = (P("dp", "lat", "lon", None), P(("dp", "lat"), "lon"))
    return jax.shard_map(shards, mesh=mesh, in_specs=in_specs, out_specs=out_specs, check_vma=False)
```

```python
import functools

import jax
import jax.numpy as jnp
from jax import lax
from jax.experimental import pallas as pl
from jax.sharding import PartitionSpec as P

HEADS = 16
RADIUS = 6

TRANS_B = (((1,), (1,)), ((), ()))


def passed_along(value, axis, steps):
    count = lax.axis_size(axis)
    pairs = [(source, (source + steps) % count) for source in range(count)]
    return lax.ppermute(value, axis, pairs)


def shifted(value, axis, by):
    count = lax.axis_size(axis)
    pairs = [(i, i + by) for i in range(count) if 0 <= i + by < count]
    return lax.ppermute(value, axis, pairs)


def extended(block, sides, width, periodic):
    for axis, dim in sides:
        count = lax.axis_size(axis)
        forward = [(i, i + 1) for i in range(count - 1)]
        if periodic:
            forward.append((count - 1, 0))
        backward = [(target, source) for source, target in forward]
        low = lax.ppermute(
            lax.slice_in_dim(block, block.shape[dim] - width, None, axis=dim), axis, forward
        )
        high = lax.ppermute(lax.slice_in_dim(block, 0, width, axis=dim), axis, backward)
        block = jnp.concatenate([low, block, high], axis=dim)
    return block


def pair_terms(q, k, v, g, bias, head_dim, scale):
    lanes = q.shape[1]
    lane = lax.broadcasted_iota(jnp.int32, (1, lanes), 1)
    zero = jnp.zeros((), q.dtype)
    sels = [(lane >= j * head_dim) & (lane < (j + 1) * head_dim) for j in range(lanes // head_dim)]
    q_scaled = (q.astype(jnp.float32) * scale).astype(q.dtype)
    g_scaled = (g.astype(jnp.float32) * scale).astype(g.dtype)
    probs_list = []
    grads_list = []
    for sel in sels:
        qj = jnp.where(sel, q_scaled, zero)
        gj = jnp.where(sel, g_scaled, zero)
        masked = lax.dot_general(qj, k, TRANS_B, preferred_element_type=jnp.float32) + bias
        peak = jnp.max(masked, axis=1, keepdims=True)
        weights = jnp.exp(masked - peak)
        probs = weights * (1.0 / jnp.sum(weights, axis=1, keepdims=True))
        grad_probs = lax.dot_general(gj, v, TRANS_B, preferred_element_type=jnp.float32)
        centre = jnp.sum(probs * grad_probs, axis=1, keepdims=True)
        grads_list.append((probs * (grad_probs - centre)).astype(jnp.bfloat16))
        probs_list.append(probs.astype(jnp.bfloat16))
    k_sel = jnp.concatenate([jnp.where(sel, k, zero) for sel in sels], axis=0)
    v_sel = jnp.concatenate([jnp.where(sel, v, zero) for sel in sels], axis=0)
    q_sel = jnp.concatenate([jnp.where(sel, q, zero) for sel in sels], axis=0)
    g_sel = jnp.concatenate([jnp.where(sel, g, zero) for sel in sels], axis=0)
    probs_cat = jnp.concatenate(probs_list, axis=1)
    grads_cat = jnp.concatenate(grads_list, axis=1)
    att = jnp.dot(probs_cat, v_sel, preferred_element_type=jnp.float32)
    gq = jnp.dot(grads_cat, k_sel, preferred_element_type=jnp.float32)
    grads_t = jnp.concatenate(
        [x.astype(jnp.float32).T.astype(jnp.bfloat16) for x in grads_list], axis=1
    )
    probs_t = jnp.concatenate(
        [x.astype(jnp.float32).T.astype(jnp.bfloat16) for x in probs_list], axis=1
    )
    grad_k = jnp.dot(grads_t, q_sel, preferred_element_type=jnp.float32)
    grad_v = jnp.dot(probs_t, g_sel, preferred_element_type=jnp.float32)
    return att, gq, grad_k, grad_v


def attention_kernel(q_ref, k_ref, v_ref, g_ref, bias_ref, att_ref, gq_ref, gkv_ref, gkv_low_ref,
                     *, head_dim, scale, lanes):
    bias = bias_ref[...].astype(jnp.float32)
    for sub in range(q_ref.shape[1] // lanes):
        cols = slice(sub * lanes, (sub + 1) * lanes)
        att, gq, grad_k, grad_v = pair_terms(
            q_ref[:, cols], k_ref[:, cols], v_ref[:, cols], g_ref[:, cols], bias, head_dim, scale
        )
        att_ref[:, cols] = att.astype(att_ref.dtype)
        gq_ref[:, cols] = gq.astype(gq_ref.dtype)
        gkv_ref[0, :, cols] = grad_k
        gkv_ref[1, :, cols] = grad_v
        gkv_low_ref[0, :, cols] = grad_k.astype(gkv_low_ref.dtype)
        gkv_low_ref[1, :, cols] = grad_v.astype(gkv_low_ref.dtype)


def block_attention(query, projected, grad_attn, bias, heads):
    queries, width = query.shape
    keys = projected.shape[0]
    head_dim = width // heads
    lanes = 256
    pairs = width // lanes
    kernel = functools.partial(
        attention_kernel, head_dim=head_dim, scale=head_dim ** (-0.5), lanes=128
    )
    flops = 2 * queries * keys * width * 2 * 6
    cost = pl.CostEstimate(
        flops=flops,
        transcendentals=queries * keys * heads,
        bytes_accessed=2 * (2 * queries * width + 2 * keys * width + 2 * queries * width)
        + 4 * queries * keys + 4 * 2 * keys * width,
    )
    return pl.pallas_call(
        kernel,
        grid=(pairs,),
        in_specs=[
            pl.BlockSpec((queries, lanes), lambda h: (0, h)),
            pl.BlockSpec((keys, lanes), lambda h: (0, h + pairs)),
            pl.BlockSpec((keys, lanes), lambda h: (0, h + 2 * pairs)),
            pl.BlockSpec((queries, lanes), lambda h: (0, h)),
            pl.BlockSpec((queries, keys), lambda h: (0, 0)),
        ],
        out_specs=[
            pl.BlockSpec((queries, lanes), lambda h: (0, h)),
            pl.BlockSpec((queries, lanes), lambda h: (0, h)),
            pl.BlockSpec((2, keys, lanes), lambda h: (0, 0, h)),
            pl.BlockSpec((2, keys, lanes), lambda h: (0, 0, h)),
        ],
        out_shape=[
            jax.ShapeDtypeStruct((queries, width), jnp.bfloat16),
            jax.ShapeDtypeStruct((queries, width), jnp.bfloat16),
            jax.ShapeDtypeStruct((2, keys, width), jnp.float32),
            jax.ShapeDtypeStruct((2, keys, width), jnp.bfloat16),
        ],
        cost_estimate=cost,
        name="block_attention",
    )(query, projected, projected, grad_attn, bias)


def grid_pairs(delta_lat, delta_lon):
    lat_count = lax.axis_size("lat")
    lon_count = lax.axis_size("lon")
    pairs = []
    for la in range(lat_count):
        if 0 <= la + delta_lat < lat_count:
            for lo in range(lon_count):
                target = (la + delta_lat) * lon_count + (lo + delta_lon) % lon_count
                pairs.append((la * lon_count + lo, target))
    return pairs


def sent_to(value, delta_lat, delta_lon):
    return lax.ppermute(value, ("lat", "lon"), grid_pairs(delta_lat, delta_lon))


def part(count, radius, step, giving):
    if step == 0:
        return slice(0, count)
    if (step < 0) == giving:
        return slice(count - radius, count)
    return slice(0, radius)


def grouped_send(pieces, axis):
    lon_count = lax.axis_size("lon")
    groups = {}
    for index, (dl, db, value) in enumerate(pieces):
        groups.setdefault((dl, db % lon_count), []).append(index)
    out = [None] * len(pieces)
    for (dl, db), members in groups.items():
        values = [pieces[i][2] for i in members]
        got = sent_to(jnp.concatenate(values, axis=axis), dl, db)
        offset = 0
        for i, value in zip(members, values):
            out[i] = lax.slice_in_dim(got, offset, offset + value.shape[axis], axis=axis)
            offset += value.shape[axis]
    return out


def halo_gather(block, radius):
    height, breadth, lanes = block.shape
    spots = []
    pieces = []
    for da in (-1, 0, 1):
        for db in (-1, 0, 1):
            if da == 0 and db == 0:
                continue
            piece = block[part(height, radius, da, True), part(breadth, radius, db, True)]
            spots.append((da, db))
            pieces.append((-da, -db, piece))
    got = dict(zip(spots, grouped_send(pieces, 1)))
    got[(0, 0)] = block
    rows = [jnp.concatenate([got[(da, db)] for db in (-1, 0, 1)], axis=1) for da in (-1, 0, 1)]
    return jnp.concatenate(rows, axis=0)


def halo_return(ext, ext_low, height, breadth, radius, extra=None):
    row_slices = {-1: slice(0, radius), 0: slice(radius, radius + height), 1: slice(radius + height, None)}
    col_slices = {-1: slice(0, radius), 0: slice(radius, radius + breadth), 1: slice(radius + breadth, None)}
    own = ext[:, row_slices[0], col_slices[0]]
    spots = []
    pieces = []
    for da in (-1, 0, 1):
        for db in (-1, 0, 1):
            if da == 0 and db == 0:
                continue
            spots.append((da, db))
            pieces.append((da, db, ext_low[:, row_slices[da], col_slices[db]]))
    if extra is not None:
        spots.append(None)
        pieces.append((0, 1, extra))
    received = grouped_send(pieces, 2)
    extra_got = received[-1] if extra is not None else None
    for spot, got in zip(spots, received):
        if spot is None:
            continue
        da, db = spot
        rs = part(height, radius, da, True)
        cs = part(breadth, radius, db, True)
        pad_rows = (rs.start, height - rs.stop)
        pad_cols = (cs.start, breadth - cs.stop)
        own = own + jnp.pad(got.astype(jnp.float32), ((0, 0), pad_rows, pad_cols, (0, 0)))
    return own, extra_got


def partner_rows_product(lhs, weights, axis):
    count = lax.axis_size(axis)
    if count != 2:
        full = lax.all_gather(weights, axis, axis=0, tiled=True)
        return lax.dot_general(lhs, full, TRANS_B, preferred_element_type=jnp.float32).astype(
            jnp.bfloat16
        )
    other = lax.ppermute(weights, axis, [(0, 1), (1, 0)])
    mine_part = lax.dot_general(lhs, weights, TRANS_B, preferred_element_type=jnp.float32)
    other_part = lax.dot_general(lhs, other, TRANS_B, preferred_element_type=jnp.float32)
    mine_part = mine_part.astype(jnp.bfloat16)
    other_part = other_part.astype(jnp.bfloat16)
    first = lax.axis_index(axis) == 0
    return jnp.where(
        first,
        jnp.concatenate([mine_part, other_part], axis=1),
        jnp.concatenate([other_part, mine_part], axis=1),
    )


def exchange_blocks(blocks, axis):
    count = lax.axis_size(axis)
    if count == 2:
        me = lax.axis_index(axis)
        mine = lax.dynamic_index_in_dim(blocks, me, 0, keepdims=False)
        theirs = lax.dynamic_index_in_dim(blocks, 1 - me, 0, keepdims=False)
        got = lax.ppermute(theirs, axis, [(0, 1), (1, 0)])
        return jnp.where(me == 0, jnp.stack([mine, got]), jnp.stack([got, mine]))
    flat = blocks.reshape((-1,) + blocks.shape[2:])
    out = lax.all_to_all(flat, axis, 0, 0, tiled=True)
    return out.reshape(blocks.shape)


def gather_members(value, axis):
    count = lax.axis_size(axis)
    if count == 2:
        me = lax.axis_index(axis)
        got = lax.ppermute(value, axis, [(0, 1), (1, 0)])
        return jnp.where(me == 0, jnp.stack([value, got]), jnp.stack([got, value]))
    return lax.all_gather(value, axis, axis=0, tiled=False)


def swap(value, axis):
    return lax.ppermute(value, axis, [(0, 1), (1, 0)])


def columns(value, index, size):
    return lax.dynamic_slice_in_dim(value, index * size, size, axis=1)


def split_rows(joined, shapes):
    out = []
    offset = 0
    for shape in shapes:
        count = 1
        for extent in shape[:-1]:
            count *= extent
        count = count * shape[-1] // joined.shape[-1]
        out.append(joined[offset : offset + count].reshape(shape))
        offset += count
    return out


def join_rows(parts, lanes):
    return jnp.concatenate([p.reshape(-1, lanes) for p in parts], axis=0)


def lat_return(ext_list, height, radius):
    owns = []
    tops = join_rows([ext[:radius] for ext in ext_list], ext_list[0].shape[-1])
    bottoms = join_rows([ext[radius + height :] for ext in ext_list], ext_list[0].shape[-1])
    shapes = [ext[:radius].shape for ext in ext_list]
    from_below = split_rows(shifted(tops.astype(jnp.bfloat16), "lat", -1), shapes)
    from_above = split_rows(shifted(bottoms.astype(jnp.bfloat16), "lat", 1), shapes)
    for ext, below, above in zip(ext_list, from_below, from_above):
        middle = (
            ext[radius : radius + height]
            + jnp.pad(below.astype(jnp.float32), ((height - radius, 0), (0, 0), (0, 0)))
            + jnp.pad(above.astype(jnp.float32), ((0, height - radius), (0, 0), (0, 0)))
        )
        owns.append(middle)
    return owns


def add_lon_rims(mid_list, from_right, from_left, breadth, radius):
    owns = []
    for mid, right, left in zip(mid_list, from_right, from_left):
        owns.append(
            mid[:, radius : radius + breadth]
            + jnp.pad(right.astype(jnp.float32), ((0, 0), (breadth - radius, 0), (0, 0)))
            + jnp.pad(left.astype(jnp.float32), ((0, 0), (0, breadth - radius), (0, 0)))
        )
    return owns


def shards(tokens, cotangent, valid_cells, w_qkv, w_out):
    inputs_here = tokens[0]
    grad_here = cotangent[0]
    height, breadth, width = inputs_here.shape
    radius = RADIUS
    ext_rows = height + 2 * radius
    ext_cols = breadth + 2 * radius
    pad_cols = -(-ext_cols // 8) * 8
    token_count = height * breadth
    key_count = ext_rows * pad_cols
    flat_inputs = inputs_here.reshape(token_count, width)
    flat_grad = grad_here.reshape(token_count, width)
    dp_count = lax.axis_size("dp")
    lat_count = lax.axis_size("lat")
    lon_count = lax.axis_size("lon")
    rows_half = width // dp_count
    cols_block = width // lon_count
    rows_block = rows_half // lat_count
    dp_index = lax.axis_index("dp")
    lon_index = lax.axis_index("lon")
    fast = dp_count == 2 and lon_count == 2

    if fast:
        qkv_other = swap(w_qkv, "dp")
        dp_got = swap(jnp.concatenate([w_out, flat_grad], axis=0), "dp")
        w_out_other = dp_got[: w_out.shape[0]]
        cot_dp = dp_got[w_out.shape[0] :]
        cot_send = jnp.concatenate(
            [columns(flat_grad, 1 - lon_index, cols_block), columns(cot_dp, 1 - lon_index, cols_block)],
            axis=0,
        )
        cot_lon = swap(cot_send, "lon")
        cot_group = jnp.concatenate(
            [
                columns(flat_grad, lon_index, cols_block),
                columns(cot_dp, lon_index, cols_block),
                cot_lon,
            ],
            axis=0,
        )
        mine_part = lax.dot_general(flat_grad, w_out, TRANS_B, preferred_element_type=jnp.float32)
        other_part = lax.dot_general(
            flat_grad, w_out_other, TRANS_B, preferred_element_type=jnp.float32
        )
        mine_part = mine_part.astype(jnp.bfloat16)
        other_part = other_part.astype(jnp.bfloat16)
        grad_attn = jnp.where(
            dp_index == 0,
            jnp.concatenate([mine_part, other_part], axis=1),
            jnp.concatenate([other_part, mine_part], axis=1),
        )

        def project(rows):
            own = jnp.dot(
                columns(rows, dp_index, rows_half), w_qkv, preferred_element_type=jnp.float32
            )
            other = jnp.dot(
                columns(rows, 1 - dp_index, rows_half), qkv_other, preferred_element_type=jnp.float32
            )
            return (own + other).astype(jnp.bfloat16)

        def back_project(grad_proj):
            own = lax.dot_general(grad_proj, w_qkv, TRANS_B, preferred_element_type=jnp.float32)
            other = lax.dot_general(grad_proj, qkv_other, TRANS_B, preferred_element_type=jnp.float32)
            own = own.astype(jnp.bfloat16)
            other = other.astype(jnp.bfloat16)
            return jnp.where(
                dp_index == 0,
                jnp.concatenate([own, other], axis=1),
                jnp.concatenate([other, own], axis=1),
            )
    else:
        panels = lax.all_gather(w_qkv, "dp", axis=0, tiled=True)
        cot_blocks = flat_grad.reshape(token_count, lon_count, cols_block).transpose(1, 0, 2)
        cot_lon = exchange_blocks(cot_blocks, "lon")
        cot_group = gather_members(cot_lon, "dp").reshape(-1, cols_block)
        grad_attn = partner_rows_product(flat_grad, w_out, "dp")


        def project(rows):
            out = jnp.dot(rows, panels, preferred_element_type=jnp.float32)
            return out.astype(jnp.bfloat16)

        def back_project(grad_proj):
            out = lax.dot_general(grad_proj, panels, TRANS_B, preferred_element_type=jnp.float32)
            return out.astype(jnp.bfloat16)

    tok_ext = halo_gather(inputs_here, radius)
    tok_ext = jnp.pad(tok_ext, ((0, 0), (0, pad_cols - ext_cols), (0, 0)))
    tok_ext = tok_ext.reshape(key_count, width)

    projected = project(tok_ext)
    query = projected.reshape(ext_rows, pad_cols, 3 * width)[
        radius : radius + height, radius : radius + breadth, :width
    ].reshape(token_count, width)

    wrapped = jnp.concatenate(
        [valid_cells[:, -radius:], valid_cells, valid_cells[:, :radius]], axis=1
    )
    framed = jnp.pad(wrapped, ((radius, radius), (0, 0)))
    valid_ext = lax.dynamic_slice(
        framed,
        (lax.axis_index("lat") * height, lon_index * breadth),
        (ext_rows, ext_cols),
    )
    valid_ext = jnp.pad(valid_ext, ((0, 0), (0, pad_cols - ext_cols))).reshape(1, key_count)
    query_pos = jnp.arange(token_count)
    key_pos = jnp.arange(key_count)
    delta_row = (key_pos // pad_cols)[None, :] - radius - (query_pos // breadth)[:, None]
    delta_col = (key_pos % pad_cols)[None, :] - radius - (query_pos % breadth)[:, None]
    inside = (jnp.abs(delta_row) <= radius) & (jnp.abs(delta_col) <= radius)
    itself = (delta_row == 0) & (delta_col == 0)
    allowed = inside & ((valid_ext == 1) | itself)
    bias = jnp.where(allowed, 0.0, -jnp.inf).astype(jnp.bfloat16)

    attended, grad_query, grad_kv, grad_kv_low = block_attention(
        query, projected, grad_attn, bias, HEADS
    )

    grad_kv_ext = grad_kv.reshape(2, ext_rows, pad_cols, width)[:, :, :ext_cols]
    grad_kv_low_ext = grad_kv_low.reshape(2, ext_rows, pad_cols, width)[:, :, :ext_cols]

    att_fits = (2 * token_count * rows_half) % (2 * height * width) == 0
    if fast and att_fits:
        own_att = columns(attended, dp_index, rows_half)
        att_from_dp = swap(columns(attended, 1 - dp_index, rows_half), "dp")
        att_dp = jnp.concatenate([own_att, att_from_dp], axis=0)
        carried = att_dp.reshape(2, height, -1, width)
        grad_kv_own, att_lon = halo_return(
            grad_kv_ext, grad_kv_low_ext, height, breadth, radius, carried
        )
        att_group = jnp.concatenate([att_dp, att_lon.reshape(att_dp.shape)], axis=0)
    else:
        grad_kv_own, _ = halo_return(grad_kv_ext, grad_kv_low_ext, height, breadth, radius)
        if fast:
            own_att = columns(attended, dp_index, rows_half)
            att_from_dp = swap(columns(attended, 1 - dp_index, rows_half), "dp")
            att_dp = jnp.concatenate([own_att, att_from_dp], axis=0)
            att_group = jnp.concatenate([att_dp, swap(att_dp, "lon")], axis=0)
        else:
            att_blocks = attended.reshape(token_count, dp_count, rows_half).transpose(1, 0, 2)
            att_dp = exchange_blocks(att_blocks, "dp")
            att_group = gather_members(att_dp, "lon")
            att_group = att_group.transpose(1, 0, 2, 3).reshape(-1, rows_half)

    device_count = dp_count * lat_count * lon_count
    partial = lax.dot_general(
        att_group, cot_group, (((0,), (0,)), ((), ())), preferred_element_type=jnp.float32
    ) * (1.0 / device_count)
    spread = lax.all_to_all(partial.astype(jnp.bfloat16), "lat", 0, 0, tiled=True)
    d_w_out = spread.astype(jnp.float32).reshape(lat_count, rows_block, cols_block).sum(axis=0)

    grad_kv_own = grad_kv_own.astype(jnp.bfloat16).reshape(2, token_count, width)
    grad_proj = jnp.concatenate([grad_query, grad_kv_own[0], grad_kv_own[1]], axis=1)
    d_input = back_project(grad_proj).reshape(1, height, breadth, width)
    return (d_input, d_w_out)


def solution(mesh):
    in_specs = (
        P("dp", "lat", "lon", None),
        P("dp", "lat", "lon", None),
        P(),
        P("dp", None),
        P("dp", None),
    )
    out_specs = (P("dp", "lat", "lon", None), P(("dp", "lat"), "lon"))
    return jax.shard_map(shards, mesh=mesh, in_specs=in_specs, out_specs=out_specs, check_vma=False)
```
